128 devices in a mesh: pipe: 2 (over x_hi), ctx: 32 (over y, z, core), tp: 2 (over x_lo).
Axes of the slice: x: 4 (x_hi: 2, x_lo: 2; x = x_hi * 2 + x_lo), y: 4, z: 4, core: 2. Of those that a mesh axis runs over, the one named last changes fastest.
Arguments:
- resid_in: bfloat16 [4096, 4096], P('ctx', 'tp'), may hold values from -6 to 6
- ssm_input: bfloat16 [4096, 8192], P('ctx', 'tp'), may hold values from -6 to 6
- ssm_gate: bfloat16 [4096, 8192], P('ctx', 'tp'), may hold values from -6 to 6
- ssm_in_b: bfloat16 [4096, 512], P('ctx', 'tp'), may hold values from -0.5 to 0.5
- ssm_out_c: bfloat16 [4096, 512], P('ctx', 'tp'), may hold values from -6 to 6
- step_size: float32 [4096, 128], P('ctx', 'tp'), as said below
- decay_rate: float32 [128], P('tp'), may hold values from 0.0001 to 1, as said below
- skip_gain: float32 [128], P('tp'), may hold values from 0.5 to 1.5
- norm_gain: float32 [8192], P('tp'), may hold values from 0.1 to 1.9
- queries: bfloat16 [4096, 8192], P('ctx', 'tp'), may hold values from -6 to 6
- keys: bfloat16 [4096, 512], P('ctx', 'tp'), may hold values from -6 to 6
- values: bfloat16 [4096, 512], P('ctx', 'tp'), may hold values from -6 to 6
- out_weights: bfloat16 [2, 8192, 4096], P('pipe', 'tp', 'ctx'), may hold values from -0.0625 to 0.0625
Outputs:
- sections_out: bfloat16 [2, 4096, 4096], P('pipe', 'ctx', 'tp')
The draws below stay inside these ranges and needn't reach their ends.
Inputs may be any that keep to these rules, and one draw needn't show every extreme that they name: `step_size`: step sizes are positive. `decay_rate`: rates are positive.
All inputs are finite; a program needn't handle non-finite values.
Results may differ from the reference program's by a relative error of at most 0.015.
Values may be sent and summed in bfloat16 or wider, within the bound.
No kernel may reach another device: no remote copies, remote signals or barrier semaphores. Data moves between devices by JAX's collectives and lax.ppermute only.
A program may use at most 256 MiB of HBM per device.

```python
import math
import jax
import jax.numpy as jnp
from jax import lax

D = 4096
MHEADS = 128
MHEAD_DIM = 64
STATE = 128
GROUPS = 4
SCAN_BLOCK = 128
QHEADS = 64
KVHEADS = 4
HEAD_DIM = 128
TOKENS = 4096
INNER = 8192
SECTIONS = 2


def forgetting_expression(key):
    parts = jax.random.split(jax.random.fold_in(key, 7), 6)
    cutoff = 5
    quick_route = jax.random.randint(parts[0], (MHEADS,), 0, 10) < cutoff
    spans = jnp.where(quick_route, jax.random.uniform(parts[1], (MHEADS,), minval=30.0, maxval=50.0), TOKENS / jax.random.uniform(parts[1], (MHEADS,), minval=1.0, maxval=1.25))
    baseline = jax.random.uniform(parts[2], (MHEADS,), minval=0.7, maxval=1.4) / jnp.sqrt(spans)
    forgetting_speeds = 1.0 / (spans * baseline)
    rough = jnp.exp(jax.random.uniform(parts[3], (TOKENS, MHEADS), minval=math.log(0.6), maxval=math.log(1.5)))
    increment_widths = baseline[None, :] * rough
    location_indices = jax.random.randint(parts[4], (2, MHEADS), 0, TOKENS)
    all_lines_mask = jnp.arange(TOKENS, dtype=jnp.int32)[:, None]
    element_batch = ((all_lines_mask == location_indices[0][None, :]) | (all_lines_mask == location_indices[1][None, :])) & jnp.logical_not(quick_route)[None, :]
    overall_quantity = jax.random.uniform(parts[5], (MHEADS,), minval=0.22, maxval=0.35)
    increment_widths = jnp.where(element_batch, (overall_quantity / forgetting_speeds)[None, :], increment_widths)
    attenuation_multiplier = 1.0 / (overall_quantity * spans)
    return (forgetting_speeds, increment_widths, element_batch, attenuation_multiplier)


def draw_step_size(key, part):
    return forgetting_expression(key)[1]


def draw_decay_rate(key, part):
    return forgetting_expression(key)[0]


def draw_ssm_input(key, part):
    forgetting_speeds, increment_widths, element_batch, attenuation_multiplier = forgetting_expression(key)
    inner_key = jax.random.fold_in(key, 19)
    drawn = jnp.clip(jax.random.normal(inner_key, (TOKENS, MHEADS, MHEAD_DIM)), -6.0, 6.0)
    multiplier_coefficient = jnp.where(element_batch, attenuation_multiplier[None, :], 1.0)[:, :, None]
    return (drawn * multiplier_coefficient).reshape(TOKENS, MHEADS * MHEAD_DIM).astype(jnp.bfloat16)


def drawn_pair(key):
    parts = jax.random.split(jax.random.fold_in(key, 13), 2)
    query_vals = jnp.clip(jax.random.normal(parts[0], (TOKENS, QHEADS * HEAD_DIM)) * 1.6, -6.0, 6.0)
    key_vals = jnp.clip(jax.random.normal(parts[1], (TOKENS, KVHEADS * HEAD_DIM)) * 1.6, -6.0, 6.0)
    return (query_vals, key_vals)


def draw_queries(key, part):
    return drawn_pair(key)[0].astype(jnp.bfloat16)


def draw_keys(key, part):
    return drawn_pair(key)[1].astype(jnp.bfloat16)


def shard_levels(stream_key, shape, shards, smallest, top_value):
    factor_of, own = 1.0, jax.random.fold_in(stream_key, 6)
    for position, blocks in shards:
        heights = jnp.exp(jax.random.uniform(jax.random.fold_in(own, position), (blocks,), jnp.float32, smallest / len(shards), top_value / len(shards)))
        factor_of = factor_of * jnp.repeat(heights, shape[position] // blocks).reshape([-1 if axis == position else 1 for axis in range(len(shape))])
    return factor_of


def centred(rng, extent, scale, bound, cuts=(), held_as=jnp.bfloat16):
    entries = jax.random.normal(rng, extent, jnp.float32) * scale
    if len(cuts) > 0:
        entries = shard_levels(rng, extent, cuts, -0.22, 0.18) * entries
    return jnp.clip(entries, min=-bound, max=bound).astype(held_as)


def setup_inputs(seed: int = 0) -> dict:
    splits = jax.random.split(jax.random.key(seed), 14)
    resid_in = centred(splits[0], (TOKENS, D), 1.0, 6.0, ((0, 32), (1, 2)))
    ssm_input = draw_ssm_input(jax.random.fold_in(splits[13], 71), 0)
    ssm_gate = centred(splits[2], (TOKENS, INNER), 1.0, 6.0, ((0, 32), (1, 2)))
    ssm_in_b = centred(splits[3], (TOKENS, GROUPS * STATE), STATE ** -0.5, 0.5, ((0, 32), (1, 2)))
    ssm_out_c = centred(splits[4], (TOKENS, GROUPS * STATE), 1.0, 6.0, ((0, 32), (1, 2)))
    step_size = draw_step_size(jax.random.fold_in(splits[13], 71), 0)
    decay_rate = draw_decay_rate(jax.random.fold_in(splits[13], 71), 0)
    skip_gain = jnp.clip(0.5 + 1.0 * jax.random.uniform(splits[7], (MHEADS,), jnp.float32) ** shard_levels(splits[7], (MHEADS,), ((0, 2),), -0.2, 0.2), 0.5, 1.5)
    norm_gain = jnp.clip(1.0 + 0.18 * jax.random.normal(splits[8], (INNER,), jnp.float32), 0.1, 1.9)
    queries = draw_queries(jax.random.fold_in(splits[13], 71), 0)
    keys = draw_keys(jax.random.fold_in(splits[13], 71), 0)
    values = centred(splits[11], (TOKENS, KVHEADS * HEAD_DIM), 1.0, 6.0, ((0, 32), (1, 2)))
    out_weights = centred(splits[12], (SECTIONS, INNER, D), INNER ** -0.5, 0.0625, ((0, 2), (1, 2), (2, 32)))
    return {"resid_in": resid_in, "ssm_input": ssm_input, "ssm_gate": ssm_gate, "ssm_in_b": ssm_in_b, "ssm_out_c": ssm_out_c, "step_size": step_size, "decay_rate": decay_rate, "skip_gain": skip_gain, "norm_gain": norm_gain, "queries": queries, "keys": keys, "values": values, "out_weights": out_weights}


exact_mode = lax.Precision.HIGHEST
norm_eps = 1e-05

def block_scan(state_now, inputs_x, input_b, output_c, step_rows, log_decay):
    width = inputs_x.shape[0]
    groups = inputs_x.shape[1]
    per_group = inputs_x.shape[2]
    running = jnp.cumsum(log_decay, axis=0)
    spread = running[:, None, :] - running[None, :, :]
    causal = jnp.arange(width, dtype=jnp.int32)[:, None] >= jnp.arange(width, dtype=jnp.int32)[None, :]
    decay_mat = jnp.exp(jnp.where(causal[:, :, None], spread, -jnp.inf))
    decay_mat = decay_mat.reshape(width, width, groups, per_group).transpose(2, 3, 0, 1)
    cross_cb = jnp.einsum('tgn,sgn->gts', output_c, input_b, precision=exact_mode)
    step_cols = step_rows.reshape(width, groups, per_group).transpose(1, 2, 0)
    mixing = cross_cb[:, None, :, :] * decay_mat * step_cols[:, :, None, :]
    within = jnp.einsum('gjts,sgjp->tgjp', mixing, inputs_x, precision=exact_mode)
    entry = jnp.exp(running).reshape(width, groups, per_group)
    carried = jnp.einsum('tgn,gjpn->tgjp', output_c, state_now, precision=exact_mode) * entry[:, :, :, None]
    tail_weight = (jnp.exp(running[-1][None, :] - running) * step_rows).reshape(width, groups, per_group)
    leaving = jnp.exp(running[-1]).reshape(groups, per_group)
    state_next = leaving[:, :, None, None] * state_now + jnp.einsum('sgj,sgjp,sgn->gjpn', tail_weight, inputs_x, input_b, precision=exact_mode)
    return (state_next, within + carried)

def gate_norm(values_y, gate_in, gains, groups):
    rows_here = values_y.shape[0]
    gated = values_y * jax.nn.silu(gate_in.astype(jnp.float32))
    grouped = gated.reshape(rows_here, groups, -1)
    meansq = lax.optimization_barrier(jnp.mean(grouped * grouped, axis=-1, keepdims=True))
    scaled = (grouped * lax.rsqrt(meansq + norm_eps)).reshape(rows_here, -1)
    return (scaled * gains[None, :]).astype(jnp.bfloat16)

def mamba_reference(ssm_input, ssm_gate, ssm_in_b, ssm_out_c, step_size, decay_rate, skip_gain, norm_gain):
    total_rows = ssm_input.shape[0]
    per_group = MHEADS // GROUPS
    block_count = total_rows // SCAN_BLOCK
    inputs_x = ssm_input.astype(jnp.float32).reshape(block_count, SCAN_BLOCK, GROUPS, per_group, MHEAD_DIM)
    input_b = ssm_in_b.astype(jnp.float32).reshape(block_count, SCAN_BLOCK, GROUPS, STATE)
    output_c = ssm_out_c.astype(jnp.float32).reshape(block_count, SCAN_BLOCK, GROUPS, STATE)
    step_rows = step_size.reshape(block_count, SCAN_BLOCK, MHEADS)
    log_decay = (-step_size * decay_rate[None, :]).reshape(block_count, SCAN_BLOCK, MHEADS)

    def block_turn(state_now, block_data):
        part_x, part_b, part_c, part_step, part_log = block_data
        return block_scan(state_now, part_x, part_b, part_c, part_step, part_log)
    start_state = jnp.zeros((GROUPS, per_group, MHEAD_DIM, STATE), jnp.float32)
    final_state, pieces = lax.scan(block_turn, start_state, (inputs_x, input_b, output_c, step_rows, log_decay))
    skipped = ssm_input.astype(jnp.float32).reshape(total_rows, MHEADS, MHEAD_DIM) * skip_gain[None, :, None]
    values_y = pieces.reshape(total_rows, MHEADS * MHEAD_DIM) + skipped.reshape(total_rows, MHEADS * MHEAD_DIM)
    return gate_norm(values_y, ssm_gate, norm_gain, GROUPS)

def attention_reference(queries, keys, values):
    total_rows = queries.shape[0]
    per_key = QHEADS // KVHEADS
    span = math.gcd(total_rows, 128)
    score_scale = 1.0 / math.sqrt(HEAD_DIM)
    key_all = keys.astype(jnp.float32).reshape(total_rows, KVHEADS, HEAD_DIM)
    value_all = values.astype(jnp.float32).reshape(total_rows, KVHEADS, HEAD_DIM)
    key_pos = jnp.arange(total_rows, dtype=jnp.int32)

    def query_block(block_index):
        begin = block_index * span
        query_rows = lax.dynamic_slice_in_dim(queries, begin, span, 0).astype(jnp.float32)
        query_rows = query_rows.reshape(span, KVHEADS, per_key, HEAD_DIM)
        scores = jnp.einsum('qgjd,kgd->gjqk', query_rows, key_all) * score_scale
        query_pos = begin + jnp.arange(span, dtype=jnp.int32)
        allowed = key_pos[None, :] <= query_pos[:, None]
        row_top = lax.optimization_barrier(jnp.max(jnp.where(allowed, scores, -jnp.inf), axis=-1, keepdims=True))
        weights_exp = jnp.where(allowed, jnp.exp(scores - row_top), 0.0)
        row_total = lax.optimization_barrier(jnp.sum(weights_exp, axis=-1))
        rounded = lax.optimization_barrier(weights_exp.astype(jnp.bfloat16)).astype(jnp.float32)
        mixed = jnp.einsum('gjqk,kgd->gjqd', rounded, value_all) / row_total[..., None]
        return mixed.transpose(2, 0, 1, 3).reshape(span, QHEADS * HEAD_DIM).astype(jnp.bfloat16)
    blocks_out = lax.map(query_block, jnp.arange(total_rows // span, dtype=jnp.int32))
    return blocks_out.reshape(total_rows, QHEADS * HEAD_DIM)

def reference(resid_in, ssm_input, ssm_gate, ssm_in_b, ssm_out_c, step_size, decay_rate, skip_gain, norm_gain, queries, keys, values, out_weights):
    mamba_mixed = mamba_reference(ssm_input, ssm_gate, ssm_in_b, ssm_out_c, step_size, decay_rate, skip_gain, norm_gain)
    attn_mixed = attention_reference(queries, keys, values)
    section_first = (resid_in.astype(jnp.float32) + jnp.dot(mamba_mixed, out_weights[0], preferred_element_type=jnp.float32)).astype(jnp.bfloat16)
    section_second = (section_first.astype(jnp.float32) + jnp.dot(attn_mixed, out_weights[1], preferred_element_type=jnp.float32)).astype(jnp.bfloat16)
    return jnp.stack([section_first, section_second], axis=0)
```

```python
import math

import jax
import jax.numpy as jnp
from jax import lax
from jax.sharding import PartitionSpec as P

MHEAD_DIM = 64
STATE = 128
SCAN_BLOCK = 128
HEAD_DIM = 128


exact_mode = lax.Precision.HIGHEST
norm_eps = 1e-05


def entering_2(x, axis, combine, identity):
    peers, position = (lax.axis_size(axis), lax.axis_index(axis))
    everything = jax.tree.map(
        lambda part, kind: lax.all_gather(part.astype(kind), axis), x, (jnp.bfloat16, jnp.bfloat16)
    )
    start = jax.tree.map(
        lambda part, zero: jnp.broadcast_to(jnp.asarray(zero, part.dtype), part.shape), x, identity
    )

    def turn(k, before):
        reached = k < position
        new = combine(
            before, jax.tree.map(lambda part, own: part[k].astype(own.dtype), everything, x)
        )
        return jax.tree.map(lambda a, b: jnp.where(reached, a, b), new, before)

    return lax.fori_loop(0, peers, turn, start)


CTX = ("y", "zc")


def gathered(x, axis):
    peers = lax.axis_size(axis)
    spread = jnp.broadcast_to(x[None], (peers,) + x.shape)
    return lax.all_to_all(spread, axis, 0, 0)


def entering_states(through_log, local_state):
    outer = lax.axis_size("y")
    inner = lax.axis_size("zc")
    peers = outer * inner
    rank = lax.axis_index("y") * inner + lax.axis_index("zc")
    logs = gathered(through_log, CTX)
    logs = logs.reshape((peers,) + through_log.shape)
    places = jnp.arange(peers, dtype=jnp.int32)

    def span_weight(k, upto):
        inside = (places[None, :] > k[:, None]) & (places[None, :] < upto)
        summed = jnp.sum(jnp.where(inside[:, :, None, None], logs[None], 0.0), axis=1)
        return jnp.where((k < upto)[:, None, None], jnp.exp(summed), 0.0)

    first = lax.axis_index("y") * inner
    near = gathered(local_state.astype(jnp.bfloat16), "zc").astype(jnp.float32)
    near_ids = first + jnp.arange(inner, dtype=jnp.int32)
    own_part = jnp.einsum(
        "kgj,kgjpn->gjpn", span_weight(near_ids, rank), near, precision=exact_mode
    )
    group_end = first + inner
    group_total = jnp.einsum(
        "kgj,kgjpn->gjpn", span_weight(near_ids, group_end), near, precision=exact_mode
    )
    far = gathered(group_total.astype(jnp.bfloat16), "y").astype(jnp.float32)
    far_ends = (jnp.arange(outer, dtype=jnp.int32) + 1) * inner - 1
    far_weight = span_weight(far_ends, rank)
    far_weight = jnp.where((far_ends < first)[:, None, None], far_weight, 0.0)
    far_part = jnp.einsum("kgj,kgjpn->gjpn", far_weight, far, precision=exact_mode)
    return own_part + far_part


def from_partner(block, axis, distance):
    count = lax.axis_size(axis)
    route = []
    for low in range(count):
        high = low | 1 << distance
        if high != low and high < count:
            route += [(low, high), (high, low)]
    return lax.ppermute(block, axis, route)


def shifted(x, axis, by):
    peers = lax.axis_size(axis)
    pairs = [(i, i + by) for i in range(peers) if 0 <= i + by < peers]
    return lax.ppermute(x, axis, pairs)


def block_scan(state_now, inputs_x, input_b, output_c, step_rows, log_decay):
    width = inputs_x.shape[0]
    groups = inputs_x.shape[1]
    per_group = inputs_x.shape[2]
    running = jnp.cumsum(log_decay, axis=0)
    spread = running[:, None, :] - running[None, :, :]
    causal = (
        jnp.arange(width, dtype=jnp.int32)[:, None] >= jnp.arange(width, dtype=jnp.int32)[None, :]
    )
    decay_mat = jnp.exp(jnp.where(causal[:, :, None], spread, -jnp.inf))
    decay_mat = decay_mat.reshape(width, width, groups, per_group).transpose(2, 3, 0, 1)
    cross_cb = jnp.einsum("tgn,sgn->gts", output_c, input_b, precision=exact_mode)
    step_cols = step_rows.reshape(width, groups, per_group).transpose(1, 2, 0)
    mixing = cross_cb[:, None, :, :] * decay_mat * step_cols[:, :, None, :]
    within = jnp.einsum("gjts,sgjp->tgjp", mixing, inputs_x, precision=exact_mode)
    entry = jnp.exp(running).reshape(width, groups, per_group)
    carried = (
        jnp.einsum("tgn,gjpn->tgjp", output_c, state_now, precision=exact_mode)
        * entry[:, :, :, None]
    )
    tail_weight = (jnp.exp(running[-1][None, :] - running) * step_rows).reshape(
        width, groups, per_group
    )
    leaving = jnp.exp(running[-1]).reshape(groups, per_group)
    state_next = leaving[:, :, None, None] * state_now + jnp.einsum(
        "sgj,sgjp,sgn->gjpn", tail_weight, inputs_x, input_b, precision=exact_mode
    )
    return (state_next, within + carried)


def gate_norm(values_y, gate_in, gains, groups):
    rows_here = values_y.shape[0]
    gated = values_y * jax.nn.silu(gate_in.astype(jnp.float32))
    grouped = gated.reshape(rows_here, groups, -1)
    meansq = jnp.mean(grouped * grouped, axis=-1, keepdims=True)
    scaled = (grouped * lax.rsqrt(meansq + norm_eps)).reshape(rows_here, -1)
    return (scaled * gains[None, :]).astype(jnp.bfloat16)


def join_states(earlier, later):
    return (earlier[0] * later[0], later[0][:, :, None, None] * earlier[1] + later[1])


def mamba_mixer(
    ssm_input, ssm_gate, ssm_in_b, ssm_out_c, step_size, decay_rate, skip_gain, norm_gain
):
    rows_here = ssm_input.shape[0]
    head_count = decay_rate.shape[0]
    groups = ssm_in_b.shape[1] // STATE
    per_group = head_count // groups
    block_count = rows_here // SCAN_BLOCK
    log_decay = -step_size * decay_rate[None, :]
    inputs_x = ssm_input.reshape(block_count, SCAN_BLOCK, groups, per_group, MHEAD_DIM)
    input_b = ssm_in_b.reshape(block_count, SCAN_BLOCK, groups, STATE)
    output_c = ssm_out_c.reshape(block_count, SCAN_BLOCK, groups, STATE)

    def block_turn(state_now, block_data):
        part_x, part_b, part_c, part_step, part_log = block_data
        return block_scan(
            state_now,
            part_x.astype(jnp.float32),
            part_b.astype(jnp.float32),
            part_c.astype(jnp.float32),
            part_step,
            part_log,
        )

    start_state = jnp.zeros((groups, per_group, MHEAD_DIM, STATE), jnp.float32)
    local_state, pieces = lax.scan(
        block_turn,
        start_state,
        (
            inputs_x,
            input_b,
            output_c,
            step_size.reshape(block_count, SCAN_BLOCK, head_count),
            log_decay.reshape(block_count, SCAN_BLOCK, head_count),
        ),
    )
    running = jnp.cumsum(log_decay, axis=0)
    entering = entering_states(running[-1].reshape(groups, per_group), local_state)
    output_all = ssm_out_c.astype(jnp.float32).reshape(rows_here, groups, STATE)
    carried = (
        jnp.einsum("tgn,gjpn->tgjp", output_all, entering, precision=exact_mode)
        * jnp.exp(running).reshape(rows_here, groups, per_group)[:, :, :, None]
    )
    skipped = (
        ssm_input.astype(jnp.float32).reshape(rows_here, groups, per_group, MHEAD_DIM)
        * skip_gain.reshape(groups, per_group)[None, :, :, None]
    )
    values_y = pieces.reshape(rows_here, groups, per_group, MHEAD_DIM) + carried + skipped
    return gate_norm(values_y.reshape(rows_here, -1), ssm_gate, norm_gain, groups)


def attention(queries, keys, values, ctx_rank):
    rows_here = queries.shape[0]
    kv_count = keys.shape[1] // HEAD_DIM
    per_key = queries.shape[1] // HEAD_DIM // kv_count
    query_groups = queries.reshape(rows_here, kv_count, per_key, HEAD_DIM)
    query_pos = ctx_rank * rows_here + jnp.arange(rows_here, dtype=jnp.int32)
    last_query = query_pos[-1]
    score_scale = 1.0 / math.sqrt(HEAD_DIM)

    def key_block(running, block_data):
        key_rows, value_rows, first_key = block_data

        def absorb(held):
            row_max, row_sum, weighted = held
            scores = (
                jnp.einsum(
                    "qgjd,kgd->gjqk", query_groups, key_rows, preferred_element_type=jnp.float32
                )
                * score_scale
            )
            key_pos = first_key + jnp.arange(key_rows.shape[0], dtype=jnp.int32)
            allowed = key_pos[None, :] <= query_pos[:, None]
            scores = jnp.where(allowed, scores, -1e30)
            new_max = jnp.maximum(row_max, jnp.max(scores, axis=-1))
            rescale = jnp.exp(row_max - new_max)
            weights_exp = jnp.where(allowed, jnp.exp(scores - new_max[..., None]), 0.0)
            row_sum = row_sum * rescale + jnp.sum(weights_exp, axis=-1)
            weighted = weighted * rescale[..., None] + jnp.einsum(
                "gjqk,kgd->gjqd",
                weights_exp.astype(jnp.bfloat16),
                value_rows,
                preferred_element_type=jnp.float32,
            )
            return (new_max, row_sum, weighted)

        return (lax.cond(first_key <= last_query, absorb, lambda held: held, running), None)

    start_state = (
        jnp.full((kv_count, per_key, rows_here), -1e30, jnp.float32),
        jnp.zeros((kv_count, per_key, rows_here), jnp.float32),
        jnp.zeros((kv_count, per_key, rows_here, HEAD_DIM), jnp.float32),
    )
    running = start_state
    both = gathered(jnp.concatenate([keys, values], axis=1), CTX)
    both = both.reshape(-1, both.shape[-1])
    key_piece = both[:, : keys.shape[1]]
    value_piece = both[:, keys.shape[1] :]
    count = key_piece.shape[0]
    width = math.gcd(count, 1024)
    blocks = count // width
    key_rows = key_piece.reshape(blocks, width, kv_count, HEAD_DIM)
    value_rows = value_piece.reshape(blocks, width, kv_count, HEAD_DIM)
    starts = width * jnp.arange(blocks, dtype=jnp.int32)
    running, unused = lax.scan(key_block, running, (key_rows, value_rows, starts))
    row_max, row_sum, weighted = running
    mixed = (weighted / row_sum[..., None]).transpose(2, 0, 1, 3).reshape(rows_here, -1)
    return mixed.astype(jnp.bfloat16)


def take_half(array, axis_dim, section):
    width = array.shape[axis_dim] // 2
    return lax.dynamic_slice_in_dim(array, section * width, width, axis_dim)


def per_device(
    resid_in,
    ssm_input,
    ssm_gate,
    ssm_in_b,
    ssm_out_c,
    step_size,
    decay_rate,
    skip_gain,
    norm_gain,
    queries,
    keys,
    values,
    out_weights,
):
    section = lax.axis_index("pipe")
    ctx_rank = lax.axis_index("y") * lax.axis_size("zc") + lax.axis_index("zc")
    mamba_part = mamba_mixer(
        take_half(ssm_input, 1, section),
        take_half(ssm_gate, 1, section),
        take_half(ssm_in_b, 1, section),
        take_half(ssm_out_c, 1, section),
        take_half(step_size, 1, section),
        take_half(decay_rate, 0, section),
        take_half(skip_gain, 0, section),
        take_half(norm_gain, 0, section),
    )
    attn_part = attention(
        take_half(queries, 1, section),
        take_half(keys, 1, section),
        take_half(values, 1, section),
        ctx_rank,
    )
    outgoing = jnp.where(section == 0, attn_part, mamba_part)
    kept_half = jnp.where(section == 0, mamba_part, attn_part)
    incoming = from_partner(outgoing, "pipe", 0)
    mixed_rows = jnp.where(
        section == 0,
        jnp.concatenate([kept_half, incoming], axis=1),
        jnp.concatenate([incoming, kept_half], axis=1),
    )
    partial_value = jnp.dot(
        mixed_rows,
        lax.all_gather(out_weights, CTX, axis=2, tiled=True)[0],
        preferred_element_type=jnp.float32,
    )
    half = partial_value.shape[1] // 2
    tp_rank = lax.axis_index("tp")
    kept = jnp.where(tp_rank == 0, partial_value[:, :half], partial_value[:, half:])
    sent = jnp.where(tp_rank == 0, partial_value[:, half:], partial_value[:, :half])
    projected = kept + from_partner(sent.astype(jnp.bfloat16), "tp", 0).astype(jnp.float32)
    own_section = (resid_in.astype(jnp.float32) + projected).astype(jnp.bfloat16)
    received = shifted(own_section, "pipe", 1)
    second_section = (received.astype(jnp.float32) + projected).astype(jnp.bfloat16)
    return jnp.where(section == 0, own_section, second_section)[None]


def solution(mesh):
    pipe, ctx, tp = (mesh.shape[name] for name in ("pipe", "ctx", "tp"))
    outer = 4 if ctx % 4 == 0 else 1
    split = jax.sharding.Mesh(
        mesh.devices.reshape(pipe, outer, ctx // outer, tp), ("pipe", "y", "zc", "tp")
    )
    return jax.shard_map(
        per_device,
        mesh=split,
        in_specs=(
            P(CTX, "tp"),
            P(CTX, "tp"),
            P(CTX, "tp"),
            P(CTX, "tp"),
            P(CTX, "tp"),
            P(CTX, "tp"),
            P("tp"),
            P("tp"),
            P("tp"),
            P(CTX, "tp"),
            P(CTX, "tp"),
            P(CTX, "tp"),
            P("pipe", "tp", CTX),
        ),
        out_specs=P("pipe", CTX, "tp"),
        check_vma=False,
    )
```

```python
import math

import jax
import jax.numpy as jnp
from jax import lax
from jax.sharding import PartitionSpec as P

MHEAD_DIM = 64
STATE = 128
SCAN_BLOCK = 128
HEAD_DIM = 128


exact_mode = lax.Precision.HIGHEST
norm_eps = 1e-05


def entering_2(x, axis, combine, identity):
    peers, position = (lax.axis_size(axis), lax.axis_index(axis))
    everything = jax.tree.map(
        lambda part, kind: lax.all_gather(part.astype(kind), axis), x, (jnp.bfloat16, jnp.bfloat16)
    )
    start = jax.tree.map(
        lambda part, zero: jnp.broadcast_to(jnp.asarray(zero, part.dtype), part.shape), x, identity
    )

    def turn(k, before):
        reached = k < position
        new = combine(
            before, jax.tree.map(lambda part, own: part[k].astype(own.dtype), everything, x)
        )
        return jax.tree.map(lambda a, b: jnp.where(reached, a, b), new, before)

    return lax.fori_loop(0, peers, turn, start)


CTX = ("y", "zc")


def gathered(x, axis):
    peers = lax.axis_size(axis)
    spread = jnp.broadcast_to(x[None], (peers,) + x.shape)
    return lax.all_to_all(spread, axis, 0, 0)


def entering_states(through_log, local_state):
    outer = lax.axis_size("y")
    inner = lax.axis_size("zc")
    peers = outer * inner
    rank = lax.axis_index("y") * inner + lax.axis_index("zc")
    logs = gathered(through_log, CTX)
    logs = logs.reshape((peers,) + through_log.shape)
    places = jnp.arange(peers, dtype=jnp.int32)

    def span_weight(k, upto):
        inside = (places[None, :] > k[:, None]) & (places[None, :] < upto)
        summed = jnp.sum(jnp.where(inside[:, :, None, None], logs[None], 0.0), axis=1)
        return jnp.where((k < upto)[:, None, None], jnp.exp(summed), 0.0)

    first = lax.axis_index("y") * inner
    near = gathered(local_state.astype(jnp.bfloat16), "zc").astype(jnp.float32)
    near_ids = first + jnp.arange(inner, dtype=jnp.int32)
    own_part = jnp.einsum(
        "kgj,kgjpn->gjpn", span_weight(near_ids, rank), near, precision=exact_mode
    )
    group_end = first + inner
    group_total = jnp.einsum(
        "kgj,kgjpn->gjpn", span_weight(near_ids, group_end), near, precision=exact_mode
    )
    far = gathered(group_total.astype(jnp.bfloat16), "y").astype(jnp.float32)
    far_ends = (jnp.arange(outer, dtype=jnp.int32) + 1) * inner - 1
    far_weight = span_weight(far_ends, rank)
    far_weight = jnp.where((far_ends < first)[:, None, None], far_weight, 0.0)
    far_part = jnp.einsum("kgj,kgjpn->gjpn", far_weight, far, precision=exact_mode)
    return own_part + far_part


def from_partner(block, axis, distance):
    count = lax.axis_size(axis)
    route = []
    for low in range(count):
        high = low | 1 << distance
        if high != low and high < count:
            route += [(low, high), (high, low)]
    return lax.ppermute(block, axis, route)


def shifted(x, axis, by):
    peers = lax.axis_size(axis)
    pairs = [(i, i + by) for i in range(peers) if 0 <= i + by < peers]
    return lax.ppermute(x, axis, pairs)


def block_scan(state_now, inputs_x, input_b, output_c, step_rows, log_decay):
    width = inputs_x.shape[0]
    groups = inputs_x.shape[1]
    per_group = inputs_x.shape[2]
    running = jnp.cumsum(log_decay, axis=0)
    spread = running[:, None, :] - running[None, :, :]
    causal = (
        jnp.arange(width, dtype=jnp.int32)[:, None] >= jnp.arange(width, dtype=jnp.int32)[None, :]
    )
    decay_mat = jnp.exp(jnp.where(causal[:, :, None], spread, -jnp.inf))
    decay_mat = decay_mat.reshape(width, width, groups, per_group).transpose(2, 3, 0, 1)
    cross_cb = jnp.einsum("tgn,sgn->gts", output_c, input_b, precision=exact_mode)
    step_cols = step_rows.reshape(width, groups, per_group).transpose(1, 2, 0)
    mixing = cross_cb[:, None, :, :] * decay_mat * step_cols[:, :, None, :]
    within = jnp.einsum("gjts,sgjp->tgjp", mixing, inputs_x, precision=exact_mode)
    entry = jnp.exp(running).reshape(width, groups, per_group)
    carried = (
        jnp.einsum("tgn,gjpn->tgjp", output_c, state_now, precision=exact_mode)
        * entry[:, :, :, None]
    )
    tail_weight = (jnp.exp(running[-1][None, :] - running) * step_rows).reshape(
        width, groups, per_group
    )
    leaving = jnp.exp(running[-1]).reshape(groups, per_group)
    state_next = leaving[:, :, None, None] * state_now + jnp.einsum(
        "sgj,sgjp,sgn->gjpn", tail_weight, inputs_x, input_b, precision=exact_mode
    )
    return (state_next, within + carried)


def gate_norm(values_y, gate_in, gains, groups):
    rows_here = values_y.shape[0]
    gated = values_y * jax.nn.silu(gate_in.astype(jnp.float32))
    grouped = gated.reshape(rows_here, groups, -1)
    meansq = jnp.mean(grouped * grouped, axis=-1, keepdims=True)
    scaled = (grouped * lax.rsqrt(meansq + norm_eps)).reshape(rows_here, -1)
    return (scaled * gains[None, :]).astype(jnp.bfloat16)


def join_states(earlier, later):
    return (earlier[0] * later[0], later[0][:, :, None, None] * earlier[1] + later[1])


def mamba_mixer(
    ssm_input, ssm_gate, ssm_in_b, ssm_out_c, step_size, decay_rate, skip_gain, norm_gain
):
    rows_here = ssm_input.shape[0]
    head_count = decay_rate.shape[0]
    groups = ssm_in_b.shape[1] // STATE
    per_group = head_count // groups
    block_count = rows_here // SCAN_BLOCK
    log_decay = -step_size * decay_rate[None, :]
    inputs_x = ssm_input.reshape(block_count, SCAN_BLOCK, groups, per_group, MHEAD_DIM)
    input_b = ssm_in_b.reshape(block_count, SCAN_BLOCK, groups, STATE)
    output_c = ssm_out_c.reshape(block_count, SCAN_BLOCK, groups, STATE)

    def block_turn(state_now, block_data):
        part_x, part_b, part_c, part_step, part_log = block_data
        return block_scan(
            state_now,
            part_x.astype(jnp.float32),
            part_b.astype(jnp.float32),
            part_c.astype(jnp.float32),
            part_step,
            part_log,
        )

    start_state = jnp.zeros((groups, per_group, MHEAD_DIM, STATE), jnp.float32)
    local_state, pieces = lax.scan(
        block_turn,
        start_state,
        (
            inputs_x,
            input_b,
            output_c,
            step_size.reshape(block_count, SCAN_BLOCK, head_count),
            log_decay.reshape(block_count, SCAN_BLOCK, head_count),
        ),
    )
    running = jnp.cumsum(log_decay, axis=0)
    entering = entering_states(running[-1].reshape(groups, per_group), local_state)
    output_all = ssm_out_c.astype(jnp.float32).reshape(rows_here, groups, STATE)
    carried = (
        jnp.einsum("tgn,gjpn->tgjp", output_all, entering, precision=exact_mode)
        * jnp.exp(running).reshape(rows_here, groups, per_group)[:, :, :, None]
    )
    skipped = (
        ssm_input.astype(jnp.float32).reshape(rows_here, groups, per_group, MHEAD_DIM)
        * skip_gain.reshape(groups, per_group)[None, :, :, None]
    )
    values_y = pieces.reshape(rows_here, groups, per_group, MHEAD_DIM) + carried + skipped
    return gate_norm(values_y.reshape(rows_here, -1), ssm_gate, norm_gain, groups)


def attention(queries, keys, values, ctx_rank):
    rows_here = queries.shape[0]
    kv_count = keys.shape[1] // HEAD_DIM
    per_key = queries.shape[1] // HEAD_DIM // kv_count
    query_groups = queries.reshape(rows_here, kv_count, per_key, HEAD_DIM)
    query_pos = ctx_rank * rows_here + jnp.arange(rows_here, dtype=jnp.int32)
    last_query = query_pos[-1]
    score_scale = 1.0 / math.sqrt(HEAD_DIM)

    def key_block(running, block_data):
        key_rows, value_rows, first_key = block_data

        def absorb(held):
            row_max, row_sum, weighted = held
            scores = (
                jnp.einsum(
                    "qgjd,kgd->gjqk", query_groups, key_rows, preferred_element_type=jnp.float32
                )
                * score_scale
            )
            key_pos = first_key + jnp.arange(key_rows.shape[0], dtype=jnp.int32)
            allowed = key_pos[None, :] <= query_pos[:, None]
            scores = jnp.where(allowed, scores, -1e30)
            new_max = jnp.maximum(row_max, jnp.max(scores, axis=-1))
            rescale = jnp.exp(row_max - new_max)
            weights_exp = jnp.where(allowed, jnp.exp(scores - new_max[..., None]), 0.0)
            row_sum = row_sum * rescale + jnp.sum(weights_exp, axis=-1)
            weighted = weighted * rescale[..., None] + jnp.einsum(
                "gjqk,kgd->gjqd",
                weights_exp.astype(jnp.bfloat16),
                value_rows,
                preferred_element_type=jnp.float32,
            )
            return (new_max, row_sum, weighted)

        return (lax.cond(first_key <= last_query, absorb, lambda held: held, running), None)

    start_state = (
        jnp.full((kv_count, per_key, rows_here), -1e30, jnp.float32),
        jnp.zeros((kv_count, per_key, rows_here), jnp.float32),
        jnp.zeros((kv_count, per_key, rows_here, HEAD_DIM), jnp.float32),
    )
    running = start_state
    both = gathered(jnp.concatenate([keys, values], axis=1), CTX)
    both = both.reshape(-1, both.shape[-1])
    key_piece = both[:, : keys.shape[1]]
    value_piece = both[:, keys.shape[1] :]
    count = key_piece.shape[0]
    width = math.gcd(count, 1024)
    blocks = count // width
    key_rows = key_piece.reshape(blocks, width, kv_count, HEAD_DIM)
    value_rows = value_piece.reshape(blocks, width, kv_count, HEAD_DIM)
    starts = width * jnp.arange(blocks, dtype=jnp.int32)
    running, unused = lax.scan(key_block, running, (key_rows, value_rows, starts))
    row_max, row_sum, weighted = running
    mixed = (weighted / row_sum[..., None]).transpose(2, 0, 1, 3).reshape(rows_here, -1)
    return mixed.astype(jnp.bfloat16)


def take_half(array, axis_dim, section):
    width = array.shape[axis_dim] // 2
    return lax.dynamic_slice_in_dim(array, section * width, width, axis_dim)


def per_device(
    resid_in,
    ssm_input,
    ssm_gate,
    ssm_in_b,
    ssm_out_c,
    step_size,
    decay_rate,
    skip_gain,
    norm_gain,
    queries,
    keys,
    values,
    out_weights,
):
    section = lax.axis_index("pipe")
    ctx_rank = lax.axis_index("y") * lax.axis_size("zc") + lax.axis_index("zc")
    mamba_part = mamba_mixer(
        take_half(ssm_input, 1, section),
        take_half(ssm_gate, 1, section),
        take_half(ssm_in_b, 1, section),
        take_half(ssm_out_c, 1, section),
        take_half(step_size, 1, section),
        take_half(decay_rate, 0, section),
        take_half(skip_gain, 0, section),
        take_half(norm_gain, 0, section),
    )
    attn_part = attention(
        take_half(queries, 1, section),
        take_half(keys, 1, section),
        take_half(values, 1, section),
        ctx_rank,
    )
    outgoing = jnp.where(section == 0, attn_part, mamba_part)
    kept_half = jnp.where(section == 0, mamba_part, attn_part)
    incoming = from_partner(outgoing, "pipe", 0)
    mixed_rows = jnp.where(
        section == 0,
        jnp.concatenate([kept_half, incoming], axis=1),
        jnp.concatenate([incoming, kept_half], axis=1),
    )
    inner = lax.axis_size("zc")
    tp_rank = lax.axis_index("tp")
    rows = gathered(mixed_rows, "zc").reshape(-1, mixed_rows.shape[1])
    columns = lax.all_gather(out_weights[0], "y", axis=0)
    partial_value = jnp.einsum(
        "tc,ycr->tyr", rows, columns, preferred_element_type=jnp.float32
    )
    half = partial_value.shape[1] // 2
    kept = jnp.where(tp_rank == 0, partial_value[:, :half], partial_value[:, half:])
    sent = jnp.where(tp_rank == 0, partial_value[:, half:], partial_value[:, :half])
    summed = kept + from_partner(sent.astype(jnp.bfloat16), "tp", 0).astype(jnp.float32)
    pieces = summed.reshape((inner, -1) + summed.shape[1:]).astype(jnp.bfloat16)
    pieces = lax.all_to_all(pieces, "zc", 0, 0)
    projected = pieces.transpose(1, 2, 0, 3).reshape(pieces.shape[1], -1).astype(jnp.float32)
    own_section = (resid_in.astype(jnp.float32) + projected).astype(jnp.bfloat16)
    received = shifted(own_section, "pipe", 1)
    second_section = (received.astype(jnp.float32) + projected).astype(jnp.bfloat16)
    return jnp.where(section == 0, own_section, second_section)[None]


def solution(mesh):
    pipe, ctx, tp = (mesh.shape[name] for name in ("pipe", "ctx", "tp"))
    outer = 4 if ctx % 4 == 0 else 1
    split = jax.sharding.Mesh(
        mesh.devices.reshape(pipe, outer, ctx // outer, tp), ("pipe", "y", "zc", "tp")
    )
    return jax.shard_map(
        per_device,
        mesh=split,
        in_specs=(
            P(CTX, "tp"),
            P(CTX, "tp"),
            P(CTX, "tp"),
            P(CTX, "tp"),
            P(CTX, "tp"),
            P(CTX, "tp"),
            P("tp"),
            P("tp"),
            P("tp"),
            P(CTX, "tp"),
            P(CTX, "tp"),
            P(CTX, "tp"),
            P("pipe", "tp", CTX),
        ),
        out_specs=P("pipe", CTX, "tp"),
        check_vma=False,
    )
```

```python
import math

import jax
import jax.numpy as jnp
from jax import lax
from jax.sharding import PartitionSpec as P

MHEAD_DIM = 64
STATE = 128
SCAN_BLOCK = 128
HEAD_DIM = 128


exact_mode = lax.Precision.HIGHEST
norm_eps = 1e-05


def entering_2(x, axis, combine, identity):
    peers, position = (lax.axis_size(axis), lax.axis_index(axis))
    everything = jax.tree.map(
        lambda part, kind: lax.all_gather(part.astype(kind), axis), x, (jnp.bfloat16, jnp.bfloat16)
    )
    start = jax.tree.map(
        lambda part, zero: jnp.broadcast_to(jnp.asarray(zero, part.dtype), part.shape), x, identity
    )

    def turn(k, before):
        reached = k < position
        new = combine(
            before, jax.tree.map(lambda part, own: part[k].astype(own.dtype), everything, x)
        )
        return jax.tree.map(lambda a, b: jnp.where(reached, a, b), new, before)

    return lax.fori_loop(0, peers, turn, start)


CTX = ("y", "zc")


def gathered(x, axis):
    peers = lax.axis_size(axis)
    spread = jnp.broadcast_to(x[None], (peers,) + x.shape)
    return lax.all_to_all(spread, axis, 0, 0)


def entering_states(through_log, local_state):
    outer = lax.axis_size("y")
    inner = lax.axis_size("zc")
    peers = outer * inner
    rank = lax.axis_index("y") * inner + lax.axis_index("zc")
    logs = gathered(through_log, CTX)
    logs = logs.reshape((peers,) + through_log.shape)
    places = jnp.arange(peers, dtype=jnp.int32)

    def span_weight(k, upto):
        inside = (places[None, :] > k[:, None]) & (places[None, :] < upto)
        summed = jnp.sum(jnp.where(inside[:, :, None, None], logs[None], 0.0), axis=1)
        return jnp.where((k < upto)[:, None, None], jnp.exp(summed), 0.0)

    first = lax.axis_index("y") * inner
    near = gathered(local_state.astype(jnp.bfloat16), "zc").astype(jnp.float32)
    near_ids = first + jnp.arange(inner, dtype=jnp.int32)
    own_part = jnp.einsum(
        "kgj,kgjpn->gjpn", span_weight(near_ids, rank), near, precision=exact_mode
    )
    group_end = first + inner
    group_total = jnp.einsum(
        "kgj,kgjpn->gjpn", span_weight(near_ids, group_end), near, precision=exact_mode
    )
    far = gathered(group_total.astype(jnp.bfloat16), "y").astype(jnp.float32)
    far_ends = (jnp.arange(outer, dtype=jnp.int32) + 1) * inner - 1
    far_weight = span_weight(far_ends, rank)
    far_weight = jnp.where((far_ends < first)[:, None, None], far_weight, 0.0)
    far_part = jnp.einsum("kgj,kgjpn->gjpn", far_weight, far, precision=exact_mode)
    return own_part + far_part


def from_partner(block, axis, distance):
    count = lax.axis_size(axis)
    route = []
    for low in range(count):
        high = low | 1 << distance
        if high != low and high < count:
            route += [(low, high), (high, low)]
    return lax.ppermute(block, axis, route)


def shifted(x, axis, by):
    peers = lax.axis_size(axis)
    pairs = [(i, i + by) for i in range(peers) if 0 <= i + by < peers]
    return lax.ppermute(x, axis, pairs)


def block_scan(state_now, inputs_x, input_b, output_c, step_rows, log_decay):
    width = inputs_x.shape[0]
    groups = inputs_x.shape[1]
    per_group = inputs_x.shape[2]
    running = jnp.cumsum(log_decay, axis=0)
    spread = running[:, None, :] - running[None, :, :]
    causal = (
        jnp.arange(width, dtype=jnp.int32)[:, None] >= jnp.arange(width, dtype=jnp.int32)[None, :]
    )
    decay_mat = jnp.exp(jnp.where(causal[:, :, None], spread, -jnp.inf))
    decay_mat = decay_mat.reshape(width, width, groups, per_group).transpose(2, 3, 0, 1)
    cross_cb = jnp.einsum("tgn,sgn->gts", output_c, input_b, precision=exact_mode)
    step_cols = step_rows.reshape(width, groups, per_group).transpose(1, 2, 0)
    mixing = cross_cb[:, None, :, :] * decay_mat * step_cols[:, :, None, :]
    within = jnp.einsum("gjts,sgjp->tgjp", mixing, inputs_x, precision=exact_mode)
    entry = jnp.exp(running).reshape(width, groups, per_group)
    carried = (
        jnp.einsum("tgn,gjpn->tgjp", output_c, state_now, precision=exact_mode)
        * entry[:, :, :, None]
    )
    tail_weight = (jnp.exp(running[-1][None, :] - running) * step_rows).reshape(
        width, groups, per_group
    )
    leaving = jnp.exp(running[-1]).reshape(groups, per_group)
    state_next = leaving[:, :, None, None] * state_now + jnp.einsum(
        "sgj,sgjp,sgn->gjpn", tail_weight, inputs_x, input_b, precision=exact_mode
    )
    return (state_next, within + carried)


def gate_norm(values_y, gate_in, gains, groups):
    rows_here = values_y.shape[0]
    gated = values_y * jax.nn.silu(gate_in.astype(jnp.float32))
    grouped = gated.reshape(rows_here, groups, -1)
    meansq = jnp.mean(grouped * grouped, axis=-1, keepdims=True)
    scaled = (grouped * lax.rsqrt(meansq + norm_eps)).reshape(rows_here, -1)
    return (scaled * gains[None, :]).astype(jnp.bfloat16)


def join_states(earlier, later):
    return (earlier[0] * later[0], later[0][:, :, None, None] * earlier[1] + later[1])


def mamba_mixer(
    ssm_input, ssm_gate, ssm_in_b, ssm_out_c, step_size, decay_rate, skip_gain, norm_gain
):
    rows_here = ssm_input.shape[0]
    head_count = decay_rate.shape[0]
    groups = ssm_in_b.shape[1] // STATE
    per_group = head_count // groups
    block_count = rows_here // SCAN_BLOCK
    log_decay = -step_size * decay_rate[None, :]
    inputs_x = ssm_input.reshape(block_count, SCAN_BLOCK, groups, per_group, MHEAD_DIM)
    input_b = ssm_in_b.reshape(block_count, SCAN_BLOCK, groups, STATE)
    output_c = ssm_out_c.reshape(block_count, SCAN_BLOCK, groups, STATE)

    def block_turn(state_now, block_data):
        part_x, part_b, part_c, part_step, part_log = block_data
        return block_scan(
            state_now,
            part_x.astype(jnp.float32),
            part_b.astype(jnp.float32),
            part_c.astype(jnp.float32),
            part_step,
            part_log,
        )

    start_state = jnp.zeros((groups, per_group, MHEAD_DIM, STATE), jnp.float32)
    local_state, pieces = lax.scan(
        block_turn,
        start_state,
        (
            inputs_x,
            input_b,
            output_c,
            step_size.reshape(block_count, SCAN_BLOCK, head_count),
            log_decay.reshape(block_count, SCAN_BLOCK, head_count),
        ),
    )
    running = jnp.cumsum(log_decay, axis=0)
    entering = entering_states(running[-1].reshape(groups, per_group), local_state)
    output_all = ssm_out_c.astype(jnp.float32).reshape(rows_here, groups, STATE)
    carried = (
        jnp.einsum("tgn,gjpn->tgjp", output_all, entering, precision=exact_mode)
        * jnp.exp(running).reshape(rows_here, groups, per_group)[:, :, :, None]
    )
    skipped = (
        ssm_input.astype(jnp.float32).reshape(rows_here, groups, per_group, MHEAD_DIM)
        * skip_gain.reshape(groups, per_group)[None, :, :, None]
    )
    values_y = pieces.reshape(rows_here, groups, per_group, MHEAD_DIM) + carried + skipped
    return gate_norm(values_y.reshape(rows_here, -1), ssm_gate, norm_gain, groups)


def attention(queries, keys, values, ctx_rank):
    rows_here = queries.shape[0]
    kv_count = keys.shape[1] // HEAD_DIM
    per_key = queries.shape[1] // HEAD_DIM // kv_count
    query_groups = queries.reshape(rows_here, kv_count, per_key, HEAD_DIM)
    query_pos = ctx_rank * rows_here + jnp.arange(rows_here, dtype=jnp.int32)
    last_query = query_pos[-1]
    score_scale = 1.0 / math.sqrt(HEAD_DIM)

    def key_block(running, block_data):
        key_rows, value_rows, first_key = block_data

        def absorb(held):
            row_max, row_sum, weighted = held
            scores = (
                jnp.einsum(
                    "qgjd,kgd->gjqk", query_groups, key_rows, preferred_element_type=jnp.float32
                )
                * score_scale
            )
            key_pos = first_key + jnp.arange(key_rows.shape[0], dtype=jnp.int32)
            allowed = key_pos[None, :] <= query_pos[:, None]
            scores = jnp.where(allowed, scores, -1e30)
            new_max = jnp.maximum(row_max, jnp.max(scores, axis=-1))
            rescale = jnp.exp(row_max - new_max)
            weights_exp = jnp.where(allowed, jnp.exp(scores - new_max[..., None]), 0.0)
            row_sum = row_sum * rescale + jnp.sum(weights_exp, axis=-1)
            weighted = weighted * rescale[..., None] + jnp.einsum(
                "gjqk,kgd->gjqd",
                weights_exp.astype(jnp.bfloat16),
                value_rows,
                preferred_element_type=jnp.float32,
            )
            return (new_max, row_sum, weighted)

        return (lax.cond(first_key <= last_query, absorb, lambda held: held, running), None)

    start_state = (
        jnp.full((kv_count, per_key, rows_here), -1e30, jnp.float32),
        jnp.zeros((kv_count, per_key, rows_here), jnp.float32),
        jnp.zeros((kv_count, per_key, rows_here, HEAD_DIM), jnp.float32),
    )
    running = start_state
    both = gathered(jnp.concatenate([keys, values], axis=1), CTX)
    both = both.reshape(-1, both.shape[-1])
    key_piece = both[:, : keys.shape[1]]
    value_piece = both[:, keys.shape[1] :]
    count = key_piece.shape[0]
    width = math.gcd(count, 1024)
    blocks = count // width
    key_rows = key_piece.reshape(blocks, width, kv_count, HEAD_DIM)
    value_rows = value_piece.reshape(blocks, width, kv_count, HEAD_DIM)
    starts = width * jnp.arange(blocks, dtype=jnp.int32)
    running, unused = lax.scan(key_block, running, (key_rows, value_rows, starts))
    row_max, row_sum, weighted = running
    mixed = (weighted / row_sum[..., None]).transpose(2, 0, 1, 3).reshape(rows_here, -1)
    return mixed.astype(jnp.bfloat16)


def take_half(array, axis_dim, section):
    width = array.shape[axis_dim] // 2
    return lax.dynamic_slice_in_dim(array, section * width, width, axis_dim)


def per_device(
    resid_in,
    ssm_input,
    ssm_gate,
    ssm_in_b,
    ssm_out_c,
    step_size,
    decay_rate,
    skip_gain,
    norm_gain,
    queries,
    keys,
    values,
    out_weights,
):
    section = lax.axis_index("pipe")
    ctx_rank = lax.axis_index("y") * lax.axis_size("zc") + lax.axis_index("zc")
    mamba_part = mamba_mixer(
        take_half(ssm_input, 1, section),
        take_half(ssm_gate, 1, section),
        take_half(ssm_in_b, 1, section),
        take_half(ssm_out_c, 1, section),
        take_half(step_size, 1, section),
        take_half(decay_rate, 0, section),
        take_half(skip_gain, 0, section),
        take_half(norm_gain, 0, section),
    )
    attn_part = attention(
        take_half(queries, 1, section),
        take_half(keys, 1, section),
        take_half(values, 1, section),
        ctx_rank,
    )
    outgoing = jnp.where(section == 0, attn_part, mamba_part)
    kept_half = jnp.where(section == 0, mamba_part, attn_part)
    incoming = from_partner(outgoing, "pipe", 0)
    mixed_rows = jnp.where(
        section == 0,
        jnp.concatenate([kept_half, incoming], axis=1),
        jnp.concatenate([incoming, kept_half], axis=1),
    )
    inner = lax.axis_size("zc")
    tp_rank = lax.axis_index("tp")
    rows = gathered(mixed_rows, "zc").reshape(-1, mixed_rows.shape[1])
    columns = gathered(out_weights[0], "y")
    partial_value = jnp.einsum(
        "tc,ycr->tyr", rows, columns, preferred_element_type=jnp.float32
    )
    half = partial_value.shape[1] // 2
    kept = jnp.where(tp_rank == 0, partial_value[:, :half], partial_value[:, half:])
    sent = jnp.where(tp_rank == 0, partial_value[:, half:], partial_value[:, :half])
    summed = kept + from_partner(sent.astype(jnp.bfloat16), "tp", 0).astype(jnp.float32)
    pieces = summed.reshape((inner, -1) + summed.shape[1:]).astype(jnp.bfloat16)
    pieces = lax.all_to_all(pieces, "zc", 0, 0)
    projected = pieces.transpose(1, 2, 0, 3).reshape(pieces.shape[1], -1).astype(jnp.float32)
    own_section = (resid_in.astype(jnp.float32) + projected).astype(jnp.bfloat16)
    received = shifted(own_section, "pipe", 1)
    second_section = (received.astype(jnp.float32) + projected).astype(jnp.bfloat16)
    return jnp.where(section == 0, own_section, second_section)[None]


def solution(mesh):
    pipe, ctx, tp = (mesh.shape[name] for name in ("pipe", "ctx", "tp"))
    outer = 4 if ctx % 4 == 0 else 1
    split = jax.sharding.Mesh(
        mesh.devices.reshape(pipe, outer, ctx // outer, tp), ("pipe", "y", "zc", "tp")
    )
    return jax.shard_map(
        per_device,
        mesh=split,
        in_specs=(
            P(CTX, "tp"),
            P(CTX, "tp"),
            P(CTX, "tp"),
            P(CTX, "tp"),
            P(CTX, "tp"),
            P(CTX, "tp"),
            P("tp"),
            P("tp"),
            P("tp"),
            P(CTX, "tp"),
            P(CTX, "tp"),
            P(CTX, "tp"),
            P("pipe", "tp", CTX),
        ),
        out_specs=P("pipe", CTX, "tp"),
        check_vma=False,
    )
```

```python
import math

import jax
import jax.numpy as jnp
from jax import lax
from jax.sharding import PartitionSpec as P

MHEAD_DIM = 64
STATE = 128
SCAN_BLOCK = 128
HEAD_DIM = 128


exact_mode = lax.Precision.HIGHEST
norm_eps = 1e-05


def entering_2(x, axis, combine, identity):
    peers, position = (lax.axis_size(axis), lax.axis_index(axis))
    everything = jax.tree.map(
        lambda part, kind: lax.all_gather(part.astype(kind), axis), x, (jnp.bfloat16, jnp.bfloat16)
    )
    start = jax.tree.map(
        lambda part, zero: jnp.broadcast_to(jnp.asarray(zero, part.dtype), part.shape), x, identity
    )

    def turn(k, before):
        reached = k < position
        new = combine(
            before, jax.tree.map(lambda part, own: part[k].astype(own.dtype), everything, x)
        )
        return jax.tree.map(lambda a, b: jnp.where(reached, a, b), new, before)

    return lax.fori_loop(0, peers, turn, start)


CTX = ("y", "zc")


def gathered(x, axis):
    peers = lax.axis_size(axis)
    spread = jnp.broadcast_to(x[None], (peers,) + x.shape)
    return lax.all_to_all(spread, axis, 0, 0)


def entering_states(through_log, local_state, riders):
    outer = lax.axis_size("y")
    inner = lax.axis_size("zc")
    peers = outer * inner
    rank = lax.axis_index("y") * inner + lax.axis_index("zc")
    logs = gathered(through_log, CTX)
    logs = logs.reshape((peers,) + through_log.shape)
    places = jnp.arange(peers, dtype=jnp.int32)

    def span_weight(k, upto):
        inside = (places[None, :] > k[:, None]) & (places[None, :] < upto)
        summed = jnp.sum(jnp.where(inside[:, :, None, None], logs[None], 0.0), axis=1)
        return jnp.where((k < upto)[:, None, None], jnp.exp(summed), 0.0)

    first = lax.axis_index("y") * inner
    state_size = local_state.size
    payload = jnp.concatenate(
        [local_state.astype(jnp.bfloat16).reshape(-1), riders.reshape(-1)]
    )
    near_all = gathered(payload, "zc")
    near = near_all[:, :state_size].reshape((inner,) + local_state.shape).astype(jnp.float32)
    near_riders = near_all[:, state_size:]
    near_ids = first + jnp.arange(inner, dtype=jnp.int32)
    own_part = jnp.einsum(
        "kgj,kgjpn->gjpn", span_weight(near_ids, rank), near, precision=exact_mode
    )
    group_end = first + inner
    group_total = jnp.einsum(
        "kgj,kgjpn->gjpn", span_weight(near_ids, group_end), near, precision=exact_mode
    )
    payload = jnp.concatenate(
        [group_total.astype(jnp.bfloat16).reshape(-1), near_riders.reshape(-1)]
    )
    far_all = gathered(payload, "y")
    far = far_all[:, :state_size].reshape((outer,) + local_state.shape).astype(jnp.float32)
    all_riders = far_all[:, state_size:].reshape((peers * riders.shape[0],) + riders.shape[1:])
    far_ends = (jnp.arange(outer, dtype=jnp.int32) + 1) * inner - 1
    far_weight = span_weight(far_ends, rank)
    far_weight = jnp.where((far_ends < first)[:, None, None], far_weight, 0.0)
    far_part = jnp.einsum("kgj,kgjpn->gjpn", far_weight, far, precision=exact_mode)
    return own_part + far_part, all_riders


def from_partner(block, axis, distance):
    count = lax.axis_size(axis)
    route = []
    for low in range(count):
        high = low | 1 << distance
        if high != low and high < count:
            route += [(low, high), (high, low)]
    return lax.ppermute(block, axis, route)


def shifted(x, axis, by):
    peers = lax.axis_size(axis)
    pairs = [(i, i + by) for i in range(peers) if 0 <= i + by < peers]
    return lax.ppermute(x, axis, pairs)


def block_scan(state_now, inputs_x, input_b, output_c, step_rows, log_decay):
    width = inputs_x.shape[0]
    groups = inputs_x.shape[1]
    per_group = inputs_x.shape[2]
    running = jnp.cumsum(log_decay, axis=0)
    spread = running[:, None, :] - running[None, :, :]
    causal = (
        jnp.arange(width, dtype=jnp.int32)[:, None] >= jnp.arange(width, dtype=jnp.int32)[None, :]
    )
    decay_mat = jnp.exp(jnp.where(causal[:, :, None], spread, -jnp.inf))
    decay_mat = decay_mat.reshape(width, width, groups, per_group).transpose(2, 3, 0, 1)
    cross_cb = jnp.einsum("tgn,sgn->gts", output_c, input_b, precision=exact_mode)
    step_cols = step_rows.reshape(width, groups, per_group).transpose(1, 2, 0)
    mixing = cross_cb[:, None, :, :] * decay_mat * step_cols[:, :, None, :]
    within = jnp.einsum("gjts,sgjp->tgjp", mixing, inputs_x, precision=exact_mode)
    entry = jnp.exp(running).reshape(width, groups, per_group)
    carried = (
        jnp.einsum("tgn,gjpn->tgjp", output_c, state_now, precision=exact_mode)
        * entry[:, :, :, None]
    )
    tail_weight = (jnp.exp(running[-1][None, :] - running) * step_rows).reshape(
        width, groups, per_group
    )
    leaving = jnp.exp(running[-1]).reshape(groups, per_group)
    state_next = leaving[:, :, None, None] * state_now + jnp.einsum(
        "sgj,sgjp,sgn->gjpn", tail_weight, inputs_x, input_b, precision=exact_mode
    )
    return (state_next, within + carried)


def gate_norm(values_y, gate_in, gains, groups):
    rows_here = values_y.shape[0]
    gated = values_y * jax.nn.silu(gate_in.astype(jnp.float32))
    grouped = gated.reshape(rows_here, groups, -1)
    meansq = jnp.mean(grouped * grouped, axis=-1, keepdims=True)
    scaled = (grouped * lax.rsqrt(meansq + norm_eps)).reshape(rows_here, -1)
    return (scaled * gains[None, :]).astype(jnp.bfloat16)


def join_states(earlier, later):
    return (earlier[0] * later[0], later[0][:, :, None, None] * earlier[1] + later[1])


def mamba_mixer(
    ssm_input, ssm_gate, ssm_in_b, ssm_out_c, step_size, decay_rate, skip_gain, norm_gain, riders
):
    rows_here = ssm_input.shape[0]
    head_count = decay_rate.shape[0]
    groups = ssm_in_b.shape[1] // STATE
    per_group = head_count // groups
    block_count = rows_here // SCAN_BLOCK
    log_decay = -step_size * decay_rate[None, :]
    inputs_x = ssm_input.reshape(block_count, SCAN_BLOCK, groups, per_group, MHEAD_DIM)
    input_b = ssm_in_b.reshape(block_count, SCAN_BLOCK, groups, STATE)
    output_c = ssm_out_c.reshape(block_count, SCAN_BLOCK, groups, STATE)

    def block_turn(state_now, block_data):
        part_x, part_b, part_c, part_step, part_log = block_data
        return block_scan(
            state_now,
            part_x.astype(jnp.float32),
            part_b.astype(jnp.float32),
            part_c.astype(jnp.float32),
            part_step,
            part_log,
        )

    start_state = jnp.zeros((groups, per_group, MHEAD_DIM, STATE), jnp.float32)
    local_state, pieces = lax.scan(
        block_turn,
        start_state,
        (
            inputs_x,
            input_b,
            output_c,
            step_size.reshape(block_count, SCAN_BLOCK, head_count),
            log_decay.reshape(block_count, SCAN_BLOCK, head_count),
        ),
    )
    running = jnp.cumsum(log_decay, axis=0)
    entering, all_riders = entering_states(
        running[-1].reshape(groups, per_group), local_state, riders
    )
    output_all = ssm_out_c.astype(jnp.float32).reshape(rows_here, groups, STATE)
    carried = (
        jnp.einsum("tgn,gjpn->tgjp", output_all, entering, precision=exact_mode)
        * jnp.exp(running).reshape(rows_here, groups, per_group)[:, :, :, None]
    )
    skipped = (
        ssm_input.astype(jnp.float32).reshape(rows_here, groups, per_group, MHEAD_DIM)
        * skip_gain.reshape(groups, per_group)[None, :, :, None]
    )
    values_y = pieces.reshape(rows_here, groups, per_group, MHEAD_DIM) + carried + skipped
    return gate_norm(values_y.reshape(rows_here, -1), ssm_gate, norm_gain, groups), all_riders


def attention(queries, both, key_width, ctx_rank):
    rows_here = queries.shape[0]
    kv_count = key_width // HEAD_DIM
    per_key = queries.shape[1] // HEAD_DIM // kv_count
    query_groups = queries.reshape(rows_here, kv_count, per_key, HEAD_DIM)
    query_pos = ctx_rank * rows_here + jnp.arange(rows_here, dtype=jnp.int32)
    last_query = query_pos[-1]
    score_scale = 1.0 / math.sqrt(HEAD_DIM)

    def key_block(running, block_data):
        key_rows, value_rows, first_key = block_data

        def absorb(held):
            row_max, row_sum, weighted = held
            scores = (
                jnp.einsum(
                    "qgjd,kgd->gjqk", query_groups, key_rows, preferred_element_type=jnp.float32
                )
                * score_scale
            )
            key_pos = first_key + jnp.arange(key_rows.shape[0], dtype=jnp.int32)
            allowed = key_pos[None, :] <= query_pos[:, None]
            scores = jnp.where(allowed, scores, -1e30)
            new_max = jnp.maximum(row_max, jnp.max(scores, axis=-1))
            rescale = jnp.exp(row_max - new_max)
            weights_exp = jnp.where(allowed, jnp.exp(scores - new_max[..., None]), 0.0)
            row_sum = row_sum * rescale + jnp.sum(weights_exp, axis=-1)
            weighted = weighted * rescale[..., None] + jnp.einsum(
                "gjqk,kgd->gjqd",
                weights_exp.astype(jnp.bfloat16),
                value_rows,
                preferred_element_type=jnp.float32,
            )
            return (new_max, row_sum, weighted)

        return (lax.cond(first_key <= last_query, absorb, lambda held: held, running), None)

    start_state = (
        jnp.full((kv_count, per_key, rows_here), -1e30, jnp.float32),
        jnp.zeros((kv_count, per_key, rows_here), jnp.float32),
        jnp.zeros((kv_count, per_key, rows_here, HEAD_DIM), jnp.float32),
    )
    running = start_state
    key_piece = both[:, :key_width]
    value_piece = both[:, key_width:]
    count = key_piece.shape[0]
    width = math.gcd(count, 1024)
    blocks = count // width
    key_rows = key_piece.reshape(blocks, width, kv_count, HEAD_DIM)
    value_rows = value_piece.reshape(blocks, width, kv_count, HEAD_DIM)
    starts = width * jnp.arange(blocks, dtype=jnp.int32)
    running, unused = lax.scan(key_block, running, (key_rows, value_rows, starts))
    row_max, row_sum, weighted = running
    mixed = (weighted / row_sum[..., None]).transpose(2, 0, 1, 3).reshape(rows_here, -1)
    return mixed.astype(jnp.bfloat16)


def take_half(array, axis_dim, section):
    width = array.shape[axis_dim] // 2
    return lax.dynamic_slice_in_dim(array, section * width, width, axis_dim)


def per_device(
    resid_in,
    ssm_input,
    ssm_gate,
    ssm_in_b,
    ssm_out_c,
    step_size,
    decay_rate,
    skip_gain,
    norm_gain,
    queries,
    keys,
    values,
    out_weights,
):
    section = lax.axis_index("pipe")
    ctx_rank = lax.axis_index("y") * lax.axis_size("zc") + lax.axis_index("zc")
    key_half = take_half(keys, 1, section)
    value_half = take_half(values, 1, section)
    mamba_part, both = mamba_mixer(
        take_half(ssm_input, 1, section),
        take_half(ssm_gate, 1, section),
        take_half(ssm_in_b, 1, section),
        take_half(ssm_out_c, 1, section),
        take_half(step_size, 1, section),
        take_half(decay_rate, 0, section),
        take_half(skip_gain, 0, section),
        take_half(norm_gain, 0, section),
        jnp.concatenate([key_half, value_half], axis=1),
    )
    attn_part = attention(take_half(queries, 1, section), both, key_half.shape[1], ctx_rank)
    outgoing = jnp.where(section == 0, attn_part, mamba_part)
    kept_half = jnp.where(section == 0, mamba_part, attn_part)
    incoming = from_partner(outgoing, "pipe", 0)
    mixed_rows = jnp.where(
        section == 0,
        jnp.concatenate([kept_half, incoming], axis=1),
        jnp.concatenate([incoming, kept_half], axis=1),
    )
    partial_value = jnp.dot(
        mixed_rows,
        lax.all_gather(out_weights, CTX, axis=2, tiled=True)[0],
        preferred_element_type=jnp.float32,
    )
    half = partial_value.shape[1] // 2
    tp_rank = lax.axis_index("tp")
    kept = jnp.where(tp_rank == 0, partial_value[:, :half], partial_value[:, half:])
    sent = jnp.where(tp_rank == 0, partial_value[:, half:], partial_value[:, :half])
    projected = kept + from_partner(sent.astype(jnp.bfloat16), "tp", 0).astype(jnp.float32)
    own_section = (resid_in.astype(jnp.float32) + projected).astype(jnp.bfloat16)
    received = shifted(own_section, "pipe", 1)
    second_section = (received.astype(jnp.float32) + projected).astype(jnp.bfloat16)
    return jnp.where(section == 0, own_section, second_section)[None]


def solution(mesh):
    pipe, ctx, tp = (mesh.shape[name] for name in ("pipe", "ctx", "tp"))
    outer = 4 if ctx % 4 == 0 else 1
    split = jax.sharding.Mesh(
        mesh.devices.reshape(pipe, outer, ctx // outer, tp), ("pipe", "y", "zc", "tp")
    )
    return jax.shard_map(
        per_device,
        mesh=split,
        in_specs=(
            P(CTX, "tp"),
            P(CTX, "tp"),
            P(CTX, "tp"),
            P(CTX, "tp"),
            P(CTX, "tp"),
            P(CTX, "tp"),
            P("tp"),
            P("tp"),
            P("tp"),
            P(CTX, "tp"),
            P(CTX, "tp"),
            P(CTX, "tp"),
            P("pipe", "tp", CTX),
        ),
        out_specs=P("pipe", CTX, "tp"),
        check_vma=False,
    )
```

```python
import math

import jax
import jax.numpy as jnp
from jax import lax
from jax.sharding import PartitionSpec as P

MHEAD_DIM = 64
STATE = 128
SCAN_BLOCK = 128
HEAD_DIM = 128


exact_mode = lax.Precision.HIGHEST
norm_eps = 1e-05


def entering_2(x, axis, combine, identity):
    peers, position = (lax.axis_size(axis), lax.axis_index(axis))
    everything = jax.tree.map(
        lambda part, kind: lax.all_gather(part.astype(kind), axis), x, (jnp.bfloat16, jnp.bfloat16)
    )
    start = jax.tree.map(
        lambda part, zero: jnp.broadcast_to(jnp.asarray(zero, part.dtype), part.shape), x, identity
    )

    def turn(k, before):
        reached = k < position
        new = combine(
            before, jax.tree.map(lambda part, own: part[k].astype(own.dtype), everything, x)
        )
        return jax.tree.map(lambda a, b: jnp.where(reached, a, b), new, before)

    return lax.fori_loop(0, peers, turn, start)


CTX = ("y", "zc")


def gathered(x, axis):
    peers = lax.axis_size(axis)
    spread = jnp.broadcast_to(x[None], (peers,) + x.shape)
    return lax.all_to_all(spread, axis, 0, 0)


def entering_states(through_log, local_state, riders):
    outer = lax.axis_size("y")
    inner = lax.axis_size("zc")
    peers = outer * inner
    rank = lax.axis_index("y") * inner + lax.axis_index("zc")
    logs = gathered(through_log, CTX)
    logs = logs.reshape((peers,) + through_log.shape)
    places = jnp.arange(peers, dtype=jnp.int32)

    def span_weight(k, upto):
        inside = (places[None, :] > k[:, None]) & (places[None, :] < upto)
        summed = jnp.sum(jnp.where(inside[:, :, None, None], logs[None], 0.0), axis=1)
        return jnp.where((k < upto)[:, None, None], jnp.exp(summed), 0.0)

    first = lax.axis_index("y") * inner
    lanes = local_state.shape[-1]
    state_rows = local_state.size // lanes
    rider_rows = riders.size // lanes
    payload = jnp.concatenate(
        [
            local_state.astype(jnp.bfloat16).reshape(state_rows, lanes),
            riders.reshape(riders.shape[0], -1, lanes).reshape(rider_rows, lanes),
        ]
    )
    near_all = gathered(payload, "zc")
    near = near_all[:, :state_rows].reshape((inner,) + local_state.shape).astype(jnp.float32)
    near_riders = near_all[:, state_rows:].reshape(inner * rider_rows, lanes)
    near_ids = first + jnp.arange(inner, dtype=jnp.int32)
    own_part = jnp.einsum(
        "kgj,kgjpn->gjpn", span_weight(near_ids, rank), near, precision=exact_mode
    )
    group_end = first + inner
    group_total = jnp.einsum(
        "kgj,kgjpn->gjpn", span_weight(near_ids, group_end), near, precision=exact_mode
    )
    payload = jnp.concatenate(
        [group_total.astype(jnp.bfloat16).reshape(state_rows, lanes), near_riders]
    )
    far_all = gathered(payload, "y")
    far = far_all[:, :state_rows].reshape((outer,) + local_state.shape).astype(jnp.float32)
    all_riders = far_all[:, state_rows:].reshape(
        (peers * riders.shape[0], -1, lanes)
    ).reshape(peers * riders.shape[0], riders.shape[1])
    far_ends = (jnp.arange(outer, dtype=jnp.int32) + 1) * inner - 1
    far_weight = span_weight(far_ends, rank)
    far_weight = jnp.where((far_ends < first)[:, None, None], far_weight, 0.0)
    far_part = jnp.einsum("kgj,kgjpn->gjpn", far_weight, far, precision=exact_mode)
    return own_part + far_part, all_riders


def from_partner(block, axis, distance):
    count = lax.axis_size(axis)
    route = []
    for low in range(count):
        high = low | 1 << distance
        if high != low and high < count:
            route += [(low, high), (high, low)]
    return lax.ppermute(block, axis, route)


def shifted(x, axis, by):
    peers = lax.axis_size(axis)
    pairs = [(i, i + by) for i in range(peers) if 0 <= i + by < peers]
    return lax.ppermute(x, axis, pairs)


def block_scan(state_now, inputs_x, input_b, output_c, step_rows, log_decay):
    width = inputs_x.shape[0]
    groups = inputs_x.shape[1]
    per_group = inputs_x.shape[2]
    running = jnp.cumsum(log_decay, axis=0)
    spread = running[:, None, :] - running[None, :, :]
    causal = (
        jnp.arange(width, dtype=jnp.int32)[:, None] >= jnp.arange(width, dtype=jnp.int32)[None, :]
    )
    decay_mat = jnp.exp(jnp.where(causal[:, :, None], spread, -jnp.inf))
    decay_mat = decay_mat.reshape(width, width, groups, per_group).transpose(2, 3, 0, 1)
    cross_cb = jnp.einsum("tgn,sgn->gts", output_c, input_b, precision=exact_mode)
    step_cols = step_rows.reshape(width, groups, per_group).transpose(1, 2, 0)
    mixing = cross_cb[:, None, :, :] * decay_mat * step_cols[:, :, None, :]
    within = jnp.einsum("gjts,sgjp->tgjp", mixing, inputs_x, precision=exact_mode)
    entry = jnp.exp(running).reshape(width, groups, per_group)
    carried = (
        jnp.einsum("tgn,gjpn->tgjp", output_c, state_now, precision=exact_mode)
        * entry[:, :, :, None]
    )
    tail_weight = (jnp.exp(running[-1][None, :] - running) * step_rows).reshape(
        width, groups, per_group
    )
    leaving = jnp.exp(running[-1]).reshape(groups, per_group)
    state_next = leaving[:, :, None, None] * state_now + jnp.einsum(
        "sgj,sgjp,sgn->gjpn", tail_weight, inputs_x, input_b, precision=exact_mode
    )
    return (state_next, within + carried)


def gate_norm(values_y, gate_in, gains, groups):
    rows_here = values_y.shape[0]
    gated = values_y * jax.nn.silu(gate_in.astype(jnp.float32))
    grouped = gated.reshape(rows_here, groups, -1)
    meansq = jnp.mean(grouped * grouped, axis=-1, keepdims=True)
    scaled = (grouped * lax.rsqrt(meansq + norm_eps)).reshape(rows_here, -1)
    return (scaled * gains[None, :]).astype(jnp.bfloat16)


def join_states(earlier, later):
    return (earlier[0] * later[0], later[0][:, :, None, None] * earlier[1] + later[1])


def mamba_mixer(
    ssm_input, ssm_gate, ssm_in_b, ssm_out_c, step_size, decay_rate, skip_gain, norm_gain, riders
):
    rows_here = ssm_input.shape[0]
    head_count = decay_rate.shape[0]
    groups = ssm_in_b.shape[1] // STATE
    per_group = head_count // groups
    block_count = rows_here // SCAN_BLOCK
    log_decay = -step_size * decay_rate[None, :]
    inputs_x = ssm_input.reshape(block_count, SCAN_BLOCK, groups, per_group, MHEAD_DIM)
    input_b = ssm_in_b.reshape(block_count, SCAN_BLOCK, groups, STATE)
    output_c = ssm_out_c.reshape(block_count, SCAN_BLOCK, groups, STATE)

    def block_turn(state_now, block_data):
        part_x, part_b, part_c, part_step, part_log = block_data
        return block_scan(
            state_now,
            part_x.astype(jnp.float32),
            part_b.astype(jnp.float32),
            part_c.astype(jnp.float32),
            part_step,
            part_log,
        )

    start_state = jnp.zeros((groups, per_group, MHEAD_DIM, STATE), jnp.float32)
    local_state, pieces = lax.scan(
        block_turn,
        start_state,
        (
            inputs_x,
            input_b,
            output_c,
            step_size.reshape(block_count, SCAN_BLOCK, head_count),
            log_decay.reshape(block_count, SCAN_BLOCK, head_count),
        ),
    )
    running = jnp.cumsum(log_decay, axis=0)
    entering, all_riders = entering_states(
        running[-1].reshape(groups, per_group), local_state, riders
    )
    output_all = ssm_out_c.astype(jnp.float32).reshape(rows_here, groups, STATE)
    carried = (
        jnp.einsum("tgn,gjpn->tgjp", output_all, entering, precision=exact_mode)
        * jnp.exp(running).reshape(rows_here, groups, per_group)[:, :, :, None]
    )
    skipped = (
        ssm_input.astype(jnp.float32).reshape(rows_here, groups, per_group, MHEAD_DIM)
        * skip_gain.reshape(groups, per_group)[None, :, :, None]
    )
    values_y = pieces.reshape(rows_here, groups, per_group, MHEAD_DIM) + carried + skipped
    return gate_norm(values_y.reshape(rows_here, -1), ssm_gate, norm_gain, groups), all_riders


def attention(queries, both, key_width, ctx_rank):
    rows_here = queries.shape[0]
    kv_count = key_width // HEAD_DIM
    per_key = queries.shape[1] // HEAD_DIM // kv_count
    query_groups = queries.reshape(rows_here, kv_count, per_key, HEAD_DIM)
    query_pos = ctx_rank * rows_here + jnp.arange(rows_here, dtype=jnp.int32)
    last_query = query_pos[-1]
    score_scale = 1.0 / math.sqrt(HEAD_DIM)

    def key_block(running, block_data):
        key_rows, value_rows, first_key = block_data

        def absorb(held):
            row_max, row_sum, weighted = held
            scores = (
                jnp.einsum(
                    "qgjd,kgd->gjqk", query_groups, key_rows, preferred_element_type=jnp.float32
                )
                * score_scale
            )
            key_pos = first_key + jnp.arange(key_rows.shape[0], dtype=jnp.int32)
            allowed = key_pos[None, :] <= query_pos[:, None]
            scores = jnp.where(allowed, scores, -1e30)
            new_max = jnp.maximum(row_max, jnp.max(scores, axis=-1))
            rescale = jnp.exp(row_max - new_max)
            weights_exp = jnp.where(allowed, jnp.exp(scores - new_max[..., None]), 0.0)
            row_sum = row_sum * rescale + jnp.sum(weights_exp, axis=-1)
            weighted = weighted * rescale[..., None] + jnp.einsum(
                "gjqk,kgd->gjqd",
                weights_exp.astype(jnp.bfloat16),
                value_rows,
                preferred_element_type=jnp.float32,
            )
            return (new_max, row_sum, weighted)

        return (lax.cond(first_key <= last_query, absorb, lambda held: held, running), None)

    start_state = (
        jnp.full((kv_count, per_key, rows_here), -1e30, jnp.float32),
        jnp.zeros((kv_count, per_key, rows_here), jnp.float32),
        jnp.zeros((kv_count, per_key, rows_here, HEAD_DIM), jnp.float32),
    )
    running = start_state
    key_piece = both[:, :key_width]
    value_piece = both[:, key_width:]
    count = key_piece.shape[0]
    width = math.gcd(count, 1024)
    blocks = count // width
    key_rows = key_piece.reshape(blocks, width, kv_count, HEAD_DIM)
    value_rows = value_piece.reshape(blocks, width, kv_count, HEAD_DIM)
    starts = width * jnp.arange(blocks, dtype=jnp.int32)
    running, unused = lax.scan(key_block, running, (key_rows, value_rows, starts))
    row_max, row_sum, weighted = running
    mixed = (weighted / row_sum[..., None]).transpose(2, 0, 1, 3).reshape(rows_here, -1)
    return mixed.astype(jnp.bfloat16)


def take_half(array, axis_dim, section):
    width = array.shape[axis_dim] // 2
    return lax.dynamic_slice_in_dim(array, section * width, width, axis_dim)


def per_device(
    resid_in,
    ssm_input,
    ssm_gate,
    ssm_in_b,
    ssm_out_c,
    step_size,
    decay_rate,
    skip_gain,
    norm_gain,
    queries,
    keys,
    values,
    out_weights,
):
    section = lax.axis_index("pipe")
    ctx_rank = lax.axis_index("y") * lax.axis_size("zc") + lax.axis_index("zc")
    key_half = take_half(keys, 1, section)
    value_half = take_half(values, 1, section)
    mamba_part, both = mamba_mixer(
        take_half(ssm_input, 1, section),
        take_half(ssm_gate, 1, section),
        take_half(ssm_in_b, 1, section),
        take_half(ssm_out_c, 1, section),
        take_half(step_size, 1, section),
        take_half(decay_rate, 0, section),
        take_half(skip_gain, 0, section),
        take_half(norm_gain, 0, section),
        jnp.concatenate([key_half, value_half], axis=1),
    )
    attn_part = attention(take_half(queries, 1, section), both, key_half.shape[1], ctx_rank)
    outgoing = jnp.where(section == 0, attn_part, mamba_part)
    kept_half = jnp.where(section == 0, mamba_part, attn_part)
    incoming = from_partner(outgoing, "pipe", 0)
    mixed_rows = jnp.where(
        section == 0,
        jnp.concatenate([kept_half, incoming], axis=1),
        jnp.concatenate([incoming, kept_half], axis=1),
    )
    partial_value = jnp.dot(
        mixed_rows,
        lax.all_gather(out_weights, CTX, axis=2, tiled=True)[0],
        preferred_element_type=jnp.float32,
    )
    half = partial_value.shape[1] // 2
    tp_rank = lax.axis_index("tp")
    kept = jnp.where(tp_rank == 0, partial_value[:, :half], partial_value[:, half:])
    sent = jnp.where(tp_rank == 0, partial_value[:, half:], partial_value[:, :half])
    projected = kept + from_partner(sent.astype(jnp.bfloat16), "tp", 0).astype(jnp.float32)
    own_section = (resid_in.astype(jnp.float32) + projected).astype(jnp.bfloat16)
    received = shifted(own_section, "pipe", 1)
    second_section = (received.astype(jnp.float32) + projected).astype(jnp.bfloat16)
    return jnp.where(section == 0, own_section, second_section)[None]


def solution(mesh):
    pipe, ctx, tp = (mesh.shape[name] for name in ("pipe", "ctx", "tp"))
    outer = 4 if ctx % 4 == 0 else 1
    split = jax.sharding.Mesh(
        mesh.devices.reshape(pipe, outer, ctx // outer, tp), ("pipe", "y", "zc", "tp")
    )
    return jax.shard_map(
        per_device,
        mesh=split,
        in_specs=(
            P(CTX, "tp"),
            P(CTX, "tp"),
            P(CTX, "tp"),
            P(CTX, "tp"),
            P(CTX, "tp"),
            P(CTX, "tp"),
            P("tp"),
            P("tp"),
            P("tp"),
            P(CTX, "tp"),
            P(CTX, "tp"),
            P(CTX, "tp"),
            P("pipe", "tp", CTX),
        ),
        out_specs=P("pipe", CTX, "tp"),
        check_vma=False,
    )
```

```python
import math

import jax
import jax.numpy as jnp
from jax import lax
from jax.sharding import PartitionSpec as P

MHEAD_DIM = 64
STATE = 128
SCAN_BLOCK = 128
HEAD_DIM = 128


exact_mode = lax.Precision.HIGHEST
norm_eps = 1e-05


def entering_2(x, axis, combine, identity):
    peers, position = (lax.axis_size(axis), lax.axis_index(axis))
    everything = jax.tree.map(
        lambda part, kind: lax.all_gather(part.astype(kind), axis), x, (jnp.bfloat16, jnp.bfloat16)
    )
    start = jax.tree.map(
        lambda part, zero: jnp.broadcast_to(jnp.asarray(zero, part.dtype), part.shape), x, identity
    )

    def turn(k, before):
        reached = k < position
        new = combine(
            before, jax.tree.map(lambda part, own: part[k].astype(own.dtype), everything, x)
        )
        return jax.tree.map(lambda a, b: jnp.where(reached, a, b), new, before)

    return lax.fori_loop(0, peers, turn, start)


CTX = ("y", "zc")


def gathered(x, axis):
    peers = lax.axis_size(axis)
    spread = jnp.broadcast_to(x[None], (peers,) + x.shape)
    return lax.all_to_all(spread, axis, 0, 0)


def entering_states(through_log, local_state, riders):
    outer = lax.axis_size("y")
    inner = lax.axis_size("zc")
    peers = outer * inner
    rank = lax.axis_index("y") * inner + lax.axis_index("zc")
    logs = gathered(through_log, CTX)
    logs = logs.reshape((peers,) + through_log.shape)
    places = jnp.arange(peers, dtype=jnp.int32)

    def span_weight(k, upto):
        inside = (places[None, :] > k[:, None]) & (places[None, :] < upto)
        summed = jnp.sum(jnp.where(inside[:, :, None, None], logs[None], 0.0), axis=1)
        return jnp.where((k < upto)[:, None, None], jnp.exp(summed), 0.0)

    first = lax.axis_index("y") * inner
    lanes = local_state.shape[-1]
    state_rows = local_state.size // lanes
    rider_rows = riders.size // lanes
    payload = jnp.concatenate(
        [
            local_state.astype(jnp.bfloat16).reshape(state_rows, lanes),
            riders.reshape(riders.shape[0], -1, lanes).reshape(rider_rows, lanes),
        ]
    )
    near_all = gathered(payload, "zc")
    near = near_all[:, :state_rows].reshape((inner,) + local_state.shape).astype(jnp.float32)
    near_riders = near_all[:, state_rows:].reshape(inner * rider_rows, lanes)
    near_ids = first + jnp.arange(inner, dtype=jnp.int32)
    own_part = jnp.einsum(
        "kgj,kgjpn->gjpn", span_weight(near_ids, rank), near, precision=exact_mode
    )
    group_end = first + inner
    group_total = jnp.einsum(
        "kgj,kgjpn->gjpn", span_weight(near_ids, group_end), near, precision=exact_mode
    )
    payload = jnp.concatenate(
        [group_total.astype(jnp.bfloat16).reshape(state_rows, lanes), near_riders]
    )
    far_all = gathered(payload, "y")
    far = far_all[:, :state_rows].reshape((outer,) + local_state.shape).astype(jnp.float32)
    all_riders = far_all[:, state_rows:].reshape(
        (peers * riders.shape[0], -1, lanes)
    ).reshape(peers * riders.shape[0], riders.shape[1])
    far_ends = (jnp.arange(outer, dtype=jnp.int32) + 1) * inner - 1
    far_weight = span_weight(far_ends, rank)
    far_weight = jnp.where((far_ends < first)[:, None, None], far_weight, 0.0)
    far_part = jnp.einsum("kgj,kgjpn->gjpn", far_weight, far, precision=exact_mode)
    return own_part + far_part, all_riders


def from_partner(block, axis, distance):
    count = lax.axis_size(axis)
    route = []
    for low in range(count):
        high = low | 1 << distance
        if high != low and high < count:
            route += [(low, high), (high, low)]
    return lax.ppermute(block, axis, route)


def shifted(x, axis, by):
    peers = lax.axis_size(axis)
    pairs = [(i, i + by) for i in range(peers) if 0 <= i + by < peers]
    return lax.ppermute(x, axis, pairs)


def block_scan(state_now, inputs_x, input_b, output_c, step_rows, log_decay):
    width = inputs_x.shape[0]
    groups = inputs_x.shape[1]
    per_group = inputs_x.shape[2]
    running = jnp.cumsum(log_decay, axis=0)
    spread = running[:, None, :] - running[None, :, :]
    causal = (
        jnp.arange(width, dtype=jnp.int32)[:, None] >= jnp.arange(width, dtype=jnp.int32)[None, :]
    )
    decay_mat = jnp.exp(jnp.where(causal[:, :, None], spread, -jnp.inf))
    decay_mat = decay_mat.reshape(width, width, groups, per_group).transpose(2, 3, 0, 1)
    cross_cb = jnp.einsum("tgn,sgn->gts", output_c, input_b, precision=exact_mode)
    step_cols = step_rows.reshape(width, groups, per_group).transpose(1, 2, 0)
    mixing = cross_cb[:, None, :, :] * decay_mat * step_cols[:, :, None, :]
    within = jnp.einsum("gjts,sgjp->tgjp", mixing, inputs_x, precision=exact_mode)
    entry = jnp.exp(running).reshape(width, groups, per_group)
    carried = (
        jnp.einsum("tgn,gjpn->tgjp", output_c, state_now, precision=exact_mode)
        * entry[:, :, :, None]
    )
    tail_weight = (jnp.exp(running[-1][None, :] - running) * step_rows).reshape(
        width, groups, per_group
    )
    leaving = jnp.exp(running[-1]).reshape(groups, per_group)
    state_next = leaving[:, :, None, None] * state_now + jnp.einsum(
        "sgj,sgjp,sgn->gjpn", tail_weight, inputs_x, input_b, precision=exact_mode
    )
    return (state_next, within + carried)


def gate_norm(values_y, gate_in, gains, groups):
    rows_here = values_y.shape[0]
    gated = values_y * jax.nn.silu(gate_in.astype(jnp.float32))
    grouped = gated.reshape(rows_here, groups, -1)
    meansq = jnp.mean(grouped * grouped, axis=-1, keepdims=True)
    scaled = (grouped * lax.rsqrt(meansq + norm_eps)).reshape(rows_here, -1)
    return (scaled * gains[None, :]).astype(jnp.bfloat16)


def join_states(earlier, later):
    return (earlier[0] * later[0], later[0][:, :, None, None] * earlier[1] + later[1])


def mamba_mixer(
    ssm_input, ssm_gate, ssm_in_b, ssm_out_c, step_size, decay_rate, skip_gain, norm_gain, riders
):
    rows_here = ssm_input.shape[0]
    head_count = decay_rate.shape[0]
    groups = ssm_in_b.shape[1] // STATE
    per_group = head_count // groups
    block_count = rows_here // SCAN_BLOCK
    log_decay = -step_size * decay_rate[None, :]
    inputs_x = ssm_input.reshape(block_count, SCAN_BLOCK, groups, per_group, MHEAD_DIM)
    input_b = ssm_in_b.reshape(block_count, SCAN_BLOCK, groups, STATE)
    output_c = ssm_out_c.reshape(block_count, SCAN_BLOCK, groups, STATE)

    def block_turn(state_now, block_data):
        part_x, part_b, part_c, part_step, part_log = block_data
        return block_scan(
            state_now,
            part_x.astype(jnp.float32),
            part_b.astype(jnp.float32),
            part_c.astype(jnp.float32),
            part_step,
            part_log,
        )

    start_state = jnp.zeros((groups, per_group, MHEAD_DIM, STATE), jnp.float32)
    local_state, pieces = lax.scan(
        block_turn,
        start_state,
        (
            inputs_x,
            input_b,
            output_c,
            step_size.reshape(block_count, SCAN_BLOCK, head_count),
            log_decay.reshape(block_count, SCAN_BLOCK, head_count),
        ),
    )
    running = jnp.cumsum(log_decay, axis=0)
    entering, all_riders = entering_states(
        running[-1].reshape(groups, per_group), local_state, riders
    )
    output_all = ssm_out_c.astype(jnp.float32).reshape(rows_here, groups, STATE)
    carried = (
        jnp.einsum("tgn,gjpn->tgjp", output_all, entering, precision=exact_mode)
        * jnp.exp(running).reshape(rows_here, groups, per_group)[:, :, :, None]
    )
    skipped = (
        ssm_input.astype(jnp.float32).reshape(rows_here, groups, per_group, MHEAD_DIM)
        * skip_gain.reshape(groups, per_group)[None, :, :, None]
    )
    values_y = pieces.reshape(rows_here, groups, per_group, MHEAD_DIM) + carried + skipped
    return gate_norm(values_y.reshape(rows_here, -1), ssm_gate, norm_gain, groups), all_riders


def attention(queries, both, key_width, ctx_rank):
    rows_here = queries.shape[0]
    kv_count = key_width // HEAD_DIM
    per_key = queries.shape[1] // HEAD_DIM // kv_count
    query_groups = queries.reshape(rows_here, kv_count, per_key, HEAD_DIM)
    query_pos = ctx_rank * rows_here + jnp.arange(rows_here, dtype=jnp.int32)
    last_query = query_pos[-1]
    score_scale = 1.0 / math.sqrt(HEAD_DIM)

    def key_block(running, block_data):
        key_rows, value_rows, first_key = block_data

        def absorb(held):
            row_max, row_sum, weighted = held
            scores = (
                jnp.einsum(
                    "qgjd,kgd->gjqk", query_groups, key_rows, preferred_element_type=jnp.float32
                )
                * score_scale
            )
            key_pos = first_key + jnp.arange(key_rows.shape[0], dtype=jnp.int32)
            allowed = key_pos[None, :] <= query_pos[:, None]
            scores = jnp.where(allowed, scores, -1e30)
            new_max = jnp.maximum(row_max, jnp.max(scores, axis=-1))
            rescale = jnp.exp(row_max - new_max)
            weights_exp = jnp.where(allowed, jnp.exp(scores - new_max[..., None]), 0.0)
            row_sum = row_sum * rescale + jnp.sum(weights_exp, axis=-1)
            weighted = weighted * rescale[..., None] + jnp.einsum(
                "gjqk,kgd->gjqd",
                weights_exp.astype(jnp.bfloat16),
                value_rows,
                preferred_element_type=jnp.float32,
            )
            return (new_max, row_sum, weighted)

        return (lax.cond(first_key <= last_query, absorb, lambda held: held, running), None)

    start_state = (
        jnp.full((kv_count, per_key, rows_here), -1e30, jnp.float32),
        jnp.zeros((kv_count, per_key, rows_here), jnp.float32),
        jnp.zeros((kv_count, per_key, rows_here, HEAD_DIM), jnp.float32),
    )
    running = start_state
    key_piece = both[:, :key_width]
    value_piece = both[:, key_width:]
    count = key_piece.shape[0]
    width = math.gcd(count, 1024)
    blocks = count // width
    key_rows = key_piece.reshape(blocks, width, kv_count, HEAD_DIM)
    value_rows = value_piece.reshape(blocks, width, kv_count, HEAD_DIM)
    starts = width * jnp.arange(blocks, dtype=jnp.int32)
    running, unused = lax.scan(key_block, running, (key_rows, value_rows, starts))
    row_max, row_sum, weighted = running
    mixed = (weighted / row_sum[..., None]).transpose(2, 0, 1, 3).reshape(rows_here, -1)
    return mixed.astype(jnp.bfloat16)


def take_half(array, axis_dim, section):
    width = array.shape[axis_dim] // 2
    return lax.dynamic_slice_in_dim(array, section * width, width, axis_dim)


def per_device(
    resid_in,
    ssm_input,
    ssm_gate,
    ssm_in_b,
    ssm_out_c,
    step_size,
    decay_rate,
    skip_gain,
    norm_gain,
    queries,
    keys,
    values,
    out_weights,
):
    section = lax.axis_index("pipe")
    ctx_rank = lax.axis_index("y") * lax.axis_size("zc") + lax.axis_index("zc")
    key_half = take_half(keys, 1, section)
    value_half = take_half(values, 1, section)
    mamba_part, both = mamba_mixer(
        take_half(ssm_input, 1, section),
        take_half(ssm_gate, 1, section),
        take_half(ssm_in_b, 1, section),
        take_half(ssm_out_c, 1, section),
        take_half(step_size, 1, section),
        take_half(decay_rate, 0, section),
        take_half(skip_gain, 0, section),
        take_half(norm_gain, 0, section),
        jnp.concatenate([key_half, value_half], axis=1),
    )
    attn_part = attention(take_half(queries, 1, section), both, key_half.shape[1], ctx_rank)
    outgoing = jnp.where(section == 0, attn_part, mamba_part)
    kept_half = jnp.where(section == 0, mamba_part, attn_part)
    incoming = from_partner(outgoing, "pipe", 0)
    mixed_rows = jnp.where(
        section == 0,
        jnp.concatenate([kept_half, incoming], axis=1),
        jnp.concatenate([incoming, kept_half], axis=1),
    )
    inner = lax.axis_size("zc")
    tp_rank = lax.axis_index("tp")
    rows = lax.all_gather(mixed_rows, "zc", axis=0, tiled=True)
    columns = lax.all_gather(out_weights[0], "y", axis=0)
    partial_value = jnp.einsum(
        "tc,ycr->tyr", rows, columns, preferred_element_type=jnp.float32
    )
    half = partial_value.shape[1] // 2
    kept = jnp.where(tp_rank == 0, partial_value[:, :half], partial_value[:, half:])
    sent = jnp.where(tp_rank == 0, partial_value[:, half:], partial_value[:, :half])
    summed = kept + from_partner(sent.astype(jnp.bfloat16), "tp", 0).astype(jnp.float32)
    pieces = summed.reshape((inner, -1) + summed.shape[1:]).astype(jnp.bfloat16)
    pieces = lax.all_to_all(pieces, "zc", 0, 0)
    projected = pieces.transpose(1, 2, 0, 3).reshape(pieces.shape[1], -1).astype(jnp.float32)
    own_section = (resid_in.astype(jnp.float32) + projected).astype(jnp.bfloat16)
    received = shifted(own_section, "pipe", 1)
    second_section = (received.astype(jnp.float32) + projected).astype(jnp.bfloat16)
    return jnp.where(section == 0, own_section, second_section)[None]


def solution(mesh):
    pipe, ctx, tp = (mesh.shape[name] for name in ("pipe", "ctx", "tp"))
    outer = 4 if ctx % 4 == 0 else 1
    split = jax.sharding.Mesh(
        mesh.devices.reshape(pipe, outer, ctx // outer, tp), ("pipe", "y", "zc", "tp")
    )
    return jax.shard_map(
        per_device,
        mesh=split,
        in_specs=(
            P(CTX, "tp"),
            P(CTX, "tp"),
            P(CTX, "tp"),
            P(CTX, "tp"),
            P(CTX, "tp"),
            P(CTX, "tp"),
            P("tp"),
            P("tp"),
            P("tp"),
            P(CTX, "tp"),
            P(CTX, "tp"),
            P(CTX, "tp"),
            P("pipe", "tp", CTX),
        ),
        out_specs=P("pipe", CTX, "tp"),
        check_vma=False,
    )
```

```python
import math

import jax
import jax.numpy as jnp
from jax import lax
from jax.sharding import PartitionSpec as P

MHEAD_DIM = 64
STATE = 128
SCAN_BLOCK = 128
HEAD_DIM = 128


exact_mode = lax.Precision.HIGHEST
norm_eps = 1e-05


def entering_2(x, axis, combine, identity):
    peers, position = (lax.axis_size(axis), lax.axis_index(axis))
    everything = jax.tree.map(
        lambda part, kind: lax.all_gather(part.astype(kind), axis), x, (jnp.bfloat16, jnp.bfloat16)
    )
    start = jax.tree.map(
        lambda part, zero: jnp.broadcast_to(jnp.asarray(zero, part.dtype), part.shape), x, identity
    )

    def turn(k, before):
        reached = k < position
        new = combine(
            before, jax.tree.map(lambda part, own: part[k].astype(own.dtype), everything, x)
        )
        return jax.tree.map(lambda a, b: jnp.where(reached, a, b), new, before)

    return lax.fori_loop(0, peers, turn, start)


CTX = ("y", "zc")


def gathered(x, axis):
    peers = lax.axis_size(axis)
    spread = jnp.broadcast_to(x[None], (peers,) + x.shape)
    return lax.all_to_all(spread, axis, 0, 0)


def entering_states(through_log, local_state):
    outer = lax.axis_size("y")
    inner = lax.axis_size("zc")
    peers = outer * inner
    rank = lax.axis_index("y") * inner + lax.axis_index("zc")
    logs = gathered(through_log, CTX)
    logs = logs.reshape((peers,) + through_log.shape)
    places = jnp.arange(peers, dtype=jnp.int32)

    def span_weight(k, upto):
        inside = (places[None, :] > k[:, None]) & (places[None, :] < upto)
        summed = jnp.sum(jnp.where(inside[:, :, None, None], logs[None], 0.0), axis=1)
        return jnp.where((k < upto)[:, None, None], jnp.exp(summed), 0.0)

    first = lax.axis_index("y") * inner
    near = gathered(local_state.astype(jnp.bfloat16), "zc").astype(jnp.float32)
    near_ids = first + jnp.arange(inner, dtype=jnp.int32)
    own_part = jnp.einsum(
        "kgj,kgjpn->gjpn", span_weight(near_ids, rank), near, precision=exact_mode
    )
    group_end = first + inner
    group_total = jnp.einsum(
        "kgj,kgjpn->gjpn", span_weight(near_ids, group_end), near, precision=exact_mode
    )
    far = gathered(group_total.astype(jnp.bfloat16), "y").astype(jnp.float32)
    far_ends = (jnp.arange(outer, dtype=jnp.int32) + 1) * inner - 1
    far_weight = span_weight(far_ends, rank)
    far_weight = jnp.where((far_ends < first)[:, None, None], far_weight, 0.0)
    far_part = jnp.einsum("kgj,kgjpn->gjpn", far_weight, far, precision=exact_mode)
    return own_part + far_part


def from_partner(block, axis, distance):
    count = lax.axis_size(axis)
    route = []
    for low in range(count):
        high = low | 1 << distance
        if high != low and high < count:
            route += [(low, high), (high, low)]
    return lax.ppermute(block, axis, route)


def shifted(x, axis, by):
    peers = lax.axis_size(axis)
    pairs = [(i, i + by) for i in range(peers) if 0 <= i + by < peers]
    return lax.ppermute(x, axis, pairs)


def block_scan(state_now, inputs_x, input_b, output_c, step_rows, log_decay):
    width = inputs_x.shape[0]
    groups = inputs_x.shape[1]
    per_group = inputs_x.shape[2]
    running = jnp.cumsum(log_decay, axis=0)
    spread = running[:, None, :] - running[None, :, :]
    causal = (
        jnp.arange(width, dtype=jnp.int32)[:, None] >= jnp.arange(width, dtype=jnp.int32)[None, :]
    )
    decay_mat = jnp.exp(jnp.where(causal[:, :, None], spread, -jnp.inf))
    decay_mat = decay_mat.reshape(width, width, groups, per_group).transpose(2, 3, 0, 1)
    cross_cb = jnp.einsum("tgn,sgn->gts", output_c, input_b, precision=exact_mode)
    step_cols = step_rows.reshape(width, groups, per_group).transpose(1, 2, 0)
    mixing = cross_cb[:, None, :, :] * decay_mat * step_cols[:, :, None, :]
    within = jnp.einsum("gjts,sgjp->tgjp", mixing, inputs_x, precision=exact_mode)
    entry = jnp.exp(running).reshape(width, groups, per_group)
    carried = (
        jnp.einsum("tgn,gjpn->tgjp", output_c, state_now, precision=exact_mode)
        * entry[:, :, :, None]
    )
    tail_weight = (jnp.exp(running[-1][None, :] - running) * step_rows).reshape(
        width, groups, per_group
    )
    leaving = jnp.exp(running[-1]).reshape(groups, per_group)
    state_next = leaving[:, :, None, None] * state_now + jnp.einsum(
        "sgj,sgjp,sgn->gjpn", tail_weight, inputs_x, input_b, precision=exact_mode
    )
    return (state_next, within + carried)


def gate_norm(values_y, gate_in, gains, groups):
    rows_here = values_y.shape[0]
    gated = values_y * jax.nn.silu(gate_in.astype(jnp.float32))
    grouped = gated.reshape(rows_here, groups, -1)
    meansq = jnp.mean(grouped * grouped, axis=-1, keepdims=True)
    scaled = (grouped * lax.rsqrt(meansq + norm_eps)).reshape(rows_here, -1)
    return (scaled * gains[None, :]).astype(jnp.bfloat16)


def join_states(earlier, later):
    return (earlier[0] * later[0], later[0][:, :, None, None] * earlier[1] + later[1])


def mamba_mixer(
    ssm_input, ssm_gate, ssm_in_b, ssm_out_c, step_size, decay_rate, skip_gain, norm_gain
):
    rows_here = ssm_input.shape[0]
    head_count = decay_rate.shape[0]
    groups = ssm_in_b.shape[1] // STATE
    per_group = head_count // groups
    block_count = rows_here // SCAN_BLOCK
    log_decay = -step_size * decay_rate[None, :]
    inputs_x = ssm_input.reshape(block_count, SCAN_BLOCK, groups, per_group, MHEAD_DIM)
    input_b = ssm_in_b.reshape(block_count, SCAN_BLOCK, groups, STATE)
    output_c = ssm_out_c.reshape(block_count, SCAN_BLOCK, groups, STATE)

    def block_turn(state_now, block_data):
        part_x, part_b, part_c, part_step, part_log = block_data
        return block_scan(
            state_now,
            part_x.astype(jnp.float32),
            part_b.astype(jnp.float32),
            part_c.astype(jnp.float32),
            part_step,
            part_log,
        )

    start_state = jnp.zeros((groups, per_group, MHEAD_DIM, STATE), jnp.float32)
    local_state, pieces = lax.scan(
        block_turn,
        start_state,
        (
            inputs_x,
            input_b,
            output_c,
            step_size.reshape(block_count, SCAN_BLOCK, head_count),
            log_decay.reshape(block_count, SCAN_BLOCK, head_count),
        ),
    )
    running = jnp.cumsum(log_decay, axis=0)
    entering = entering_states(running[-1].reshape(groups, per_group), local_state)
    output_all = ssm_out_c.astype(jnp.float32).reshape(rows_here, groups, STATE)
    carried = (
        jnp.einsum("tgn,gjpn->tgjp", output_all, entering, precision=exact_mode)
        * jnp.exp(running).reshape(rows_here, groups, per_group)[:, :, :, None]
    )
    skipped = (
        ssm_input.astype(jnp.float32).reshape(rows_here, groups, per_group, MHEAD_DIM)
        * skip_gain.reshape(groups, per_group)[None, :, :, None]
    )
    values_y = pieces.reshape(rows_here, groups, per_group, MHEAD_DIM) + carried + skipped
    return gate_norm(values_y.reshape(rows_here, -1), ssm_gate, norm_gain, groups)


def attention(queries, keys, values, ctx_rank):
    rows_here = queries.shape[0]
    kv_count = keys.shape[1] // HEAD_DIM
    per_key = queries.shape[1] // HEAD_DIM // kv_count
    query_groups = queries.reshape(rows_here, kv_count, per_key, HEAD_DIM)
    query_pos = ctx_rank * rows_here + jnp.arange(rows_here, dtype=jnp.int32)
    last_query = query_pos[-1]
    score_scale = 1.0 / math.sqrt(HEAD_DIM)

    def key_block(running, block_data):
        key_rows, value_rows, first_key = block_data

        def absorb(held):
            row_max, row_sum, weighted = held
            scores = (
                jnp.einsum(
                    "qgjd,kgd->gjqk", query_groups, key_rows, preferred_element_type=jnp.float32
                )
                * score_scale
            )
            key_pos = first_key + jnp.arange(key_rows.shape[0], dtype=jnp.int32)
            allowed = key_pos[None, :] <= query_pos[:, None]
            scores = jnp.where(allowed, scores, -1e30)
            new_max = jnp.maximum(row_max, jnp.max(scores, axis=-1))
            rescale = jnp.exp(row_max - new_max)
            weights_exp = jnp.where(allowed, jnp.exp(scores - new_max[..., None]), 0.0)
            row_sum = row_sum * rescale + jnp.sum(weights_exp, axis=-1)
            weighted = weighted * rescale[..., None] + jnp.einsum(
                "gjqk,kgd->gjqd",
                weights_exp.astype(jnp.bfloat16),
                value_rows,
                preferred_element_type=jnp.float32,
            )
            return (new_max, row_sum, weighted)

        return (lax.cond(first_key <= last_query, absorb, lambda held: held, running), None)

    start_state = (
        jnp.full((kv_count, per_key, rows_here), -1e30, jnp.float32),
        jnp.zeros((kv_count, per_key, rows_here), jnp.float32),
        jnp.zeros((kv_count, per_key, rows_here, HEAD_DIM), jnp.float32),
    )
    running = start_state
    both = gathered(jnp.concatenate([keys, values], axis=1), CTX)
    both = both.reshape(-1, both.shape[-1])
    key_piece = both[:, : keys.shape[1]]
    value_piece = both[:, keys.shape[1] :]
    count = key_piece.shape[0]
    width = math.gcd(count, 1024)
    blocks = count // width
    key_rows = key_piece.reshape(blocks, width, kv_count, HEAD_DIM)
    value_rows = value_piece.reshape(blocks, width, kv_count, HEAD_DIM)
    starts = width * jnp.arange(blocks, dtype=jnp.int32)
    running, unused = lax.scan(key_block, running, (key_rows, value_rows, starts))
    row_max, row_sum, weighted = running
    mixed = (weighted / row_sum[..., None]).transpose(2, 0, 1, 3).reshape(rows_here, -1)
    return mixed.astype(jnp.bfloat16)


def take_half(array, axis_dim, section):
    width = array.shape[axis_dim] // 2
    return lax.dynamic_slice_in_dim(array, section * width, width, axis_dim)


def per_device(
    resid_in,
    ssm_input,
    ssm_gate,
    ssm_in_b,
    ssm_out_c,
    step_size,
    decay_rate,
    skip_gain,
    norm_gain,
    queries,
    keys,
    values,
    out_weights,
):
    section = lax.axis_index("pipe")
    ctx_rank = lax.axis_index("y") * lax.axis_size("zc") + lax.axis_index("zc")
    mamba_part = mamba_mixer(
        take_half(ssm_input, 1, section),
        take_half(ssm_gate, 1, section),
        take_half(ssm_in_b, 1, section),
        take_half(ssm_out_c, 1, section),
        take_half(step_size, 1, section),
        take_half(decay_rate, 0, section),
        take_half(skip_gain, 0, section),
        take_half(norm_gain, 0, section),
    )
    attn_part = attention(
        take_half(queries, 1, section),
        take_half(keys, 1, section),
        take_half(values, 1, section),
        ctx_rank,
    )
    outgoing = jnp.where(section == 0, attn_part, mamba_part)
    kept_half = jnp.where(section == 0, mamba_part, attn_part)
    incoming = from_partner(outgoing, "pipe", 0)
    mixed_rows = jnp.where(
        section == 0,
        jnp.concatenate([kept_half, incoming], axis=1),
        jnp.concatenate([incoming, kept_half], axis=1),
    )
    weights_all = lax.all_gather(out_weights, CTX, axis=2, tiled=True)[0]
    half = weights_all.shape[1] // 2
    tp_rank = lax.axis_index("tp")
    sent_cols = lax.dynamic_slice_in_dim(weights_all, (1 - tp_rank) * half, half, 1)
    kept_cols = lax.dynamic_slice_in_dim(weights_all, tp_rank * half, half, 1)
    sent = jnp.dot(mixed_rows, sent_cols, preferred_element_type=jnp.float32).astype(jnp.bfloat16)
    from_tp = from_partner(sent, "tp", 0)
    kept = jnp.dot(mixed_rows, kept_cols, preferred_element_type=jnp.float32)
    kept_low = kept.astype(jnp.bfloat16)
    first_kept = shifted(kept_low, "pipe", 1)
    first_sent = lax.ppermute(sent, ("pipe", "tp"), [(0, 3), (1, 2)])
    base = resid_in.astype(jnp.float32)
    own_section = (
        (base + kept_low.astype(jnp.float32)) + from_tp.astype(jnp.float32)
    ).astype(jnp.bfloat16)
    rebuilt = (
        (base + first_kept.astype(jnp.float32)) + first_sent.astype(jnp.float32)
    ).astype(jnp.bfloat16)
    second_section = (
        rebuilt.astype(jnp.float32) + (kept + from_tp.astype(jnp.float32))
    ).astype(jnp.bfloat16)
    return jnp.where(section == 0, own_section, second_section)[None]


def solution(mesh):
    pipe, ctx, tp = (mesh.shape[name] for name in ("pipe", "ctx", "tp"))
    outer = 4 if ctx % 4 == 0 else 1
    split = jax.sharding.Mesh(
        mesh.devices.reshape(pipe, outer, ctx // outer, tp), ("pipe", "y", "zc", "tp")
    )
    return jax.shard_map(
        per_device,
        mesh=split,
        in_specs=(
            P(CTX, "tp"),
            P(CTX, "tp"),
            P(CTX, "tp"),
            P(CTX, "tp"),
            P(CTX, "tp"),
            P(CTX, "tp"),
            P("tp"),
            P("tp"),
            P("tp"),
            P(CTX, "tp"),
            P(CTX, "tp"),
            P(CTX, "tp"),
            P("pipe", "tp", CTX),
        ),
        out_specs=P("pipe", CTX, "tp"),
        check_vma=False,
    )
```

```python
import math

import jax
import jax.numpy as jnp
from jax import lax
from jax.sharding import PartitionSpec as P

MHEAD_DIM = 64
STATE = 128
SCAN_BLOCK = 128
HEAD_DIM = 128


exact_mode = lax.Precision.HIGHEST
norm_eps = 1e-05


def entering_2(x, axis, combine, identity):
    peers, position = (lax.axis_size(axis), lax.axis_index(axis))
    everything = jax.tree.map(
        lambda part, kind: lax.all_gather(part.astype(kind), axis), x, (jnp.bfloat16, jnp.bfloat16)
    )
    start = jax.tree.map(
        lambda part, zero: jnp.broadcast_to(jnp.asarray(zero, part.dtype), part.shape), x, identity
    )

    def turn(k, before):
        reached = k < position
        new = combine(
            before, jax.tree.map(lambda part, own: part[k].astype(own.dtype), everything, x)
        )
        return jax.tree.map(lambda a, b: jnp.where(reached, a, b), new, before)

    return lax.fori_loop(0, peers, turn, start)


CTX = ("y", "zc")


def gathered(x, axis):
    peers = lax.axis_size(axis)
    spread = jnp.broadcast_to(x[None], (peers,) + x.shape)
    return lax.all_to_all(spread, axis, 0, 0)


def entering_states(logs, local_state):
    outer = lax.axis_size("y")
    inner = lax.axis_size("zc")
    peers = outer * inner
    rank = lax.axis_index("y") * inner + lax.axis_index("zc")
    places = jnp.arange(peers, dtype=jnp.int32)

    def span_weight(k, upto):
        inside = (places[None, :] > k[:, None]) & (places[None, :] < upto)
        summed = jnp.sum(jnp.where(inside[:, :, None, None], logs[None], 0.0), axis=1)
        return jnp.where((k < upto)[:, None, None], jnp.exp(summed), 0.0)

    first = lax.axis_index("y") * inner
    near = gathered(local_state.astype(jnp.bfloat16), "zc").astype(jnp.float32)
    near_ids = first + jnp.arange(inner, dtype=jnp.int32)
    own_part = jnp.einsum(
        "kgj,kgjpn->gjpn", span_weight(near_ids, rank), near, precision=exact_mode
    )
    group_end = first + inner
    group_total = jnp.einsum(
        "kgj,kgjpn->gjpn", span_weight(near_ids, group_end), near, precision=exact_mode
    )
    far = gathered(group_total.astype(jnp.bfloat16), "y").astype(jnp.float32)
    far_ends = (jnp.arange(outer, dtype=jnp.int32) + 1) * inner - 1
    far_weight = span_weight(far_ends, rank)
    far_weight = jnp.where((far_ends < first)[:, None, None], far_weight, 0.0)
    far_part = jnp.einsum("kgj,kgjpn->gjpn", far_weight, far, precision=exact_mode)
    return own_part + far_part


def from_partner(block, axis, distance):
    count = lax.axis_size(axis)
    route = []
    for low in range(count):
        high = low | 1 << distance
        if high != low and high < count:
            route += [(low, high), (high, low)]
    return lax.ppermute(block, axis, route)


def shifted(x, axis, by):
    peers = lax.axis_size(axis)
    pairs = [(i, i + by) for i in range(peers) if 0 <= i + by < peers]
    return lax.ppermute(x, axis, pairs)


def block_scan(state_now, inputs_x, input_b, output_c, step_rows, log_decay):
    width = inputs_x.shape[0]
    groups = inputs_x.shape[1]
    per_group = inputs_x.shape[2]
    running = jnp.cumsum(log_decay, axis=0)
    spread = running[:, None, :] - running[None, :, :]
    causal = (
        jnp.arange(width, dtype=jnp.int32)[:, None] >= jnp.arange(width, dtype=jnp.int32)[None, :]
    )
    decay_mat = jnp.exp(jnp.where(causal[:, :, None], spread, -jnp.inf))
    decay_mat = decay_mat.reshape(width, width, groups, per_group).transpose(2, 3, 0, 1)
    cross_cb = jnp.einsum("tgn,sgn->gts", output_c, input_b, precision=exact_mode)
    step_cols = step_rows.reshape(width, groups, per_group).transpose(1, 2, 0)
    mixing = cross_cb[:, None, :, :] * decay_mat * step_cols[:, :, None, :]
    within = jnp.einsum("gjts,sgjp->tgjp", mixing, inputs_x, precision=exact_mode)
    entry = jnp.exp(running).reshape(width, groups, per_group)
    carried = (
        jnp.einsum("tgn,gjpn->tgjp", output_c, state_now, precision=exact_mode)
        * entry[:, :, :, None]
    )
    tail_weight = (jnp.exp(running[-1][None, :] - running) * step_rows).reshape(
        width, groups, per_group
    )
    leaving = jnp.exp(running[-1]).reshape(groups, per_group)
    state_next = leaving[:, :, None, None] * state_now + jnp.einsum(
        "sgj,sgjp,sgn->gjpn", tail_weight, inputs_x, input_b, precision=exact_mode
    )
    return (state_next, within + carried)


def gate_norm(values_y, gate_in, gains, groups):
    rows_here = values_y.shape[0]
    gated = values_y * jax.nn.silu(gate_in.astype(jnp.float32))
    grouped = gated.reshape(rows_here, groups, -1)
    meansq = jnp.mean(grouped * grouped, axis=-1, keepdims=True)
    scaled = (grouped * lax.rsqrt(meansq + norm_eps)).reshape(rows_here, -1)
    return (scaled * gains[None, :]).astype(jnp.bfloat16)


def join_states(earlier, later):
    return (earlier[0] * later[0], later[0][:, :, None, None] * earlier[1] + later[1])


def mamba_mixer(
    ssm_input, ssm_gate, ssm_in_b, ssm_out_c, step_size, decay_rate, skip_gain, norm_gain, logs
):
    rows_here = ssm_input.shape[0]
    head_count = decay_rate.shape[0]
    groups = ssm_in_b.shape[1] // STATE
    per_group = head_count // groups
    block_count = rows_here // SCAN_BLOCK
    log_decay = -step_size * decay_rate[None, :]
    inputs_x = ssm_input.reshape(block_count, SCAN_BLOCK, groups, per_group, MHEAD_DIM)
    input_b = ssm_in_b.reshape(block_count, SCAN_BLOCK, groups, STATE)
    output_c = ssm_out_c.reshape(block_count, SCAN_BLOCK, groups, STATE)

    def block_turn(state_now, block_data):
        part_x, part_b, part_c, part_step, part_log = block_data
        return block_scan(
            state_now,
            part_x.astype(jnp.float32),
            part_b.astype(jnp.float32),
            part_c.astype(jnp.float32),
            part_step,
            part_log,
        )

    start_state = jnp.zeros((groups, per_group, MHEAD_DIM, STATE), jnp.float32)
    local_state, pieces = lax.scan(
        block_turn,
        start_state,
        (
            inputs_x,
            input_b,
            output_c,
            step_size.reshape(block_count, SCAN_BLOCK, head_count),
            log_decay.reshape(block_count, SCAN_BLOCK, head_count),
        ),
    )
    running = jnp.cumsum(log_decay, axis=0)
    entering = entering_states(logs.reshape((-1, groups, per_group)), local_state)
    output_all = ssm_out_c.astype(jnp.float32).reshape(rows_here, groups, STATE)
    carried = (
        jnp.einsum("tgn,gjpn->tgjp", output_all, entering, precision=exact_mode)
        * jnp.exp(running).reshape(rows_here, groups, per_group)[:, :, :, None]
    )
    skipped = (
        ssm_input.astype(jnp.float32).reshape(rows_here, groups, per_group, MHEAD_DIM)
        * skip_gain.reshape(groups, per_group)[None, :, :, None]
    )
    values_y = pieces.reshape(rows_here, groups, per_group, MHEAD_DIM) + carried + skipped
    return gate_norm(values_y.reshape(rows_here, -1), ssm_gate, norm_gain, groups)


def attention(queries, both, key_width, ctx_rank):
    rows_here = queries.shape[0]
    kv_count = key_width // HEAD_DIM
    per_key = queries.shape[1] // HEAD_DIM // kv_count
    query_groups = queries.reshape(rows_here, kv_count, per_key, HEAD_DIM)
    query_pos = ctx_rank * rows_here + jnp.arange(rows_here, dtype=jnp.int32)
    last_query = query_pos[-1]
    score_scale = 1.0 / math.sqrt(HEAD_DIM)

    def key_block(running, block_data):
        key_rows, value_rows, first_key = block_data

        def absorb(held):
            row_max, row_sum, weighted = held
            scores = (
                jnp.einsum(
                    "qgjd,kgd->gjqk", query_groups, key_rows, preferred_element_type=jnp.float32
                )
                * score_scale
            )
            key_pos = first_key + jnp.arange(key_rows.shape[0], dtype=jnp.int32)
            allowed = key_pos[None, :] <= query_pos[:, None]
            scores = jnp.where(allowed, scores, -1e30)
            new_max = jnp.maximum(row_max, jnp.max(scores, axis=-1))
            rescale = jnp.exp(row_max - new_max)
            weights_exp = jnp.where(allowed, jnp.exp(scores - new_max[..., None]), 0.0)
            row_sum = row_sum * rescale + jnp.sum(weights_exp, axis=-1)
            weighted = weighted * rescale[..., None] + jnp.einsum(
                "gjqk,kgd->gjqd",
                weights_exp.astype(jnp.bfloat16),
                value_rows,
                preferred_element_type=jnp.float32,
            )
            return (new_max, row_sum, weighted)

        return (lax.cond(first_key <= last_query, absorb, lambda held: held, running), None)

    start_state = (
        jnp.full((kv_count, per_key, rows_here), -1e30, jnp.float32),
        jnp.zeros((kv_count, per_key, rows_here), jnp.float32),
        jnp.zeros((kv_count, per_key, rows_here, HEAD_DIM), jnp.float32),
    )
    running = start_state
    key_piece = both[:, :key_width]
    value_piece = both[:, key_width:]
    count = key_piece.shape[0]
    width = math.gcd(count, 1024)
    blocks = count // width
    key_rows = key_piece.reshape(blocks, width, kv_count, HEAD_DIM)
    value_rows = value_piece.reshape(blocks, width, kv_count, HEAD_DIM)
    starts = width * jnp.arange(blocks, dtype=jnp.int32)
    running, unused = lax.scan(key_block, running, (key_rows, value_rows, starts))
    row_max, row_sum, weighted = running
    mixed = (weighted / row_sum[..., None]).transpose(2, 0, 1, 3).reshape(rows_here, -1)
    return mixed.astype(jnp.bfloat16)


def take_half(array, axis_dim, section):
    width = array.shape[axis_dim] // 2
    return lax.dynamic_slice_in_dim(array, section * width, width, axis_dim)


def per_device(
    resid_in,
    ssm_input,
    ssm_gate,
    ssm_in_b,
    ssm_out_c,
    step_size,
    decay_rate,
    skip_gain,
    norm_gain,
    queries,
    keys,
    values,
    out_weights,
):
    section = lax.axis_index("pipe")
    ctx_rank = lax.axis_index("y") * lax.axis_size("zc") + lax.axis_index("zc")
    step_half = take_half(step_size, 1, section)
    rate_half = take_half(decay_rate, 0, section)
    own_log = jnp.cumsum(-step_half * rate_half[None, :], axis=0)[-1]
    log_high = own_log.astype(jnp.bfloat16)
    log_low = (own_log - log_high.astype(jnp.float32)).astype(jnp.bfloat16)
    key_half = take_half(keys, 1, section)
    kv_own = jnp.concatenate([key_half, take_half(values, 1, section)], axis=1)
    width = kv_own.shape[1]
    heads_here = own_log.shape[0]
    extra = jnp.zeros((8, width), jnp.bfloat16)
    extra = extra.at[0, :heads_here].set(log_high).at[0, heads_here : 2 * heads_here].set(log_low)
    arrived = gathered(jnp.concatenate([kv_own, extra], axis=0), CTX)
    rows_here = kv_own.shape[0]
    both = arrived[:, :rows_here].reshape(-1, width)
    logs = arrived[:, rows_here, :heads_here].astype(jnp.float32) + arrived[
        :, rows_here, heads_here : 2 * heads_here
    ].astype(jnp.float32)
    mamba_part = mamba_mixer(
        take_half(ssm_input, 1, section),
        take_half(ssm_gate, 1, section),
        take_half(ssm_in_b, 1, section),
        take_half(ssm_out_c, 1, section),
        take_half(step_size, 1, section),
        take_half(decay_rate, 0, section),
        take_half(skip_gain, 0, section),
        take_half(norm_gain, 0, section),
        logs,
    )
    attn_part = attention(take_half(queries, 1, section), both, key_half.shape[1], ctx_rank)
    outgoing = jnp.where(section == 0, attn_part, mamba_part)
    kept_half = jnp.where(section == 0, mamba_part, attn_part)
    incoming = from_partner(outgoing, "pipe", 0)
    mixed_rows = jnp.where(
        section == 0,
        jnp.concatenate([kept_half, incoming], axis=1),
        jnp.concatenate([incoming, kept_half], axis=1),
    )
    weights_all = lax.all_gather(out_weights, CTX, axis=2, tiled=True)[0]
    half = weights_all.shape[1] // 2
    tp_rank = lax.axis_index("tp")
    sent_cols = lax.dynamic_slice_in_dim(weights_all, (1 - tp_rank) * half, half, 1)
    kept_cols = lax.dynamic_slice_in_dim(weights_all, tp_rank * half, half, 1)
    sent = jnp.dot(mixed_rows, sent_cols, preferred_element_type=jnp.float32).astype(jnp.bfloat16)
    from_tp = from_partner(sent, "tp", 0)
    kept = jnp.dot(mixed_rows, kept_cols, preferred_element_type=jnp.float32)
    kept_low = kept.astype(jnp.bfloat16)
    first_kept = shifted(kept_low, "pipe", 1)
    first_sent = lax.ppermute(sent, ("pipe", "tp"), [(0, 3), (1, 2)])
    base = resid_in.astype(jnp.float32)
    own_section = (
        (base + kept_low.astype(jnp.float32)) + from_tp.astype(jnp.float32)
    ).astype(jnp.bfloat16)
    rebuilt = (
        (base + first_kept.astype(jnp.float32)) + first_sent.astype(jnp.float32)
    ).astype(jnp.bfloat16)
    second_section = (
        rebuilt.astype(jnp.float32) + (kept + from_tp.astype(jnp.float32))
    ).astype(jnp.bfloat16)
    return jnp.where(section == 0, own_section, second_section)[None]


def solution(mesh):
    pipe, ctx, tp = (mesh.shape[name] for name in ("pipe", "ctx", "tp"))
    outer = 4 if ctx % 4 == 0 else 1
    split = jax.sharding.Mesh(
        mesh.devices.reshape(pipe, outer, ctx // outer, tp), ("pipe", "y", "zc", "tp")
    )
    return jax.shard_map(
        per_device,
        mesh=split,
        in_specs=(
            P(CTX, "tp"),
            P(CTX, "tp"),
            P(CTX, "tp"),
            P(CTX, "tp"),
            P(CTX, "tp"),
            P(CTX, "tp"),
            P("tp"),
            P("tp"),
            P("tp"),
            P(CTX, "tp"),
            P(CTX, "tp"),
            P(CTX, "tp"),
            P("pipe", "tp", CTX),
        ),
        out_specs=P("pipe", CTX, "tp"),
        check_vma=False,
    )
```

```python
import math

import jax
import jax.numpy as jnp
from jax import lax
from jax.sharding import PartitionSpec as P

MHEAD_DIM = 64
STATE = 128
SCAN_BLOCK = 128
HEAD_DIM = 128


exact_mode = lax.Precision.HIGHEST
norm_eps = 1e-05


def entering_2(x, axis, combine, identity):
    peers, position = (lax.axis_size(axis), lax.axis_index(axis))
    everything = jax.tree.map(
        lambda part, kind: lax.all_gather(part.astype(kind), axis), x, (jnp.bfloat16, jnp.bfloat16)
    )
    start = jax.tree.map(
        lambda part, zero: jnp.broadcast_to(jnp.asarray(zero, part.dtype), part.shape), x, identity
    )

    def turn(k, before):
        reached = k < position
        new = combine(
            before, jax.tree.map(lambda part, own: part[k].astype(own.dtype), everything, x)
        )
        return jax.tree.map(lambda a, b: jnp.where(reached, a, b), new, before)

    return lax.fori_loop(0, peers, turn, start)


CTX = ("y", "zc")


def gathered(x, axis):
    peers = lax.axis_size(axis)
    spread = jnp.broadcast_to(x[None], (peers,) + x.shape)
    return lax.all_to_all(spread, axis, 0, 0)


def entering_states(through_log, local_state):
    outer = lax.axis_size("y")
    inner = lax.axis_size("zc")
    peers = outer * inner
    rank = lax.axis_index("y") * inner + lax.axis_index("zc")
    logs = gathered(through_log, CTX)
    logs = logs.reshape((peers,) + through_log.shape)
    places = jnp.arange(peers, dtype=jnp.int32)

    def span_weight(k, upto):
        inside = (places[None, :] > k[:, None]) & (places[None, :] < upto)
        summed = jnp.sum(jnp.where(inside[:, :, None, None], logs[None], 0.0), axis=1)
        return jnp.where((k < upto)[:, None, None], jnp.exp(summed), 0.0)

    first = lax.axis_index("y") * inner
    near = gathered(local_state.astype(jnp.bfloat16), "zc").astype(jnp.float32)
    near_ids = first + jnp.arange(inner, dtype=jnp.int32)
    own_part = jnp.einsum(
        "kgj,kgjpn->gjpn", span_weight(near_ids, rank), near, precision=exact_mode
    )
    group_end = first + inner
    group_total = jnp.einsum(
        "kgj,kgjpn->gjpn", span_weight(near_ids, group_end), near, precision=exact_mode
    )
    far = gathered(group_total.astype(jnp.bfloat16), "y").astype(jnp.float32)
    far_ends = (jnp.arange(outer, dtype=jnp.int32) + 1) * inner - 1
    far_weight = span_weight(far_ends, rank)
    far_weight = jnp.where((far_ends < first)[:, None, None], far_weight, 0.0)
    far_part = jnp.einsum("kgj,kgjpn->gjpn", far_weight, far, precision=exact_mode)
    return own_part + far_part


def from_partner(block, axis, distance):
    count = lax.axis_size(axis)
    route = []
    for low in range(count):
        high = low | 1 << distance
        if high != low and high < count:
            route += [(low, high), (high, low)]
    return lax.ppermute(block, axis, route)


def shifted(x, axis, by):
    peers = lax.axis_size(axis)
    pairs = [(i, i + by) for i in range(peers) if 0 <= i + by < peers]
    return lax.ppermute(x, axis, pairs)


def block_scan(state_now, inputs_x, input_b, output_c, step_rows, log_decay):
    width = inputs_x.shape[0]
    groups = inputs_x.shape[1]
    per_group = inputs_x.shape[2]
    running = jnp.cumsum(log_decay, axis=0)
    spread = running[:, None, :] - running[None, :, :]
    causal = (
        jnp.arange(width, dtype=jnp.int32)[:, None] >= jnp.arange(width, dtype=jnp.int32)[None, :]
    )
    decay_mat = jnp.exp(jnp.where(causal[:, :, None], spread, -jnp.inf))
    decay_mat = decay_mat.reshape(width, width, groups, per_group).transpose(2, 3, 0, 1)
    cross_cb = jnp.einsum("tgn,sgn->gts", output_c, input_b, precision=exact_mode)
    step_cols = step_rows.reshape(width, groups, per_group).transpose(1, 2, 0)
    mixing = cross_cb[:, None, :, :] * decay_mat * step_cols[:, :, None, :]
    within = jnp.einsum("gjts,sgjp->tgjp", mixing, inputs_x, precision=exact_mode)
    entry = jnp.exp(running).reshape(width, groups, per_group)
    carried = (
        jnp.einsum("tgn,gjpn->tgjp", output_c, state_now, precision=exact_mode)
        * entry[:, :, :, None]
    )
    tail_weight = (jnp.exp(running[-1][None, :] - running) * step_rows).reshape(
        width, groups, per_group
    )
    leaving = jnp.exp(running[-1]).reshape(groups, per_group)
    state_next = leaving[:, :, None, None] * state_now + jnp.einsum(
        "sgj,sgjp,sgn->gjpn", tail_weight, inputs_x, input_b, precision=exact_mode
    )
    return (state_next, within + carried)


def gate_norm(values_y, gate_in, gains, groups):
    rows_here = values_y.shape[0]
    gated = values_y * jax.nn.silu(gate_in.astype(jnp.float32))
    grouped = gated.reshape(rows_here, groups, -1)
    meansq = jnp.mean(grouped * grouped, axis=-1, keepdims=True)
    scaled = (grouped * lax.rsqrt(meansq + norm_eps)).reshape(rows_here, -1)
    return (scaled * gains[None, :]).astype(jnp.bfloat16)


def join_states(earlier, later):
    return (earlier[0] * later[0], later[0][:, :, None, None] * earlier[1] + later[1])


def mamba_mixer(
    ssm_input, ssm_gate, ssm_in_b, ssm_out_c, step_size, decay_rate, skip_gain, norm_gain
):
    rows_here = ssm_input.shape[0]
    head_count = decay_rate.shape[0]
    groups = ssm_in_b.shape[1] // STATE
    per_group = head_count // groups
    block_count = rows_here // SCAN_BLOCK
    log_decay = -step_size * decay_rate[None, :]
    inputs_x = ssm_input.reshape(block_count, SCAN_BLOCK, groups, per_group, MHEAD_DIM)
    input_b = ssm_in_b.reshape(block_count, SCAN_BLOCK, groups, STATE)
    output_c = ssm_out_c.reshape(block_count, SCAN_BLOCK, groups, STATE)

    def block_turn(state_now, block_data):
        part_x, part_b, part_c, part_step, part_log = block_data
        return block_scan(
            state_now,
            part_x.astype(jnp.float32),
            part_b.astype(jnp.float32),
            part_c.astype(jnp.float32),
            part_step,
            part_log,
        )

    start_state = jnp.zeros((groups, per_group, MHEAD_DIM, STATE), jnp.float32)
    local_state, pieces = lax.scan(
        block_turn,
        start_state,
        (
            inputs_x,
            input_b,
            output_c,
            step_size.reshape(block_count, SCAN_BLOCK, head_count),
            log_decay.reshape(block_count, SCAN_BLOCK, head_count),
        ),
    )
    running = jnp.cumsum(log_decay, axis=0)
    entering = entering_states(running[-1].reshape(groups, per_group), local_state)
    output_all = ssm_out_c.astype(jnp.float32).reshape(rows_here, groups, STATE)
    carried = (
        jnp.einsum("tgn,gjpn->tgjp", output_all, entering, precision=exact_mode)
        * jnp.exp(running).reshape(rows_here, groups, per_group)[:, :, :, None]
    )
    skipped = (
        ssm_input.astype(jnp.float32).reshape(rows_here, groups, per_group, MHEAD_DIM)
        * skip_gain.reshape(groups, per_group)[None, :, :, None]
    )
    values_y = pieces.reshape(rows_here, groups, per_group, MHEAD_DIM) + carried + skipped
    return gate_norm(values_y.reshape(rows_here, -1), ssm_gate, norm_gain, groups)


def attention(queries, keys, values, ctx_rank):
    rows_here = queries.shape[0]
    kv_count = keys.shape[1] // HEAD_DIM
    per_key = queries.shape[1] // HEAD_DIM // kv_count
    query_groups = queries.reshape(rows_here, kv_count, per_key, HEAD_DIM)
    query_pos = ctx_rank * rows_here + jnp.arange(rows_here, dtype=jnp.int32)
    last_query = query_pos[-1]
    score_scale = 1.0 / math.sqrt(HEAD_DIM)

    def key_block(running, block_data):
        key_rows, value_rows, first_key = block_data

        def absorb(held):
            row_max, row_sum, weighted = held
            scores = (
                jnp.einsum(
                    "qgjd,kgd->gjqk", query_groups, key_rows, preferred_element_type=jnp.float32
                )
                * score_scale
            )
            key_pos = first_key + jnp.arange(key_rows.shape[0], dtype=jnp.int32)
            allowed = key_pos[None, :] <= query_pos[:, None]
            scores = jnp.where(allowed, scores, -1e30)
            new_max = jnp.maximum(row_max, jnp.max(scores, axis=-1))
            rescale = jnp.exp(row_max - new_max)
            weights_exp = jnp.where(allowed, jnp.exp(scores - new_max[..., None]), 0.0)
            row_sum = row_sum * rescale + jnp.sum(weights_exp, axis=-1)
            weighted = weighted * rescale[..., None] + jnp.einsum(
                "gjqk,kgd->gjqd",
                weights_exp.astype(jnp.bfloat16),
                value_rows,
                preferred_element_type=jnp.float32,
            )
            return (new_max, row_sum, weighted)

        return (lax.cond(first_key <= last_query, absorb, lambda held: held, running), None)

    start_state = (
        jnp.full((kv_count, per_key, rows_here), -1e30, jnp.float32),
        jnp.zeros((kv_count, per_key, rows_here), jnp.float32),
        jnp.zeros((kv_count, per_key, rows_here, HEAD_DIM), jnp.float32),
    )
    running = start_state
    both = gathered(jnp.concatenate([keys, values], axis=1), CTX)
    both = both.reshape(-1, both.shape[-1])
    key_piece = both[:, : keys.shape[1]]
    value_piece = both[:, keys.shape[1] :]
    count = key_piece.shape[0]
    width = math.gcd(count, 1024)
    blocks = count // width
    key_rows = key_piece.reshape(blocks, width, kv_count, HEAD_DIM)
    value_rows = value_piece.reshape(blocks, width, kv_count, HEAD_DIM)
    starts = width * jnp.arange(blocks, dtype=jnp.int32)
    running, unused = lax.scan(key_block, running, (key_rows, value_rows, starts))
    row_max, row_sum, weighted = running
    mixed = (weighted / row_sum[..., None]).transpose(2, 0, 1, 3).reshape(rows_here, -1)
    return mixed.astype(jnp.bfloat16)


def take_half(array, axis_dim, section):
    width = array.shape[axis_dim] // 2
    return lax.dynamic_slice_in_dim(array, section * width, width, axis_dim)


def per_device(
    resid_in,
    ssm_input,
    ssm_gate,
    ssm_in_b,
    ssm_out_c,
    step_size,
    decay_rate,
    skip_gain,
    norm_gain,
    queries,
    keys,
    values,
    out_weights,
):
    section = lax.axis_index("pipe")
    ctx_rank = lax.axis_index("y") * lax.axis_size("zc") + lax.axis_index("zc")
    mamba_part = mamba_mixer(
        take_half(ssm_input, 1, section),
        take_half(ssm_gate, 1, section),
        take_half(ssm_in_b, 1, section),
        take_half(ssm_out_c, 1, section),
        take_half(step_size, 1, section),
        take_half(decay_rate, 0, section),
        take_half(skip_gain, 0, section),
        take_half(norm_gain, 0, section),
    )
    attn_part = attention(
        take_half(queries, 1, section),
        take_half(keys, 1, section),
        take_half(values, 1, section),
        ctx_rank,
    )
    outgoing = jnp.where(section == 0, attn_part, mamba_part)
    kept_half = jnp.where(section == 0, mamba_part, attn_part)
    incoming = from_partner(outgoing, "pipe", 0)
    weights_all = lax.all_gather(out_weights, CTX, axis=2, tiled=True)[0]
    width = kept_half.shape[1]
    half = weights_all.shape[1] // 2
    tp_rank = lax.axis_index("tp")
    own_w = lax.dynamic_slice_in_dim(weights_all, section * width, width, 0)
    other_w = lax.dynamic_slice_in_dim(weights_all, (1 - section) * width, width, 0)

    def project(start):
        near = jnp.dot(
            kept_half,
            lax.dynamic_slice_in_dim(own_w, start, half, 1),
            preferred_element_type=jnp.float32,
        )
        far = jnp.dot(
            incoming,
            lax.dynamic_slice_in_dim(other_w, start, half, 1),
            preferred_element_type=jnp.float32,
        )
        return near + far

    sent = project((1 - tp_rank) * half).astype(jnp.bfloat16)
    from_tp = from_partner(sent, "tp", 0)
    kept = project(tp_rank * half)
    kept_low = kept.astype(jnp.bfloat16)
    first_kept = shifted(kept_low, "pipe", 1)
    first_sent = lax.ppermute(sent, ("pipe", "tp"), [(0, 3), (1, 2)])
    base = resid_in.astype(jnp.float32)
    own_section = (
        (base + kept_low.astype(jnp.float32)) + from_tp.astype(jnp.float32)
    ).astype(jnp.bfloat16)
    rebuilt = (
        (base + first_kept.astype(jnp.float32)) + first_sent.astype(jnp.float32)
    ).astype(jnp.bfloat16)
    second_section = (
        rebuilt.astype(jnp.float32) + (kept + from_tp.astype(jnp.float32))
    ).astype(jnp.bfloat16)
    return jnp.where(section == 0, own_section, second_section)[None]


def solution(mesh):
    pipe, ctx, tp = (mesh.shape[name] for name in ("pipe", "ctx", "tp"))
    outer = 4 if ctx % 4 == 0 else 1
    split = jax.sharding.Mesh(
        mesh.devices.reshape(pipe, outer, ctx // outer, tp), ("pipe", "y", "zc", "tp")
    )
    return jax.shard_map(
        per_device,
        mesh=split,
        in_specs=(
            P(CTX, "tp"),
            P(CTX, "tp"),
            P(CTX, "tp"),
            P(CTX, "tp"),
            P(CTX, "tp"),
            P(CTX, "tp"),
            P("tp"),
            P("tp"),
            P("tp"),
            P(CTX, "tp"),
            P(CTX, "tp"),
            P(CTX, "tp"),
            P("pipe", "tp", CTX),
        ),
        out_specs=P("pipe", CTX, "tp"),
        check_vma=False,
    )
```

```python
import math

import jax
import jax.numpy as jnp
from jax import lax
from jax.sharding import PartitionSpec as P

MHEAD_DIM = 64
STATE = 128
SCAN_BLOCK = 128
HEAD_DIM = 128


exact_mode = lax.Precision.HIGHEST
norm_eps = 1e-05


def entering_2(x, axis, combine, identity):
    peers, position = (lax.axis_size(axis), lax.axis_index(axis))
    everything = jax.tree.map(
        lambda part, kind: lax.all_gather(part.astype(kind), axis), x, (jnp.bfloat16, jnp.bfloat16)
    )
    start = jax.tree.map(
        lambda part, zero: jnp.broadcast_to(jnp.asarray(zero, part.dtype), part.shape), x, identity
    )

    def turn(k, before):
        reached = k < position
        new = combine(
            before, jax.tree.map(lambda part, own: part[k].astype(own.dtype), everything, x)
        )
        return jax.tree.map(lambda a, b: jnp.where(reached, a, b), new, before)

    return lax.fori_loop(0, peers, turn, start)


CTX = ("y", "zc")


def gathered(x, axis):
    peers = lax.axis_size(axis)
    spread = jnp.broadcast_to(x[None], (peers,) + x.shape)
    return lax.all_to_all(spread, axis, 0, 0)


def entering_states(through_log, local_state):
    outer = lax.axis_size("y")
    inner = lax.axis_size("zc")
    peers = outer * inner
    rank = lax.axis_index("y") * inner + lax.axis_index("zc")
    logs = gathered(through_log, CTX)
    logs = logs.reshape((peers,) + through_log.shape)
    places = jnp.arange(peers, dtype=jnp.int32)

    def span_weight(k, upto):
        inside = (places[None, :] > k[:, None]) & (places[None, :] < upto)
        summed = jnp.sum(jnp.where(inside[:, :, None, None], logs[None], 0.0), axis=1)
        return jnp.where((k < upto)[:, None, None], jnp.exp(summed), 0.0)

    first = lax.axis_index("y") * inner
    near = gathered(local_state.astype(jnp.bfloat16), "zc").astype(jnp.float32)
    near_ids = first + jnp.arange(inner, dtype=jnp.int32)
    own_part = jnp.einsum(
        "kgj,kgjpn->gjpn", span_weight(near_ids, rank), near, precision=exact_mode
    )
    group_end = first + inner
    group_total = jnp.einsum(
        "kgj,kgjpn->gjpn", span_weight(near_ids, group_end), near, precision=exact_mode
    )
    far = gathered(group_total.astype(jnp.bfloat16), "y").astype(jnp.float32)
    far_ends = (jnp.arange(outer, dtype=jnp.int32) + 1) * inner - 1
    far_weight = span_weight(far_ends, rank)
    far_weight = jnp.where((far_ends < first)[:, None, None], far_weight, 0.0)
    far_part = jnp.einsum("kgj,kgjpn->gjpn", far_weight, far, precision=exact_mode)
    return own_part + far_part


def from_partner(block, axis, distance):
    count = lax.axis_size(axis)
    route = []
    for low in range(count):
        high = low | 1 << distance
        if high != low and high < count:
            route += [(low, high), (high, low)]
    return lax.ppermute(block, axis, route)


def shifted(x, axis, by):
    peers = lax.axis_size(axis)
    pairs = [(i, i + by) for i in range(peers) if 0 <= i + by < peers]
    return lax.ppermute(x, axis, pairs)


def block_scan(state_now, inputs_x, input_b, output_c, step_rows, log_decay):
    width = inputs_x.shape[0]
    groups = inputs_x.shape[1]
    per_group = inputs_x.shape[2]
    running = jnp.cumsum(log_decay, axis=0)
    spread = running[:, None, :] - running[None, :, :]
    causal = (
        jnp.arange(width, dtype=jnp.int32)[:, None] >= jnp.arange(width, dtype=jnp.int32)[None, :]
    )
    decay_mat = jnp.exp(jnp.where(causal[:, :, None], spread, -jnp.inf))
    decay_mat = decay_mat.reshape(width, width, groups, per_group).transpose(2, 3, 0, 1)
    cross_cb = jnp.einsum("tgn,sgn->gts", output_c, input_b, precision=exact_mode)
    step_cols = step_rows.reshape(width, groups, per_group).transpose(1, 2, 0)
    mixing = cross_cb[:, None, :, :] * decay_mat * step_cols[:, :, None, :]
    within = jnp.einsum("gjts,sgjp->tgjp", mixing, inputs_x, precision=exact_mode)
    entry = jnp.exp(running).reshape(width, groups, per_group)
    carried = (
        jnp.einsum("tgn,gjpn->tgjp", output_c, state_now, precision=exact_mode)
        * entry[:, :, :, None]
    )
    tail_weight = (jnp.exp(running[-1][None, :] - running) * step_rows).reshape(
        width, groups, per_group
    )
    leaving = jnp.exp(running[-1]).reshape(groups, per_group)
    state_next = leaving[:, :, None, None] * state_now + jnp.einsum(
        "sgj,sgjp,sgn->gjpn", tail_weight, inputs_x, input_b, precision=exact_mode
    )
    return (state_next, within + carried)


def gate_norm(values_y, gate_in, gains, groups):
    rows_here = values_y.shape[0]
    gated = values_y * jax.nn.silu(gate_in.astype(jnp.float32))
    grouped = gated.reshape(rows_here, groups, -1)
    meansq = jnp.mean(grouped * grouped, axis=-1, keepdims=True)
    scaled = (grouped * lax.rsqrt(meansq + norm_eps)).reshape(rows_here, -1)
    return (scaled * gains[None, :]).astype(jnp.bfloat16)


def join_states(earlier, later):
    return (earlier[0] * later[0], later[0][:, :, None, None] * earlier[1] + later[1])


def mamba_mixer(
    ssm_input, ssm_gate, ssm_in_b, ssm_out_c, step_size, decay_rate, skip_gain, norm_gain
):
    rows_here = ssm_input.shape[0]
    head_count = decay_rate.shape[0]
    groups = ssm_in_b.shape[1] // STATE
    per_group = head_count // groups
    block_count = rows_here // SCAN_BLOCK
    log_decay = -step_size * decay_rate[None, :]
    inputs_x = ssm_input.reshape(block_count, SCAN_BLOCK, groups, per_group, MHEAD_DIM)
    input_b = ssm_in_b.reshape(block_count, SCAN_BLOCK, groups, STATE)
    output_c = ssm_out_c.reshape(block_count, SCAN_BLOCK, groups, STATE)

    def block_turn(state_now, block_data):
        part_x, part_b, part_c, part_step, part_log = block_data
        return block_scan(
            state_now,
            part_x.astype(jnp.float32),
            part_b.astype(jnp.float32),
            part_c.astype(jnp.float32),
            part_step,
            part_log,
        )

    start_state = jnp.zeros((groups, per_group, MHEAD_DIM, STATE), jnp.float32)
    local_state, pieces = lax.scan(
        block_turn,
        start_state,
        (
            inputs_x,
            input_b,
            output_c,
            step_size.reshape(block_count, SCAN_BLOCK, head_count),
            log_decay.reshape(block_count, SCAN_BLOCK, head_count),
        ),
    )
    running = jnp.cumsum(log_decay, axis=0)
    entering = entering_states(running[-1].reshape(groups, per_group), local_state)
    output_all = ssm_out_c.astype(jnp.float32).reshape(rows_here, groups, STATE)
    carried = (
        jnp.einsum("tgn,gjpn->tgjp", output_all, entering, precision=exact_mode)
        * jnp.exp(running).reshape(rows_here, groups, per_group)[:, :, :, None]
    )
    skipped = (
        ssm_input.astype(jnp.float32).reshape(rows_here, groups, per_group, MHEAD_DIM)
        * skip_gain.reshape(groups, per_group)[None, :, :, None]
    )
    values_y = pieces.reshape(rows_here, groups, per_group, MHEAD_DIM) + carried + skipped
    return gate_norm(values_y.reshape(rows_here, -1), ssm_gate, norm_gain, groups)


def attention(queries, keys, values, ctx_rank):
    rows_here = queries.shape[0]
    kv_count = keys.shape[1] // HEAD_DIM
    per_key = queries.shape[1] // HEAD_DIM // kv_count
    query_groups = queries.reshape(rows_here, kv_count, per_key, HEAD_DIM)
    query_pos = ctx_rank * rows_here + jnp.arange(rows_here, dtype=jnp.int32)
    last_query = query_pos[-1]
    score_scale = 1.0 / math.sqrt(HEAD_DIM)

    def key_block(running, block_data):
        key_rows, value_rows, first_key = block_data

        def absorb(held):
            row_max, row_sum, weighted = held
            scores = (
                jnp.einsum(
                    "qgjd,kgd->gjqk", query_groups, key_rows, preferred_element_type=jnp.float32
                )
                * score_scale
            )
            key_pos = first_key + jnp.arange(key_rows.shape[0], dtype=jnp.int32)
            allowed = key_pos[None, :] <= query_pos[:, None]
            scores = jnp.where(allowed, scores, -1e30)
            new_max = jnp.maximum(row_max, jnp.max(scores, axis=-1))
            rescale = jnp.exp(row_max - new_max)
            weights_exp = jnp.where(allowed, jnp.exp(scores - new_max[..., None]), 0.0)
            row_sum = row_sum * rescale + jnp.sum(weights_exp, axis=-1)
            weighted = weighted * rescale[..., None] + jnp.einsum(
                "gjqk,kgd->gjqd",
                weights_exp.astype(jnp.bfloat16),
                value_rows,
                preferred_element_type=jnp.float32,
            )
            return (new_max, row_sum, weighted)

        return (lax.cond(first_key <= last_query, absorb, lambda held: held, running), None)

    start_state = (
        jnp.full((kv_count, per_key, rows_here), -1e30, jnp.float32),
        jnp.zeros((kv_count, per_key, rows_here), jnp.float32),
        jnp.zeros((kv_count, per_key, rows_here, HEAD_DIM), jnp.float32),
    )
    running = start_state
    both = lax.all_gather(jnp.concatenate([keys, values], axis=1), CTX, axis=0, tiled=True)
    key_piece = both[:, : keys.shape[1]]
    value_piece = both[:, keys.shape[1] :]
    count = key_piece.shape[0]
    width = math.gcd(count, 1024)
    blocks = count // width
    key_rows = key_piece.reshape(blocks, width, kv_count, HEAD_DIM)
    value_rows = value_piece.reshape(blocks, width, kv_count, HEAD_DIM)
    starts = width * jnp.arange(blocks, dtype=jnp.int32)
    running, unused = lax.scan(key_block, running, (key_rows, value_rows, starts))
    row_max, row_sum, weighted = running
    mixed = (weighted / row_sum[..., None]).transpose(2, 0, 1, 3).reshape(rows_here, -1)
    return mixed.astype(jnp.bfloat16)


def take_half(array, axis_dim, section):
    width = array.shape[axis_dim] // 2
    return lax.dynamic_slice_in_dim(array, section * width, width, axis_dim)


def per_device(
    resid_in,
    ssm_input,
    ssm_gate,
    ssm_in_b,
    ssm_out_c,
    step_size,
    decay_rate,
    skip_gain,
    norm_gain,
    queries,
    keys,
    values,
    out_weights,
):
    section = lax.axis_index("pipe")
    ctx_rank = lax.axis_index("y") * lax.axis_size("zc") + lax.axis_index("zc")
    mamba_part = mamba_mixer(
        take_half(ssm_input, 1, section),
        take_half(ssm_gate, 1, section),
        take_half(ssm_in_b, 1, section),
        take_half(ssm_out_c, 1, section),
        take_half(step_size, 1, section),
        take_half(decay_rate, 0, section),
        take_half(skip_gain, 0, section),
        take_half(norm_gain, 0, section),
    )
    attn_part = attention(
        take_half(queries, 1, section),
        take_half(keys, 1, section),
        take_half(values, 1, section),
        ctx_rank,
    )
    outgoing = jnp.where(section == 0, attn_part, mamba_part)
    kept_half = jnp.where(section == 0, mamba_part, attn_part)
    incoming = from_partner(outgoing, "pipe", 0)
    mixed_rows = jnp.where(
        section == 0,
        jnp.concatenate([kept_half, incoming], axis=1),
        jnp.concatenate([incoming, kept_half], axis=1),
    )
    weights_all = lax.all_gather(out_weights, CTX, axis=2, tiled=True)[0]
    half = weights_all.shape[1] // 2
    tp_rank = lax.axis_index("tp")
    sent_cols = lax.dynamic_slice_in_dim(weights_all, (1 - tp_rank) * half, half, 1)
    kept_cols = lax.dynamic_slice_in_dim(weights_all, tp_rank * half, half, 1)
    sent = jnp.dot(mixed_rows, sent_cols, preferred_element_type=jnp.float32).astype(jnp.bfloat16)
    from_tp = from_partner(sent, "tp", 0)
    kept = jnp.dot(mixed_rows, kept_cols, preferred_element_type=jnp.float32)
    kept_low = kept.astype(jnp.bfloat16)
    first_kept = shifted(kept_low, "pipe", 1)
    first_sent = lax.ppermute(sent, ("pipe", "tp"), [(0, 3), (1, 2)])
    base = resid_in.astype(jnp.float32)
    own_section = (
        (base + kept_low.astype(jnp.float32)) + from_tp.astype(jnp.float32)
    ).astype(jnp.bfloat16)
    rebuilt = (
        (base + first_kept.astype(jnp.float32)) + first_sent.astype(jnp.float32)
    ).astype(jnp.bfloat16)
    second_section = (
        rebuilt.astype(jnp.float32) + (kept + from_tp.astype(jnp.float32))
    ).astype(jnp.bfloat16)
    return jnp.where(section == 0, own_section, second_section)[None]


def solution(mesh):
    pipe, ctx, tp = (mesh.shape[name] for name in ("pipe", "ctx", "tp"))
    outer = 4 if ctx % 4 == 0 else 1
    split = jax.sharding.Mesh(
        mesh.devices.reshape(pipe, outer, ctx // outer, tp), ("pipe", "y", "zc", "tp")
    )
    return jax.shard_map(
        per_device,
        mesh=split,
        in_specs=(
            P(CTX, "tp"),
            P(CTX, "tp"),
            P(CTX, "tp"),
            P(CTX, "tp"),
            P(CTX, "tp"),
            P(CTX, "tp"),
            P("tp"),
            P("tp"),
            P("tp"),
            P(CTX, "tp"),
            P(CTX, "tp"),
            P(CTX, "tp"),
            P("pipe", "tp", CTX),
        ),
        out_specs=P("pipe", CTX, "tp"),
        check_vma=False,
    )
```

```python
import math

import jax
import jax.numpy as jnp
from jax import lax
from jax.sharding import PartitionSpec as P

MHEAD_DIM = 64
STATE = 128
SCAN_BLOCK = 128
HEAD_DIM = 128


exact_mode = lax.Precision.HIGHEST
norm_eps = 1e-05


def entering_2(x, axis, combine, identity):
    peers, position = (lax.axis_size(axis), lax.axis_index(axis))
    everything = jax.tree.map(
        lambda part, kind: lax.all_gather(part.astype(kind), axis), x, (jnp.bfloat16, jnp.bfloat16)
    )
    start = jax.tree.map(
        lambda part, zero: jnp.broadcast_to(jnp.asarray(zero, part.dtype), part.shape), x, identity
    )

    def turn(k, before):
        reached = k < position
        new = combine(
            before, jax.tree.map(lambda part, own: part[k].astype(own.dtype), everything, x)
        )
        return jax.tree.map(lambda a, b: jnp.where(reached, a, b), new, before)

    return lax.fori_loop(0, peers, turn, start)


CTX = ("y", "zc")


def gathered(x, axis):
    peers = lax.axis_size(axis)
    spread = jnp.broadcast_to(x[None], (peers,) + x.shape)
    return lax.all_to_all(spread, axis, 0, 0)


def entering_states(through_log, local_state):
    outer = lax.axis_size("y")
    inner = lax.axis_size("zc")
    peers = outer * inner
    rank = lax.axis_index("y") * inner + lax.axis_index("zc")
    logs = gathered(through_log, CTX)
    logs = logs.reshape((peers,) + through_log.shape)
    places = jnp.arange(peers, dtype=jnp.int32)

    def span_weight(k, upto):
        inside = (places[None, :] > k[:, None]) & (places[None, :] < upto)
        summed = jnp.sum(jnp.where(inside[:, :, None, None], logs[None], 0.0), axis=1)
        return jnp.where((k < upto)[:, None, None], jnp.exp(summed), 0.0)

    first = lax.axis_index("y") * inner
    near = gathered(local_state.astype(jnp.bfloat16), "zc").astype(jnp.float32)
    near_ids = first + jnp.arange(inner, dtype=jnp.int32)
    own_part = jnp.einsum(
        "kgj,kgjpn->gjpn", span_weight(near_ids, rank), near, precision=exact_mode
    )
    group_end = first + inner
    group_total = jnp.einsum(
        "kgj,kgjpn->gjpn", span_weight(near_ids, group_end), near, precision=exact_mode
    )
    far = gathered(group_total.astype(jnp.bfloat16), "y").astype(jnp.float32)
    far_ends = (jnp.arange(outer, dtype=jnp.int32) + 1) * inner - 1
    far_weight = span_weight(far_ends, rank)
    far_weight = jnp.where((far_ends < first)[:, None, None], far_weight, 0.0)
    far_part = jnp.einsum("kgj,kgjpn->gjpn", far_weight, far, precision=exact_mode)
    return own_part + far_part


def from_partner(block, axis, distance):
    count = lax.axis_size(axis)
    route = []
    for low in range(count):
        high = low | 1 << distance
        if high != low and high < count:
            route += [(low, high), (high, low)]
    return lax.ppermute(block, axis, route)


def shifted(x, axis, by):
    peers = lax.axis_size(axis)
    pairs = [(i, i + by) for i in range(peers) if 0 <= i + by < peers]
    return lax.ppermute(x, axis, pairs)


def block_scan(state_now, inputs_x, input_b, output_c, step_rows, log_decay):
    width = inputs_x.shape[0]
    groups = inputs_x.shape[1]
    per_group = inputs_x.shape[2]
    running = jnp.cumsum(log_decay, axis=0)
    spread = running[:, None, :] - running[None, :, :]
    causal = (
        jnp.arange(width, dtype=jnp.int32)[:, None] >= jnp.arange(width, dtype=jnp.int32)[None, :]
    )
    decay_mat = jnp.exp(jnp.where(causal[:, :, None], spread, -jnp.inf))
    decay_mat = decay_mat.reshape(width, width, groups, per_group).transpose(2, 3, 0, 1)
    cross_cb = jnp.einsum("tgn,sgn->gts", output_c, input_b, precision=exact_mode)
    step_cols = step_rows.reshape(width, groups, per_group).transpose(1, 2, 0)
    mixing = cross_cb[:, None, :, :] * decay_mat * step_cols[:, :, None, :]
    within = jnp.einsum("gjts,sgjp->tgjp", mixing, inputs_x, precision=exact_mode)
    entry = jnp.exp(running).reshape(width, groups, per_group)
    carried = (
        jnp.einsum("tgn,gjpn->tgjp", output_c, state_now, precision=exact_mode)
        * entry[:, :, :, None]
    )
    tail_weight = (jnp.exp(running[-1][None, :] - running) * step_rows).reshape(
        width, groups, per_group
    )
    leaving = jnp.exp(running[-1]).reshape(groups, per_group)
    state_next = leaving[:, :, None, None] * state_now + jnp.einsum(
        "sgj,sgjp,sgn->gjpn", tail_weight, inputs_x, input_b, precision=exact_mode
    )
    return (state_next, within + carried)


def gate_norm(values_y, gate_in, gains, groups):
    rows_here = values_y.shape[0]
    gated = values_y * jax.nn.silu(gate_in.astype(jnp.float32))
    grouped = gated.reshape(rows_here, groups, -1)
    meansq = jnp.mean(grouped * grouped, axis=-1, keepdims=True)
    scaled = (grouped * lax.rsqrt(meansq + norm_eps)).reshape(rows_here, -1)
    return (scaled * gains[None, :]).astype(jnp.bfloat16)


def join_states(earlier, later):
    return (earlier[0] * later[0], later[0][:, :, None, None] * earlier[1] + later[1])


def mamba_mixer(
    ssm_input, ssm_gate, ssm_in_b, ssm_out_c, step_size, decay_rate, skip_gain, norm_gain
):
    rows_here = ssm_input.shape[0]
    head_count = decay_rate.shape[0]
    groups = ssm_in_b.shape[1] // STATE
    per_group = head_count // groups
    block_count = rows_here // SCAN_BLOCK
    log_decay = -step_size * decay_rate[None, :]
    inputs_x = ssm_input.reshape(block_count, SCAN_BLOCK, groups, per_group, MHEAD_DIM)
    input_b = ssm_in_b.reshape(block_count, SCAN_BLOCK, groups, STATE)
    output_c = ssm_out_c.reshape(block_count, SCAN_BLOCK, groups, STATE)

    def block_turn(state_now, block_data):
        part_x, part_b, part_c, part_step, part_log = block_data
        return block_scan(
            state_now,
            part_x.astype(jnp.float32),
            part_b.astype(jnp.float32),
            part_c.astype(jnp.float32),
            part_step,
            part_log,
        )

    start_state = jnp.zeros((groups, per_group, MHEAD_DIM, STATE), jnp.float32)
    local_state, pieces = lax.scan(
        block_turn,
        start_state,
        (
            inputs_x,
            input_b,
            output_c,
            step_size.reshape(block_count, SCAN_BLOCK, head_count),
            log_decay.reshape(block_count, SCAN_BLOCK, head_count),
        ),
    )
    running = jnp.cumsum(log_decay, axis=0)
    entering = entering_states(running[-1].reshape(groups, per_group), local_state)
    output_all = ssm_out_c.astype(jnp.float32).reshape(rows_here, groups, STATE)
    carried = (
        jnp.einsum("tgn,gjpn->tgjp", output_all, entering, precision=exact_mode)
        * jnp.exp(running).reshape(rows_here, groups, per_group)[:, :, :, None]
    )
    skipped = (
        ssm_input.astype(jnp.float32).reshape(rows_here, groups, per_group, MHEAD_DIM)
        * skip_gain.reshape(groups, per_group)[None, :, :, None]
    )
    values_y = pieces.reshape(rows_here, groups, per_group, MHEAD_DIM) + carried + skipped
    return gate_norm(values_y.reshape(rows_here, -1), ssm_gate, norm_gain, groups)


def attention(queries, both, key_width, ctx_rank):
    rows_here = queries.shape[0]
    kv_count = key_width // HEAD_DIM
    per_key = queries.shape[1] // HEAD_DIM // kv_count
    query_groups = queries.reshape(rows_here, kv_count, per_key, HEAD_DIM)
    query_pos = ctx_rank * rows_here + jnp.arange(rows_here, dtype=jnp.int32)
    last_query = query_pos[-1]
    score_scale = 1.0 / math.sqrt(HEAD_DIM)

    def key_block(running, block_data):
        key_rows, value_rows, first_key = block_data

        def absorb(held):
            row_max, row_sum, weighted = held
            scores = (
                jnp.einsum(
                    "qgjd,kgd->gjqk", query_groups, key_rows, preferred_element_type=jnp.float32
                )
                * score_scale
            )
            key_pos = first_key + jnp.arange(key_rows.shape[0], dtype=jnp.int32)
            allowed = key_pos[None, :] <= query_pos[:, None]
            scores = jnp.where(allowed, scores, -1e30)
            new_max = jnp.maximum(row_max, jnp.max(scores, axis=-1))
            rescale = jnp.exp(row_max - new_max)
            weights_exp = jnp.where(allowed, jnp.exp(scores - new_max[..., None]), 0.0)
            row_sum = row_sum * rescale + jnp.sum(weights_exp, axis=-1)
            weighted = weighted * rescale[..., None] + jnp.einsum(
                "gjqk,kgd->gjqd",
                weights_exp.astype(jnp.bfloat16),
                value_rows,
                preferred_element_type=jnp.float32,
            )
            return (new_max, row_sum, weighted)

        return (lax.cond(first_key <= last_query, absorb, lambda held: held, running), None)

    start_state = (
        jnp.full((kv_count, per_key, rows_here), -1e30, jnp.float32),
        jnp.zeros((kv_count, per_key, rows_here), jnp.float32),
        jnp.zeros((kv_count, per_key, rows_here, HEAD_DIM), jnp.float32),
    )
    running = start_state
    key_piece = both[:, :key_width]
    value_piece = both[:, key_width:]
    count = key_piece.shape[0]
    width = math.gcd(count, 1024)
    blocks = count // width
    key_rows = key_piece.reshape(blocks, width, kv_count, HEAD_DIM)
    value_rows = value_piece.reshape(blocks, width, kv_count, HEAD_DIM)
    starts = width * jnp.arange(blocks, dtype=jnp.int32)
    running, unused = lax.scan(key_block, running, (key_rows, value_rows, starts))
    row_max, row_sum, weighted = running
    mixed = (weighted / row_sum[..., None]).transpose(2, 0, 1, 3).reshape(rows_here, -1)
    return mixed.astype(jnp.bfloat16)


def take_half(array, axis_dim, section):
    width = array.shape[axis_dim] // 2
    return lax.dynamic_slice_in_dim(array, section * width, width, axis_dim)


def per_device(
    resid_in,
    ssm_input,
    ssm_gate,
    ssm_in_b,
    ssm_out_c,
    step_size,
    decay_rate,
    skip_gain,
    norm_gain,
    queries,
    keys,
    values,
    out_weights,
):
    section = lax.axis_index("pipe")
    ctx_rank = lax.axis_index("y") * lax.axis_size("zc") + lax.axis_index("zc")
    mamba_part = mamba_mixer(
        take_half(ssm_input, 1, section),
        take_half(ssm_gate, 1, section),
        take_half(ssm_in_b, 1, section),
        take_half(ssm_out_c, 1, section),
        take_half(step_size, 1, section),
        take_half(decay_rate, 0, section),
        take_half(skip_gain, 0, section),
        take_half(norm_gain, 0, section),
    )
    key_half = take_half(keys, 1, section)
    kv_own = jnp.concatenate([key_half, take_half(values, 1, section)], axis=1)
    weights_own = out_weights[0].T
    channels = weights_own.shape[1]
    joint = lax.all_gather(
        jnp.concatenate([weights_own, kv_own], axis=1), CTX, axis=0, tiled=True
    )
    weights_t = joint[:, :channels]
    attn_part = attention(
        take_half(queries, 1, section), joint[:, channels:], key_half.shape[1], ctx_rank
    )
    outgoing = jnp.where(section == 0, attn_part, mamba_part)
    kept_half = jnp.where(section == 0, mamba_part, attn_part)
    incoming = from_partner(outgoing, "pipe", 0)
    mixed_rows = jnp.where(
        section == 0,
        jnp.concatenate([kept_half, incoming], axis=1),
        jnp.concatenate([incoming, kept_half], axis=1),
    )
    half = weights_t.shape[0] // 2
    tp_rank = lax.axis_index("tp")
    sent_cols = lax.dynamic_slice_in_dim(weights_t, (1 - tp_rank) * half, half, 0)
    kept_cols = lax.dynamic_slice_in_dim(weights_t, tp_rank * half, half, 0)
    sent = jnp.einsum(
        "tc,dc->td", mixed_rows, sent_cols, preferred_element_type=jnp.float32
    ).astype(jnp.bfloat16)
    from_tp = from_partner(sent, "tp", 0)
    kept = jnp.einsum("tc,dc->td", mixed_rows, kept_cols, preferred_element_type=jnp.float32)
    kept_low = kept.astype(jnp.bfloat16)
    first_kept = shifted(kept_low, "pipe", 1)
    first_sent = lax.ppermute(sent, ("pipe", "tp"), [(0, 3), (1, 2)])
    base = resid_in.astype(jnp.float32)
    own_section = (
        (base + kept_low.astype(jnp.float32)) + from_tp.astype(jnp.float32)
    ).astype(jnp.bfloat16)
    rebuilt = (
        (base + first_kept.astype(jnp.float32)) + first_sent.astype(jnp.float32)
    ).astype(jnp.bfloat16)
    second_section = (
        rebuilt.astype(jnp.float32) + (kept + from_tp.astype(jnp.float32))
    ).astype(jnp.bfloat16)
    return jnp.where(section == 0, own_section, second_section)[None]


def solution(mesh):
    pipe, ctx, tp = (mesh.shape[name] for name in ("pipe", "ctx", "tp"))
    outer = 4 if ctx % 4 == 0 else 1
    split = jax.sharding.Mesh(
        mesh.devices.reshape(pipe, outer, ctx // outer, tp), ("pipe", "y", "zc", "tp")
    )
    return jax.shard_map(
        per_device,
        mesh=split,
        in_specs=(
            P(CTX, "tp"),
            P(CTX, "tp"),
            P(CTX, "tp"),
            P(CTX, "tp"),
            P(CTX, "tp"),
            P(CTX, "tp"),
            P("tp"),
            P("tp"),
            P("tp"),
            P(CTX, "tp"),
            P(CTX, "tp"),
            P(CTX, "tp"),
            P("pipe", "tp", CTX),
        ),
        out_specs=P("pipe", CTX, "tp"),
        check_vma=False,
    )
```

```python
import math

import jax
import jax.numpy as jnp
from jax import lax
from jax.sharding import PartitionSpec as P

MHEAD_DIM = 64
STATE = 128
SCAN_BLOCK = 128
HEAD_DIM = 128


exact_mode = lax.Precision.HIGHEST
norm_eps = 1e-05


def entering_2(x, axis, combine, identity):
    peers, position = (lax.axis_size(axis), lax.axis_index(axis))
    everything = jax.tree.map(
        lambda part, kind: lax.all_gather(part.astype(kind), axis), x, (jnp.bfloat16, jnp.bfloat16)
    )
    start = jax.tree.map(
        lambda part, zero: jnp.broadcast_to(jnp.asarray(zero, part.dtype), part.shape), x, identity
    )

    def turn(k, before):
        reached = k < position
        new = combine(
            before, jax.tree.map(lambda part, own: part[k].astype(own.dtype), everything, x)
        )
        return jax.tree.map(lambda a, b: jnp.where(reached, a, b), new, before)

    return lax.fori_loop(0, peers, turn, start)


CTX = ("y", "z", "c")


def gathered(x, axis):
    peers = lax.axis_size(axis)
    spread = jnp.broadcast_to(x[None], (peers,) + x.shape)
    return lax.all_to_all(spread, axis, 0, 0)


def entering_states(through_log, local_state):
    outer, middle, pair = (lax.axis_size(name) for name in CTX)
    inner = middle * pair
    peers = outer * inner
    rank = lax.axis_index("y") * inner + lax.axis_index("z") * pair + lax.axis_index("c")
    logs = gathered(through_log, CTX)
    logs = logs.reshape((peers,) + through_log.shape)
    places = jnp.arange(peers, dtype=jnp.int32)

    def span_weight(k, upto):
        inside = (places[None, :] > k[:, None]) & (places[None, :] < upto)
        summed = jnp.sum(jnp.where(inside[:, :, None, None], logs[None], 0.0), axis=1)
        return jnp.where((k < upto)[:, None, None], jnp.exp(summed), 0.0)

    def mix(weight, states):
        return jnp.einsum("kgj,kgjpn->gjpn", weight, states, precision=exact_mode)

    first = lax.axis_index("y") * inner
    pair_first = first + lax.axis_index("z") * pair
    near = gathered(local_state.astype(jnp.bfloat16), "c").astype(jnp.float32)
    near_ids = pair_first + jnp.arange(pair, dtype=jnp.int32)
    pair_part = mix(span_weight(near_ids, rank), near)
    pair_total = mix(span_weight(near_ids, pair_first + pair), near)
    mid = gathered(pair_total.astype(jnp.bfloat16), "z").astype(jnp.float32)
    mid_ends = first + (jnp.arange(middle, dtype=jnp.int32) + 1) * pair - 1
    mid_weight = jnp.where((mid_ends < pair_first)[:, None, None], span_weight(mid_ends, rank), 0.0)
    group_part = mix(mid_weight, mid)
    group_total = mix(span_weight(mid_ends, first + inner), mid)
    far = gathered(group_total.astype(jnp.bfloat16), "y").astype(jnp.float32)
    far_ends = (jnp.arange(outer, dtype=jnp.int32) + 1) * inner - 1
    far_weight = jnp.where((far_ends < first)[:, None, None], span_weight(far_ends, rank), 0.0)
    far_part = mix(far_weight, far)
    return pair_part + group_part + far_part


def from_partner(block, axis, distance):
    count = lax.axis_size(axis)
    route = []
    for low in range(count):
        high = low | 1 << distance
        if high != low and high < count:
            route += [(low, high), (high, low)]
    return lax.ppermute(block, axis, route)


def shifted(x, axis, by):
    peers = lax.axis_size(axis)
    pairs = [(i, i + by) for i in range(peers) if 0 <= i + by < peers]
    return lax.ppermute(x, axis, pairs)


def block_scan(state_now, inputs_x, input_b, output_c, step_rows, log_decay):
    width = inputs_x.shape[0]
    groups = inputs_x.shape[1]
    per_group = inputs_x.shape[2]
    running = jnp.cumsum(log_decay, axis=0)
    spread = running[:, None, :] - running[None, :, :]
    causal = (
        jnp.arange(width, dtype=jnp.int32)[:, None] >= jnp.arange(width, dtype=jnp.int32)[None, :]
    )
    decay_mat = jnp.exp(jnp.where(causal[:, :, None], spread, -jnp.inf))
    decay_mat = decay_mat.reshape(width, width, groups, per_group).transpose(2, 3, 0, 1)
    cross_cb = jnp.einsum("tgn,sgn->gts", output_c, input_b, precision=exact_mode)
    step_cols = step_rows.reshape(width, groups, per_group).transpose(1, 2, 0)
    mixing = cross_cb[:, None, :, :] * decay_mat * step_cols[:, :, None, :]
    within = jnp.einsum("gjts,sgjp->tgjp", mixing, inputs_x, precision=exact_mode)
    entry = jnp.exp(running).reshape(width, groups, per_group)
    carried = (
        jnp.einsum("tgn,gjpn->tgjp", output_c, state_now, precision=exact_mode)
        * entry[:, :, :, None]
    )
    tail_weight = (jnp.exp(running[-1][None, :] - running) * step_rows).reshape(
        width, groups, per_group
    )
    leaving = jnp.exp(running[-1]).reshape(groups, per_group)
    state_next = leaving[:, :, None, None] * state_now + jnp.einsum(
        "sgj,sgjp,sgn->gjpn", tail_weight, inputs_x, input_b, precision=exact_mode
    )
    return (state_next, within + carried)


def gate_norm(values_y, gate_in, gains, groups):
    rows_here = values_y.shape[0]
    gated = values_y * jax.nn.silu(gate_in.astype(jnp.float32))
    grouped = gated.reshape(rows_here, groups, -1)
    meansq = jnp.mean(grouped * grouped, axis=-1, keepdims=True)
    scaled = (grouped * lax.rsqrt(meansq + norm_eps)).reshape(rows_here, -1)
    return (scaled * gains[None, :]).astype(jnp.bfloat16)


def join_states(earlier, later):
    return (earlier[0] * later[0], later[0][:, :, None, None] * earlier[1] + later[1])


def mamba_mixer(
    ssm_input, ssm_gate, ssm_in_b, ssm_out_c, step_size, decay_rate, skip_gain, norm_gain
):
    rows_here = ssm_input.shape[0]
    head_count = decay_rate.shape[0]
    groups = ssm_in_b.shape[1] // STATE
    per_group = head_count // groups
    block_count = rows_here // SCAN_BLOCK
    log_decay = -step_size * decay_rate[None, :]
    inputs_x = ssm_input.reshape(block_count, SCAN_BLOCK, groups, per_group, MHEAD_DIM)
    input_b = ssm_in_b.reshape(block_count, SCAN_BLOCK, groups, STATE)
    output_c = ssm_out_c.reshape(block_count, SCAN_BLOCK, groups, STATE)

    def block_turn(state_now, block_data):
        part_x, part_b, part_c, part_step, part_log = block_data
        return block_scan(
            state_now,
            part_x.astype(jnp.float32),
            part_b.astype(jnp.float32),
            part_c.astype(jnp.float32),
            part_step,
            part_log,
        )

    start_state = jnp.zeros((groups, per_group, MHEAD_DIM, STATE), jnp.float32)
    local_state, pieces = lax.scan(
        block_turn,
        start_state,
        (
            inputs_x,
            input_b,
            output_c,
            step_size.reshape(block_count, SCAN_BLOCK, head_count),
            log_decay.reshape(block_count, SCAN_BLOCK, head_count),
        ),
    )
    running = jnp.cumsum(log_decay, axis=0)
    entering = entering_states(running[-1].reshape(groups, per_group), local_state)
    output_all = ssm_out_c.astype(jnp.float32).reshape(rows_here, groups, STATE)
    carried = (
        jnp.einsum("tgn,gjpn->tgjp", output_all, entering, precision=exact_mode)
        * jnp.exp(running).reshape(rows_here, groups, per_group)[:, :, :, None]
    )
    skipped = (
        ssm_input.astype(jnp.float32).reshape(rows_here, groups, per_group, MHEAD_DIM)
        * skip_gain.reshape(groups, per_group)[None, :, :, None]
    )
    values_y = pieces.reshape(rows_here, groups, per_group, MHEAD_DIM) + carried + skipped
    return gate_norm(values_y.reshape(rows_here, -1), ssm_gate, norm_gain, groups)


def attention(queries, keys, values, ctx_rank):
    rows_here = queries.shape[0]
    kv_count = keys.shape[1] // HEAD_DIM
    per_key = queries.shape[1] // HEAD_DIM // kv_count
    query_groups = queries.reshape(rows_here, kv_count, per_key, HEAD_DIM)
    query_pos = ctx_rank * rows_here + jnp.arange(rows_here, dtype=jnp.int32)
    last_query = query_pos[-1]
    score_scale = 1.0 / math.sqrt(HEAD_DIM)

    def key_block(running, block_data):
        key_rows, value_rows, first_key = block_data

        def absorb(held):
            row_max, row_sum, weighted = held
            scores = (
                jnp.einsum(
                    "qgjd,kgd->gjqk", query_groups, key_rows, preferred_element_type=jnp.float32
                )
                * score_scale
            )
            key_pos = first_key + jnp.arange(key_rows.shape[0], dtype=jnp.int32)
            allowed = key_pos[None, :] <= query_pos[:, None]
            scores = jnp.where(allowed, scores, -1e30)
            new_max = jnp.maximum(row_max, jnp.max(scores, axis=-1))
            rescale = jnp.exp(row_max - new_max)
            weights_exp = jnp.where(allowed, jnp.exp(scores - new_max[..., None]), 0.0)
            row_sum = row_sum * rescale + jnp.sum(weights_exp, axis=-1)
            weighted = weighted * rescale[..., None] + jnp.einsum(
                "gjqk,kgd->gjqd",
                weights_exp.astype(jnp.bfloat16),
                value_rows,
                preferred_element_type=jnp.float32,
            )
            return (new_max, row_sum, weighted)

        return (lax.cond(first_key <= last_query, absorb, lambda held: held, running), None)

    start_state = (
        jnp.full((kv_count, per_key, rows_here), -1e30, jnp.float32),
        jnp.zeros((kv_count, per_key, rows_here), jnp.float32),
        jnp.zeros((kv_count, per_key, rows_here, HEAD_DIM), jnp.float32),
    )
    running = start_state
    both = lax.all_gather(jnp.concatenate([keys, values], axis=1), CTX, axis=0, tiled=True)
    key_piece = both[:, : keys.shape[1]]
    value_piece = both[:, keys.shape[1] :]
    count = key_piece.shape[0]
    width = math.gcd(count, 1024)
    blocks = count // width
    key_rows = key_piece.reshape(blocks, width, kv_count, HEAD_DIM)
    value_rows = value_piece.reshape(blocks, width, kv_count, HEAD_DIM)
    starts = width * jnp.arange(blocks, dtype=jnp.int32)
    running, unused = lax.scan(key_block, running, (key_rows, value_rows, starts))
    row_max, row_sum, weighted = running
    mixed = (weighted / row_sum[..., None]).transpose(2, 0, 1, 3).reshape(rows_here, -1)
    return mixed.astype(jnp.bfloat16)


def take_half(array, axis_dim, section):
    width = array.shape[axis_dim] // 2
    return lax.dynamic_slice_in_dim(array, section * width, width, axis_dim)


def per_device(
    resid_in,
    ssm_input,
    ssm_gate,
    ssm_in_b,
    ssm_out_c,
    step_size,
    decay_rate,
    skip_gain,
    norm_gain,
    queries,
    keys,
    values,
    out_weights,
):
    section = lax.axis_index("pipe")
    ctx_rank = (lax.axis_index("y") * lax.axis_size("z") + lax.axis_index("z")) * lax.axis_size(
        "c"
    ) + lax.axis_index("c")
    mamba_part = mamba_mixer(
        take_half(ssm_input, 1, section),
        take_half(ssm_gate, 1, section),
        take_half(ssm_in_b, 1, section),
        take_half(ssm_out_c, 1, section),
        take_half(step_size, 1, section),
        take_half(decay_rate, 0, section),
        take_half(skip_gain, 0, section),
        take_half(norm_gain, 0, section),
    )
    attn_part = attention(
        take_half(queries, 1, section),
        take_half(keys, 1, section),
        take_half(values, 1, section),
        ctx_rank,
    )
    outgoing = jnp.where(section == 0, attn_part, mamba_part)
    kept_half = jnp.where(section == 0, mamba_part, attn_part)
    incoming = from_partner(outgoing, "pipe", 0)
    mixed_rows = jnp.where(
        section == 0,
        jnp.concatenate([kept_half, incoming], axis=1),
        jnp.concatenate([incoming, kept_half], axis=1),
    )
    weights_all = lax.all_gather(out_weights, CTX, axis=2, tiled=True)[0]
    half = weights_all.shape[1] // 2
    tp_rank = lax.axis_index("tp")
    sent_cols = lax.dynamic_slice_in_dim(weights_all, (1 - tp_rank) * half, half, 1)
    kept_cols = lax.dynamic_slice_in_dim(weights_all, tp_rank * half, half, 1)
    sent = jnp.dot(mixed_rows, sent_cols, preferred_element_type=jnp.float32).astype(jnp.bfloat16)
    from_tp = from_partner(sent, "tp", 0)
    kept = jnp.dot(mixed_rows, kept_cols, preferred_element_type=jnp.float32)
    kept_low = kept.astype(jnp.bfloat16)
    first_kept = shifted(kept_low, "pipe", 1)
    first_sent = lax.ppermute(sent, ("pipe", "tp"), [(0, 3), (1, 2)])
    base = resid_in.astype(jnp.float32)
    own_section = (
        (base + kept_low.astype(jnp.float32)) + from_tp.astype(jnp.float32)
    ).astype(jnp.bfloat16)
    rebuilt = (
        (base + first_kept.astype(jnp.float32)) + first_sent.astype(jnp.float32)
    ).astype(jnp.bfloat16)
    second_section = (
        rebuilt.astype(jnp.float32) + (kept + from_tp.astype(jnp.float32))
    ).astype(jnp.bfloat16)
    return jnp.where(section == 0, own_section, second_section)[None]


def solution(mesh):
    pipe, ctx, tp = (mesh.shape[name] for name in ("pipe", "ctx", "tp"))
    outer = 4 if ctx % 4 == 0 else 1
    pair = 2 if ctx % (2 * outer) == 0 else 1
    split = jax.sharding.Mesh(
        mesh.devices.reshape(pipe, outer, ctx // outer // pair, pair, tp),
        ("pipe", "y", "z", "c", "tp"),
    )
    return jax.shard_map(
        per_device,
        mesh=split,
        in_specs=(
            P(CTX, "tp"),
            P(CTX, "tp"),
            P(CTX, "tp"),
            P(CTX, "tp"),
            P(CTX, "tp"),
            P(CTX, "tp"),
            P("tp"),
            P("tp"),
            P("tp"),
            P(CTX, "tp"),
            P(CTX, "tp"),
            P(CTX, "tp"),
            P("pipe", "tp", CTX),
        ),
        out_specs=P("pipe", CTX, "tp"),
        check_vma=False,
    )
```

```python
import math

import jax
import jax.numpy as jnp
from jax import lax
from jax.sharding import PartitionSpec as P

MHEAD_DIM = 64
STATE = 128
SCAN_BLOCK = 128
HEAD_DIM = 128


exact_mode = lax.Precision.HIGHEST
norm_eps = 1e-05


def entering_2(x, axis, combine, identity):
    peers, position = (lax.axis_size(axis), lax.axis_index(axis))
    everything = jax.tree.map(
        lambda part, kind: lax.all_gather(part.astype(kind), axis), x, (jnp.bfloat16, jnp.bfloat16)
    )
    start = jax.tree.map(
        lambda part, zero: jnp.broadcast_to(jnp.asarray(zero, part.dtype), part.shape), x, identity
    )

    def turn(k, before):
        reached = k < position
        new = combine(
            before, jax.tree.map(lambda part, own: part[k].astype(own.dtype), everything, x)
        )
        return jax.tree.map(lambda a, b: jnp.where(reached, a, b), new, before)

    return lax.fori_loop(0, peers, turn, start)


CTX = ("y", "z", "c")


def gathered(x, axis):
    peers = lax.axis_size(axis)
    spread = jnp.broadcast_to(x[None], (peers,) + x.shape)
    return lax.all_to_all(spread, axis, 0, 0)


def entering_states(through_log, local_state, riders):
    outer, middle, pair = (lax.axis_size(name) for name in CTX)
    inner = middle * pair
    peers = outer * inner
    rank = lax.axis_index("y") * inner + lax.axis_index("z") * pair + lax.axis_index("c")
    logs = gathered(through_log, CTX)
    logs = logs.reshape((peers,) + through_log.shape)
    places = jnp.arange(peers, dtype=jnp.int32)

    def span_weight(k, upto):
        inside = (places[None, :] > k[:, None]) & (places[None, :] < upto)
        summed = jnp.sum(jnp.where(inside[:, :, None, None], logs[None], 0.0), axis=1)
        return jnp.where((k < upto)[:, None, None], jnp.exp(summed), 0.0)

    def mix(weight, states):
        return jnp.einsum("kgj,kgjpn->gjpn", weight, states, precision=exact_mode)

    first = lax.axis_index("y") * inner
    pair_first = first + lax.axis_index("z") * pair
    lanes = local_state.shape[-1]
    rows = local_state.size // lanes

    def split(arrived, count):
        held = arrived[:, :rows].reshape((count,) + local_state.shape).astype(jnp.float32)
        return held, arrived[:, rows:].reshape(-1, lanes)

    payload = jnp.concatenate(
        [local_state.astype(jnp.bfloat16).reshape(rows, lanes), riders.reshape(-1, lanes)]
    )
    near, pair_riders = split(gathered(payload, "c"), pair)
    near_ids = pair_first + jnp.arange(pair, dtype=jnp.int32)
    pair_part = mix(span_weight(near_ids, rank), near)
    pair_total = mix(span_weight(near_ids, pair_first + pair), near)
    payload = jnp.concatenate([pair_total.astype(jnp.bfloat16).reshape(rows, lanes), pair_riders])
    mid, group_riders = split(gathered(payload, "z"), middle)
    mid_ends = first + (jnp.arange(middle, dtype=jnp.int32) + 1) * pair - 1
    mid_weight = jnp.where((mid_ends < pair_first)[:, None, None], span_weight(mid_ends, rank), 0.0)
    group_part = mix(mid_weight, mid)
    group_total = mix(span_weight(mid_ends, first + inner), mid)
    payload = jnp.concatenate(
        [group_total.astype(jnp.bfloat16).reshape(rows, lanes), group_riders]
    )
    far, all_riders = split(gathered(payload, "y"), outer)
    all_riders = all_riders.reshape(-1, riders.shape[1])
    far_ends = (jnp.arange(outer, dtype=jnp.int32) + 1) * inner - 1
    far_weight = jnp.where((far_ends < first)[:, None, None], span_weight(far_ends, rank), 0.0)
    far_part = mix(far_weight, far)
    return pair_part + group_part + far_part, all_riders


def from_partner(block, axis, distance):
    count = lax.axis_size(axis)
    route = []
    for low in range(count):
        high = low | 1 << distance
        if high != low and high < count:
            route += [(low, high), (high, low)]
    return lax.ppermute(block, axis, route)


def shifted(x, axis, by):
    peers = lax.axis_size(axis)
    pairs = [(i, i + by) for i in range(peers) if 0 <= i + by < peers]
    return lax.ppermute(x, axis, pairs)


def block_scan(state_now, inputs_x, input_b, output_c, step_rows, log_decay):
    width = inputs_x.shape[0]
    groups = inputs_x.shape[1]
    per_group = inputs_x.shape[2]
    running = jnp.cumsum(log_decay, axis=0)
    spread = running[:, None, :] - running[None, :, :]
    causal = (
        jnp.arange(width, dtype=jnp.int32)[:, None] >= jnp.arange(width, dtype=jnp.int32)[None, :]
    )
    decay_mat = jnp.exp(jnp.where(causal[:, :, None], spread, -jnp.inf))
    decay_mat = decay_mat.reshape(width, width, groups, per_group).transpose(2, 3, 0, 1)
    cross_cb = jnp.einsum("tgn,sgn->gts", output_c, input_b, precision=exact_mode)
    step_cols = step_rows.reshape(width, groups, per_group).transpose(1, 2, 0)
    mixing = cross_cb[:, None, :, :] * decay_mat * step_cols[:, :, None, :]
    within = jnp.einsum("gjts,sgjp->tgjp", mixing, inputs_x, precision=exact_mode)
    entry = jnp.exp(running).reshape(width, groups, per_group)
    carried = (
        jnp.einsum("tgn,gjpn->tgjp", output_c, state_now, precision=exact_mode)
        * entry[:, :, :, None]
    )
    tail_weight = (jnp.exp(running[-1][None, :] - running) * step_rows).reshape(
        width, groups, per_group
    )
    leaving = jnp.exp(running[-1]).reshape(groups, per_group)
    state_next = leaving[:, :, None, None] * state_now + jnp.einsum(
        "sgj,sgjp,sgn->gjpn", tail_weight, inputs_x, input_b, precision=exact_mode
    )
    return (state_next, within + carried)


def gate_norm(values_y, gate_in, gains, groups):
    rows_here = values_y.shape[0]
    gated = values_y * jax.nn.silu(gate_in.astype(jnp.float32))
    grouped = gated.reshape(rows_here, groups, -1)
    meansq = jnp.mean(grouped * grouped, axis=-1, keepdims=True)
    scaled = (grouped * lax.rsqrt(meansq + norm_eps)).reshape(rows_here, -1)
    return (scaled * gains[None, :]).astype(jnp.bfloat16)


def join_states(earlier, later):
    return (earlier[0] * later[0], later[0][:, :, None, None] * earlier[1] + later[1])


def mamba_mixer(
    ssm_input, ssm_gate, ssm_in_b, ssm_out_c, step_size, decay_rate, skip_gain, norm_gain, riders
):
    rows_here = ssm_input.shape[0]
    head_count = decay_rate.shape[0]
    groups = ssm_in_b.shape[1] // STATE
    per_group = head_count // groups
    block_count = rows_here // SCAN_BLOCK
    log_decay = -step_size * decay_rate[None, :]
    inputs_x = ssm_input.reshape(block_count, SCAN_BLOCK, groups, per_group, MHEAD_DIM)
    input_b = ssm_in_b.reshape(block_count, SCAN_BLOCK, groups, STATE)
    output_c = ssm_out_c.reshape(block_count, SCAN_BLOCK, groups, STATE)

    def block_turn(state_now, block_data):
        part_x, part_b, part_c, part_step, part_log = block_data
        return block_scan(
            state_now,
            part_x.astype(jnp.float32),
            part_b.astype(jnp.float32),
            part_c.astype(jnp.float32),
            part_step,
            part_log,
        )

    start_state = jnp.zeros((groups, per_group, MHEAD_DIM, STATE), jnp.float32)
    local_state, pieces = lax.scan(
        block_turn,
        start_state,
        (
            inputs_x,
            input_b,
            output_c,
            step_size.reshape(block_count, SCAN_BLOCK, head_count),
            log_decay.reshape(block_count, SCAN_BLOCK, head_count),
        ),
    )
    running = jnp.cumsum(log_decay, axis=0)
    entering, all_riders = entering_states(
        running[-1].reshape(groups, per_group), local_state, riders
    )
    output_all = ssm_out_c.astype(jnp.float32).reshape(rows_here, groups, STATE)
    carried = (
        jnp.einsum("tgn,gjpn->tgjp", output_all, entering, precision=exact_mode)
        * jnp.exp(running).reshape(rows_here, groups, per_group)[:, :, :, None]
    )
    skipped = (
        ssm_input.astype(jnp.float32).reshape(rows_here, groups, per_group, MHEAD_DIM)
        * skip_gain.reshape(groups, per_group)[None, :, :, None]
    )
    values_y = pieces.reshape(rows_here, groups, per_group, MHEAD_DIM) + carried + skipped
    return gate_norm(values_y.reshape(rows_here, -1), ssm_gate, norm_gain, groups), all_riders


def attention(queries, both, key_width, ctx_rank):
    rows_here = queries.shape[0]
    kv_count = key_width // HEAD_DIM
    per_key = queries.shape[1] // HEAD_DIM // kv_count
    query_groups = queries.reshape(rows_here, kv_count, per_key, HEAD_DIM)
    query_pos = ctx_rank * rows_here + jnp.arange(rows_here, dtype=jnp.int32)
    last_query = query_pos[-1]
    score_scale = 1.0 / math.sqrt(HEAD_DIM)

    def key_block(running, block_data):
        key_rows, value_rows, first_key = block_data

        def absorb(held):
            row_max, row_sum, weighted = held
            scores = (
                jnp.einsum(
                    "qgjd,kgd->gjqk", query_groups, key_rows, preferred_element_type=jnp.float32
                )
                * score_scale
            )
            key_pos = first_key + jnp.arange(key_rows.shape[0], dtype=jnp.int32)
            allowed = key_pos[None, :] <= query_pos[:, None]
            scores = jnp.where(allowed, scores, -1e30)
            new_max = jnp.maximum(row_max, jnp.max(scores, axis=-1))
            rescale = jnp.exp(row_max - new_max)
            weights_exp = jnp.where(allowed, jnp.exp(scores - new_max[..., None]), 0.0)
            row_sum = row_sum * rescale + jnp.sum(weights_exp, axis=-1)
            weighted = weighted * rescale[..., None] + jnp.einsum(
                "gjqk,kgd->gjqd",
                weights_exp.astype(jnp.bfloat16),
                value_rows,
                preferred_element_type=jnp.float32,
            )
            return (new_max, row_sum, weighted)

        return (lax.cond(first_key <= last_query, absorb, lambda held: held, running), None)

    start_state = (
        jnp.full((kv_count, per_key, rows_here), -1e30, jnp.float32),
        jnp.zeros((kv_count, per_key, rows_here), jnp.float32),
        jnp.zeros((kv_count, per_key, rows_here, HEAD_DIM), jnp.float32),
    )
    running = start_state
    key_piece = both[:, :key_width]
    value_piece = both[:, key_width:]
    count = key_piece.shape[0]
    width = math.gcd(count, 1024)
    blocks = count // width
    key_rows = key_piece.reshape(blocks, width, kv_count, HEAD_DIM)
    value_rows = value_piece.reshape(blocks, width, kv_count, HEAD_DIM)
    starts = width * jnp.arange(blocks, dtype=jnp.int32)
    running, unused = lax.scan(key_block, running, (key_rows, value_rows, starts))
    row_max, row_sum, weighted = running
    mixed = (weighted / row_sum[..., None]).transpose(2, 0, 1, 3).reshape(rows_here, -1)
    return mixed.astype(jnp.bfloat16)


def take_half(array, axis_dim, section):
    width = array.shape[axis_dim] // 2
    return lax.dynamic_slice_in_dim(array, section * width, width, axis_dim)


def per_device(
    resid_in,
    ssm_input,
    ssm_gate,
    ssm_in_b,
    ssm_out_c,
    step_size,
    decay_rate,
    skip_gain,
    norm_gain,
    queries,
    keys,
    values,
    out_weights,
):
    section = lax.axis_index("pipe")
    ctx_rank = (lax.axis_index("y") * lax.axis_size("z") + lax.axis_index("z")) * lax.axis_size(
        "c"
    ) + lax.axis_index("c")
    key_half = take_half(keys, 1, section)
    kv_own = jnp.concatenate([key_half, take_half(values, 1, section)], axis=1)
    mamba_part, both = mamba_mixer(
        take_half(ssm_input, 1, section),
        take_half(ssm_gate, 1, section),
        take_half(ssm_in_b, 1, section),
        take_half(ssm_out_c, 1, section),
        take_half(step_size, 1, section),
        take_half(decay_rate, 0, section),
        take_half(skip_gain, 0, section),
        take_half(norm_gain, 0, section),
        kv_own,
    )
    attn_part = attention(take_half(queries, 1, section), both, key_half.shape[1], ctx_rank)
    outgoing = jnp.where(section == 0, attn_part, mamba_part)
    kept_half = jnp.where(section == 0, mamba_part, attn_part)
    incoming = from_partner(outgoing, "pipe", 0)
    mixed_rows = jnp.where(
        section == 0,
        jnp.concatenate([kept_half, incoming], axis=1),
        jnp.concatenate([incoming, kept_half], axis=1),
    )
    weights_all = lax.all_gather(out_weights, CTX, axis=2, tiled=True)[0]
    half = weights_all.shape[1] // 2
    tp_rank = lax.axis_index("tp")
    sent_cols = lax.dynamic_slice_in_dim(weights_all, (1 - tp_rank) * half, half, 1)
    kept_cols = lax.dynamic_slice_in_dim(weights_all, tp_rank * half, half, 1)
    sent = jnp.dot(mixed_rows, sent_cols, preferred_element_type=jnp.float32).astype(jnp.bfloat16)
    from_tp = from_partner(sent, "tp", 0)
    kept = jnp.dot(mixed_rows, kept_cols, preferred_element_type=jnp.float32)
    kept_low = kept.astype(jnp.bfloat16)
    first_kept = shifted(kept_low, "pipe", 1)
    first_sent = lax.ppermute(sent, ("pipe", "tp"), [(0, 3), (1, 2)])
    base = resid_in.astype(jnp.float32)
    own_section = (
        (base + kept_low.astype(jnp.float32)) + from_tp.astype(jnp.float32)
    ).astype(jnp.bfloat16)
    rebuilt = (
        (base + first_kept.astype(jnp.float32)) + first_sent.astype(jnp.float32)
    ).astype(jnp.bfloat16)
    second_section = (
        rebuilt.astype(jnp.float32) + (kept + from_tp.astype(jnp.float32))
    ).astype(jnp.bfloat16)
    return jnp.where(section == 0, own_section, second_section)[None]


def solution(mesh):
    pipe, ctx, tp = (mesh.shape[name] for name in ("pipe", "ctx", "tp"))
    outer = 4 if ctx % 4 == 0 else 1
    pair = 2 if ctx % (2 * outer) == 0 else 1
    split = jax.sharding.Mesh(
        mesh.devices.reshape(pipe, outer, ctx // outer // pair, pair, tp),
        ("pipe", "y", "z", "c", "tp"),
    )
    return jax.shard_map(
        per_device,
        mesh=split,
        in_specs=(
            P(CTX, "tp"),
            P(CTX, "tp"),
            P(CTX, "tp"),
            P(CTX, "tp"),
            P(CTX, "tp"),
            P(CTX, "tp"),
            P("tp"),
            P("tp"),
            P("tp"),
            P(CTX, "tp"),
            P(CTX, "tp"),
            P(CTX, "tp"),
            P("pipe", "tp", CTX),
        ),
        out_specs=P("pipe", CTX, "tp"),
        check_vma=False,
    )
```

```python
import math

import jax
import jax.numpy as jnp
from jax import lax
from jax.sharding import PartitionSpec as P

MHEAD_DIM = 64
STATE = 128
SCAN_BLOCK = 128
HEAD_DIM = 128


exact_mode = lax.Precision.HIGHEST
norm_eps = 1e-05


def entering_2(x, axis, combine, identity):
    peers, position = (lax.axis_size(axis), lax.axis_index(axis))
    everything = jax.tree.map(
        lambda part, kind: lax.all_gather(part.astype(kind), axis), x, (jnp.bfloat16, jnp.bfloat16)
    )
    start = jax.tree.map(
        lambda part, zero: jnp.broadcast_to(jnp.asarray(zero, part.dtype), part.shape), x, identity
    )

    def turn(k, before):
        reached = k < position
        new = combine(
            before, jax.tree.map(lambda part, own: part[k].astype(own.dtype), everything, x)
        )
        return jax.tree.map(lambda a, b: jnp.where(reached, a, b), new, before)

    return lax.fori_loop(0, peers, turn, start)


CTX = ("y", "z", "c")


def gathered(x, axis):
    peers = lax.axis_size(axis)
    spread = jnp.broadcast_to(x[None], (peers,) + x.shape)
    return lax.all_to_all(spread, axis, 0, 0)


def entering_states(through_log, local_state):
    outer, middle, pair = (lax.axis_size(name) for name in CTX)
    inner = middle * pair
    peers = outer * inner
    rank = lax.axis_index("y") * inner + lax.axis_index("z") * pair + lax.axis_index("c")
    logs = gathered(through_log, CTX)
    logs = logs.reshape((peers,) + through_log.shape)
    places = jnp.arange(peers, dtype=jnp.int32)

    def span_weight(k, upto):
        inside = (places[None, :] > k[:, None]) & (places[None, :] < upto)
        summed = jnp.sum(jnp.where(inside[:, :, None, None], logs[None], 0.0), axis=1)
        return jnp.where((k < upto)[:, None, None], jnp.exp(summed), 0.0)

    def mix(weight, states):
        return jnp.einsum("kgj,kgjpn->gjpn", weight, states, precision=exact_mode)

    first = lax.axis_index("y") * inner
    pair_first = first + lax.axis_index("z") * pair
    near = gathered(local_state.astype(jnp.bfloat16), "c").astype(jnp.float32)
    near_ids = pair_first + jnp.arange(pair, dtype=jnp.int32)
    pair_part = mix(span_weight(near_ids, rank), near)
    pair_total = mix(span_weight(near_ids, pair_first + pair), near)
    mid = gathered(pair_total.astype(jnp.bfloat16), "z").astype(jnp.float32)
    mid_ends = first + (jnp.arange(middle, dtype=jnp.int32) + 1) * pair - 1
    mid_weight = jnp.where((mid_ends < pair_first)[:, None, None], span_weight(mid_ends, rank), 0.0)
    group_part = mix(mid_weight, mid)
    group_total = mix(span_weight(mid_ends, first + inner), mid)
    far = gathered(group_total.astype(jnp.bfloat16), "y").astype(jnp.float32)
    far_ends = (jnp.arange(outer, dtype=jnp.int32) + 1) * inner - 1
    far_weight = jnp.where((far_ends < first)[:, None, None], span_weight(far_ends, rank), 0.0)
    far_part = mix(far_weight, far)
    return pair_part + group_part + far_part


def from_partner(block, axis, distance):
    count = lax.axis_size(axis)
    route = []
    for low in range(count):
        high = low | 1 << distance
        if high != low and high < count:
            route += [(low, high), (high, low)]
    return lax.ppermute(block, axis, route)


def shifted(x, axis, by):
    peers = lax.axis_size(axis)
    pairs = [(i, i + by) for i in range(peers) if 0 <= i + by < peers]
    return lax.ppermute(x, axis, pairs)


def block_scan(state_now, inputs_x, input_b, output_c, step_rows, log_decay):
    width = inputs_x.shape[0]
    groups = inputs_x.shape[1]
    per_group = inputs_x.shape[2]
    running = jnp.cumsum(log_decay, axis=0)
    spread = running[:, None, :] - running[None, :, :]
    causal = (
        jnp.arange(width, dtype=jnp.int32)[:, None] >= jnp.arange(width, dtype=jnp.int32)[None, :]
    )
    decay_mat = jnp.exp(jnp.where(causal[:, :, None], spread, -jnp.inf))
    decay_mat = decay_mat.reshape(width, width, groups, per_group).transpose(2, 3, 0, 1)
    cross_cb = jnp.einsum("tgn,sgn->gts", output_c, input_b, precision=exact_mode)
    step_cols = step_rows.reshape(width, groups, per_group).transpose(1, 2, 0)
    mixing = cross_cb[:, None, :, :] * decay_mat * step_cols[:, :, None, :]
    within = jnp.einsum("gjts,sgjp->tgjp", mixing, inputs_x, precision=exact_mode)
    entry = jnp.exp(running).reshape(width, groups, per_group)
    carried = (
        jnp.einsum("tgn,gjpn->tgjp", output_c, state_now, precision=exact_mode)
        * entry[:, :, :, None]
    )
    tail_weight = (jnp.exp(running[-1][None, :] - running) * step_rows).reshape(
        width, groups, per_group
    )
    leaving = jnp.exp(running[-1]).reshape(groups, per_group)
    state_next = leaving[:, :, None, None] * state_now + jnp.einsum(
        "sgj,sgjp,sgn->gjpn", tail_weight, inputs_x, input_b, precision=exact_mode
    )
    return (state_next, within + carried)


def gate_norm(values_y, gate_in, gains, groups):
    rows_here = values_y.shape[0]
    gated = values_y * jax.nn.silu(gate_in.astype(jnp.float32))
    grouped = gated.reshape(rows_here, groups, -1)
    meansq = jnp.mean(grouped * grouped, axis=-1, keepdims=True)
    scaled = (grouped * lax.rsqrt(meansq + norm_eps)).reshape(rows_here, -1)
    return (scaled * gains[None, :]).astype(jnp.bfloat16)


def join_states(earlier, later):
    return (earlier[0] * later[0], later[0][:, :, None, None] * earlier[1] + later[1])


def mamba_mixer(
    ssm_input, ssm_gate, ssm_in_b, ssm_out_c, step_size, decay_rate, skip_gain, norm_gain
):
    rows_here = ssm_input.shape[0]
    head_count = decay_rate.shape[0]
    groups = ssm_in_b.shape[1] // STATE
    per_group = head_count // groups
    block_count = rows_here // SCAN_BLOCK
    log_decay = -step_size * decay_rate[None, :]
    inputs_x = ssm_input.reshape(block_count, SCAN_BLOCK, groups, per_group, MHEAD_DIM)
    input_b = ssm_in_b.reshape(block_count, SCAN_BLOCK, groups, STATE)
    output_c = ssm_out_c.reshape(block_count, SCAN_BLOCK, groups, STATE)

    def block_turn(state_now, block_data):
        part_x, part_b, part_c, part_step, part_log = block_data
        return block_scan(
            state_now,
            part_x.astype(jnp.float32),
            part_b.astype(jnp.float32),
            part_c.astype(jnp.float32),
            part_step,
            part_log,
        )

    start_state = jnp.zeros((groups, per_group, MHEAD_DIM, STATE), jnp.float32)
    local_state, pieces = lax.scan(
        block_turn,
        start_state,
        (
            inputs_x,
            input_b,
            output_c,
            step_size.reshape(block_count, SCAN_BLOCK, head_count),
            log_decay.reshape(block_count, SCAN_BLOCK, head_count),
        ),
    )
    running = jnp.cumsum(log_decay, axis=0)
    entering = entering_states(running[-1].reshape(groups, per_group), local_state)
    output_all = ssm_out_c.astype(jnp.float32).reshape(rows_here, groups, STATE)
    carried = (
        jnp.einsum("tgn,gjpn->tgjp", output_all, entering, precision=exact_mode)
        * jnp.exp(running).reshape(rows_here, groups, per_group)[:, :, :, None]
    )
    skipped = (
        ssm_input.astype(jnp.float32).reshape(rows_here, groups, per_group, MHEAD_DIM)
        * skip_gain.reshape(groups, per_group)[None, :, :, None]
    )
    values_y = pieces.reshape(rows_here, groups, per_group, MHEAD_DIM) + carried + skipped
    return gate_norm(values_y.reshape(rows_here, -1), ssm_gate, norm_gain, groups)


def attention(queries, keys, values, ctx_rank):
    rows_here = queries.shape[0]
    kv_count = keys.shape[1] // HEAD_DIM
    per_key = queries.shape[1] // HEAD_DIM // kv_count
    query_groups = queries.reshape(rows_here, kv_count, per_key, HEAD_DIM)
    query_pos = ctx_rank * rows_here + jnp.arange(rows_here, dtype=jnp.int32)
    last_query = query_pos[-1]
    score_scale = 1.0 / math.sqrt(HEAD_DIM)

    def key_block(running, block_data):
        key_rows, value_rows, first_key = block_data

        def absorb(held):
            row_max, row_sum, weighted = held
            scores = (
                jnp.einsum(
                    "qgjd,kgd->gjqk", query_groups, key_rows, preferred_element_type=jnp.float32
                )
                * score_scale
            )
            key_pos = first_key + jnp.arange(key_rows.shape[0], dtype=jnp.int32)
            allowed = key_pos[None, :] <= query_pos[:, None]
            scores = jnp.where(allowed, scores, -1e30)
            new_max = jnp.maximum(row_max, jnp.max(scores, axis=-1))
            rescale = jnp.exp(row_max - new_max)
            weights_exp = jnp.where(allowed, jnp.exp(scores - new_max[..., None]), 0.0)
            row_sum = row_sum * rescale + jnp.sum(weights_exp, axis=-1)
            weighted = weighted * rescale[..., None] + jnp.einsum(
                "gjqk,kgd->gjqd",
                weights_exp.astype(jnp.bfloat16),
                value_rows,
                preferred_element_type=jnp.float32,
            )
            return (new_max, row_sum, weighted)

        return (lax.cond(first_key <= last_query, absorb, lambda held: held, running), None)

    start_state = (
        jnp.full((kv_count, per_key, rows_here), -1e30, jnp.float32),
        jnp.zeros((kv_count, per_key, rows_here), jnp.float32),
        jnp.zeros((kv_count, per_key, rows_here, HEAD_DIM), jnp.float32),
    )
    running = start_state
    both = lax.all_gather(jnp.concatenate([keys, values], axis=1), CTX, axis=0, tiled=True)
    key_piece = both[:, : keys.shape[1]]
    value_piece = both[:, keys.shape[1] :]
    count = key_piece.shape[0]
    width = math.gcd(count, 1024)
    blocks = count // width
    key_rows = key_piece.reshape(blocks, width, kv_count, HEAD_DIM)
    value_rows = value_piece.reshape(blocks, width, kv_count, HEAD_DIM)
    starts = width * jnp.arange(blocks, dtype=jnp.int32)
    running, unused = lax.scan(key_block, running, (key_rows, value_rows, starts))
    row_max, row_sum, weighted = running
    mixed = (weighted / row_sum[..., None]).transpose(2, 0, 1, 3).reshape(rows_here, -1)
    return mixed.astype(jnp.bfloat16)


def take_half(array, axis_dim, section):
    width = array.shape[axis_dim] // 2
    return lax.dynamic_slice_in_dim(array, section * width, width, axis_dim)


def per_device(
    resid_in,
    ssm_input,
    ssm_gate,
    ssm_in_b,
    ssm_out_c,
    step_size,
    decay_rate,
    skip_gain,
    norm_gain,
    queries,
    keys,
    values,
    out_weights,
):
    section = lax.axis_index("pipe")
    ctx_rank = (lax.axis_index("y") * lax.axis_size("z") + lax.axis_index("z")) * lax.axis_size(
        "c"
    ) + lax.axis_index("c")
    mamba_part = mamba_mixer(
        take_half(ssm_input, 1, section),
        take_half(ssm_gate, 1, section),
        take_half(ssm_in_b, 1, section),
        take_half(ssm_out_c, 1, section),
        take_half(step_size, 1, section),
        take_half(decay_rate, 0, section),
        take_half(skip_gain, 0, section),
        take_half(norm_gain, 0, section),
    )
    attn_part = attention(
        take_half(queries, 1, section),
        take_half(keys, 1, section),
        take_half(values, 1, section),
        ctx_rank,
    )
    outgoing = jnp.where(section == 0, attn_part, mamba_part)
    kept_half = jnp.where(section == 0, mamba_part, attn_part)
    incoming = from_partner(outgoing, "pipe", 0)
    mixed_rows = jnp.where(
        section == 0,
        jnp.concatenate([kept_half, incoming], axis=1),
        jnp.concatenate([incoming, kept_half], axis=1),
    )
    depth = out_weights.shape[1] // 2
    upper = lax.all_gather(out_weights[:, :depth], CTX, axis=2, tiled=True)[0]
    lower = lax.all_gather(out_weights[:, depth:], CTX, axis=2, tiled=True)[0]
    half = upper.shape[1] // 2
    tp_rank = lax.axis_index("tp")

    def project(start):
        near = jnp.dot(
            mixed_rows[:, :depth],
            lax.dynamic_slice_in_dim(upper, start, half, 1),
            preferred_element_type=jnp.float32,
        )
        far = jnp.dot(
            mixed_rows[:, depth:],
            lax.dynamic_slice_in_dim(lower, start, half, 1),
            preferred_element_type=jnp.float32,
        )
        return near + far

    sent = project((1 - tp_rank) * half).astype(jnp.bfloat16)
    from_tp = from_partner(sent, "tp", 0)
    kept = project(tp_rank * half)
    kept_low = kept.astype(jnp.bfloat16)
    first_kept = shifted(kept_low, "pipe", 1)
    first_sent = lax.ppermute(sent, ("pipe", "tp"), [(0, 3), (1, 2)])
    base = resid_in.astype(jnp.float32)
    own_section = (
        (base + kept_low.astype(jnp.float32)) + from_tp.astype(jnp.float32)
    ).astype(jnp.bfloat16)
    rebuilt = (
        (base + first_kept.astype(jnp.float32)) + first_sent.astype(jnp.float32)
    ).astype(jnp.bfloat16)
    second_section = (
        rebuilt.astype(jnp.float32) + (kept + from_tp.astype(jnp.float32))
    ).astype(jnp.bfloat16)
    return jnp.where(section == 0, own_section, second_section)[None]


def solution(mesh):
    pipe, ctx, tp = (mesh.shape[name] for name in ("pipe", "ctx", "tp"))
    outer = 4 if ctx % 4 == 0 else 1
    pair = 2 if ctx % (2 * outer) == 0 else 1
    split = jax.sharding.Mesh(
        mesh.devices.reshape(pipe, outer, ctx // outer // pair, pair, tp),
        ("pipe", "y", "z", "c", "tp"),
    )
    return jax.shard_map(
        per_device,
        mesh=split,
        in_specs=(
            P(CTX, "tp"),
            P(CTX, "tp"),
            P(CTX, "tp"),
            P(CTX, "tp"),
            P(CTX, "tp"),
            P(CTX, "tp"),
            P("tp"),
            P("tp"),
            P("tp"),
            P(CTX, "tp"),
            P(CTX, "tp"),
            P(CTX, "tp"),
            P("pipe", "tp", CTX),
        ),
        out_specs=P("pipe", CTX, "tp"),
        check_vma=False,
    )
```

```python
import math

import jax
import jax.numpy as jnp
from jax import lax
from jax.sharding import PartitionSpec as P

MHEAD_DIM = 64
STATE = 128
SCAN_BLOCK = 128
HEAD_DIM = 128


exact_mode = lax.Precision.HIGHEST
norm_eps = 1e-05


def entering_2(x, axis, combine, identity):
    peers, position = (lax.axis_size(axis), lax.axis_index(axis))
    everything = jax.tree.map(
        lambda part, kind: lax.all_gather(part.astype(kind), axis), x, (jnp.bfloat16, jnp.bfloat16)
    )
    start = jax.tree.map(
        lambda part, zero: jnp.broadcast_to(jnp.asarray(zero, part.dtype), part.shape), x, identity
    )

    def turn(k, before):
        reached = k < position
        new = combine(
            before, jax.tree.map(lambda part, own: part[k].astype(own.dtype), everything, x)
        )
        return jax.tree.map(lambda a, b: jnp.where(reached, a, b), new, before)

    return lax.fori_loop(0, peers, turn, start)


CTX = ("y", "z", "c")


def gathered(x, axis):
    peers = lax.axis_size(axis)
    spread = jnp.broadcast_to(x[None], (peers,) + x.shape)
    return lax.all_to_all(spread, axis, 0, 0)


def entering_states(through_log, local_state):
    outer, middle, pair = (lax.axis_size(name) for name in CTX)
    inner = middle * pair
    peers = outer * inner
    rank = lax.axis_index("y") * inner + lax.axis_index("z") * pair + lax.axis_index("c")
    logs = gathered(through_log, CTX)
    logs = logs.reshape((peers,) + through_log.shape)
    places = jnp.arange(peers, dtype=jnp.int32)

    def span_weight(k, upto):
        inside = (places[None, :] > k[:, None]) & (places[None, :] < upto)
        summed = jnp.sum(jnp.where(inside[:, :, None, None], logs[None], 0.0), axis=1)
        return jnp.where((k < upto)[:, None, None], jnp.exp(summed), 0.0)

    def mix(weight, states):
        return jnp.einsum("kgj,kgjpn->gjpn", weight, states)

    first = lax.axis_index("y") * inner
    pair_first = first + lax.axis_index("z") * pair
    near = gathered(local_state.astype(jnp.bfloat16), "c").astype(jnp.float32)
    near_ids = pair_first + jnp.arange(pair, dtype=jnp.int32)
    pair_part = mix(span_weight(near_ids, rank), near)
    pair_total = mix(span_weight(near_ids, pair_first + pair), near)
    mid = gathered(pair_total.astype(jnp.bfloat16), "z").astype(jnp.float32)
    mid_ends = first + (jnp.arange(middle, dtype=jnp.int32) + 1) * pair - 1
    mid_weight = jnp.where((mid_ends < pair_first)[:, None, None], span_weight(mid_ends, rank), 0.0)
    group_part = mix(mid_weight, mid)
    group_total = mix(span_weight(mid_ends, first + inner), mid)
    far = gathered(group_total.astype(jnp.bfloat16), "y").astype(jnp.float32)
    far_ends = (jnp.arange(outer, dtype=jnp.int32) + 1) * inner - 1
    far_weight = jnp.where((far_ends < first)[:, None, None], span_weight(far_ends, rank), 0.0)
    far_part = mix(far_weight, far)
    return pair_part + group_part + far_part


def from_partner(block, axis, distance):
    count = lax.axis_size(axis)
    route = []
    for low in range(count):
        high = low | 1 << distance
        if high != low and high < count:
            route += [(low, high), (high, low)]
    return lax.ppermute(block, axis, route)


def shifted(x, axis, by):
    peers = lax.axis_size(axis)
    pairs = [(i, i + by) for i in range(peers) if 0 <= i + by < peers]
    return lax.ppermute(x, axis, pairs)


def block_scan(state_now, inputs_x, input_b, output_c, step_rows, log_decay):
    width = inputs_x.shape[0]
    groups = inputs_x.shape[1]
    per_group = inputs_x.shape[2]
    running = jnp.cumsum(log_decay, axis=0)
    spread = running[:, None, :] - running[None, :, :]
    causal = (
        jnp.arange(width, dtype=jnp.int32)[:, None] >= jnp.arange(width, dtype=jnp.int32)[None, :]
    )
    decay_mat = jnp.exp(jnp.where(causal[:, :, None], spread, -jnp.inf))
    decay_mat = decay_mat.reshape(width, width, groups, per_group).transpose(2, 3, 0, 1)
    cross_cb = jnp.einsum("tgn,sgn->gts", output_c, input_b, precision=exact_mode)
    step_cols = step_rows.reshape(width, groups, per_group).transpose(1, 2, 0)
    mixing = cross_cb[:, None, :, :] * decay_mat * step_cols[:, :, None, :]
    within = jnp.einsum("gjts,sgjp->tgjp", mixing, inputs_x, precision=exact_mode)
    entry = jnp.exp(running).reshape(width, groups, per_group)
    carried = (
        jnp.einsum("tgn,gjpn->tgjp", output_c, state_now, precision=exact_mode)
        * entry[:, :, :, None]
    )
    tail_weight = (jnp.exp(running[-1][None, :] - running) * step_rows).reshape(
        width, groups, per_group
    )
    leaving = jnp.exp(running[-1]).reshape(groups, per_group)
    state_next = leaving[:, :, None, None] * state_now + jnp.einsum(
        "sgj,sgjp,sgn->gjpn", tail_weight, inputs_x, input_b, precision=exact_mode
    )
    return (state_next, within + carried)


def gate_norm(values_y, gate_in, gains, groups):
    rows_here = values_y.shape[0]
    gated = values_y * jax.nn.silu(gate_in.astype(jnp.float32))
    grouped = gated.reshape(rows_here, groups, -1)
    meansq = jnp.mean(grouped * grouped, axis=-1, keepdims=True)
    scaled = (grouped * lax.rsqrt(meansq + norm_eps)).reshape(rows_here, -1)
    return (scaled * gains[None, :]).astype(jnp.bfloat16)


def join_states(earlier, later):
    return (earlier[0] * later[0], later[0][:, :, None, None] * earlier[1] + later[1])


def mamba_mixer(
    ssm_input, ssm_gate, ssm_in_b, ssm_out_c, step_size, decay_rate, skip_gain, norm_gain
):
    rows_here = ssm_input.shape[0]
    head_count = decay_rate.shape[0]
    groups = ssm_in_b.shape[1] // STATE
    per_group = head_count // groups
    block_count = rows_here // SCAN_BLOCK
    log_decay = -step_size * decay_rate[None, :]
    inputs_x = ssm_input.reshape(block_count, SCAN_BLOCK, groups, per_group, MHEAD_DIM)
    input_b = ssm_in_b.reshape(block_count, SCAN_BLOCK, groups, STATE)
    output_c = ssm_out_c.reshape(block_count, SCAN_BLOCK, groups, STATE)

    def block_turn(state_now, block_data):
        part_x, part_b, part_c, part_step, part_log = block_data
        return block_scan(
            state_now,
            part_x.astype(jnp.float32),
            part_b.astype(jnp.float32),
            part_c.astype(jnp.float32),
            part_step,
            part_log,
        )

    start_state = jnp.zeros((groups, per_group, MHEAD_DIM, STATE), jnp.float32)
    local_state, pieces = lax.scan(
        block_turn,
        start_state,
        (
            inputs_x,
            input_b,
            output_c,
            step_size.reshape(block_count, SCAN_BLOCK, head_count),
            log_decay.reshape(block_count, SCAN_BLOCK, head_count),
        ),
    )
    running = jnp.cumsum(log_decay, axis=0)
    entering = entering_states(running[-1].reshape(groups, per_group), local_state)
    output_all = ssm_out_c.astype(jnp.float32).reshape(rows_here, groups, STATE)
    carried = (
        jnp.einsum("tgn,gjpn->tgjp", output_all, entering, precision=exact_mode)
        * jnp.exp(running).reshape(rows_here, groups, per_group)[:, :, :, None]
    )
    skipped = (
        ssm_input.astype(jnp.float32).reshape(rows_here, groups, per_group, MHEAD_DIM)
        * skip_gain.reshape(groups, per_group)[None, :, :, None]
    )
    values_y = pieces.reshape(rows_here, groups, per_group, MHEAD_DIM) + carried + skipped
    return gate_norm(values_y.reshape(rows_here, -1), ssm_gate, norm_gain, groups)


def attention(queries, keys, values, ctx_rank):
    rows_here = queries.shape[0]
    kv_count = keys.shape[1] // HEAD_DIM
    per_key = queries.shape[1] // HEAD_DIM // kv_count
    query_groups = queries.reshape(rows_here, kv_count, per_key, HEAD_DIM)
    query_pos = ctx_rank * rows_here + jnp.arange(rows_here, dtype=jnp.int32)
    last_query = query_pos[-1]
    score_scale = 1.0 / math.sqrt(HEAD_DIM)

    def key_block(running, block_data):
        key_rows, value_rows, first_key = block_data

        def absorb(held):
            row_max, row_sum, weighted = held
            scores = (
                jnp.einsum(
                    "qgjd,kgd->gjqk", query_groups, key_rows, preferred_element_type=jnp.float32
                )
                * score_scale
            )
            key_pos = first_key + jnp.arange(key_rows.shape[0], dtype=jnp.int32)
            allowed = key_pos[None, :] <= query_pos[:, None]
            scores = jnp.where(allowed, scores, -1e30)
            new_max = jnp.maximum(row_max, jnp.max(scores, axis=-1))
            rescale = jnp.exp(row_max - new_max)
            weights_exp = jnp.where(allowed, jnp.exp(scores - new_max[..., None]), 0.0)
            row_sum = row_sum * rescale + jnp.sum(weights_exp, axis=-1)
            weighted = weighted * rescale[..., None] + jnp.einsum(
                "gjqk,kgd->gjqd",
                weights_exp.astype(jnp.bfloat16),
                value_rows,
                preferred_element_type=jnp.float32,
            )
            return (new_max, row_sum, weighted)

        return (lax.cond(first_key <= last_query, absorb, lambda held: held, running), None)

    start_state = (
        jnp.full((kv_count, per_key, rows_here), -1e30, jnp.float32),
        jnp.zeros((kv_count, per_key, rows_here), jnp.float32),
        jnp.zeros((kv_count, per_key, rows_here, HEAD_DIM), jnp.float32),
    )
    running = start_state
    both = lax.all_gather(jnp.concatenate([keys, values], axis=1), CTX, axis=0, tiled=True)
    key_piece = both[:, : keys.shape[1]]
    value_piece = both[:, keys.shape[1] :]
    count = key_piece.shape[0]
    width = math.gcd(count, 1024)
    blocks = count // width
    key_rows = key_piece.reshape(blocks, width, kv_count, HEAD_DIM)
    value_rows = value_piece.reshape(blocks, width, kv_count, HEAD_DIM)
    starts = width * jnp.arange(blocks, dtype=jnp.int32)
    running, unused = lax.scan(key_block, running, (key_rows, value_rows, starts))
    row_max, row_sum, weighted = running
    mixed = (weighted / row_sum[..., None]).transpose(2, 0, 1, 3).reshape(rows_here, -1)
    return mixed.astype(jnp.bfloat16)


def take_half(array, axis_dim, section):
    width = array.shape[axis_dim] // 2
    return lax.dynamic_slice_in_dim(array, section * width, width, axis_dim)


def per_device(
    resid_in,
    ssm_input,
    ssm_gate,
    ssm_in_b,
    ssm_out_c,
    step_size,
    decay_rate,
    skip_gain,
    norm_gain,
    queries,
    keys,
    values,
    out_weights,
):
    section = lax.axis_index("pipe")
    ctx_rank = (lax.axis_index("y") * lax.axis_size("z") + lax.axis_index("z")) * lax.axis_size(
        "c"
    ) + lax.axis_index("c")
    mamba_part = mamba_mixer(
        take_half(ssm_input, 1, section),
        take_half(ssm_gate, 1, section),
        take_half(ssm_in_b, 1, section),
        take_half(ssm_out_c, 1, section),
        take_half(step_size, 1, section),
        take_half(decay_rate, 0, section),
        take_half(skip_gain, 0, section),
        take_half(norm_gain, 0, section),
    )
    attn_part = attention(
        take_half(queries, 1, section),
        take_half(keys, 1, section),
        take_half(values, 1, section),
        ctx_rank,
    )
    outgoing = jnp.where(section == 0, attn_part, mamba_part)
    kept_half = jnp.where(section == 0, mamba_part, attn_part)
    incoming = from_partner(outgoing, "pipe", 0)
    mixed_rows = jnp.where(
        section == 0,
        jnp.concatenate([kept_half, incoming], axis=1),
        jnp.concatenate([incoming, kept_half], axis=1),
    )
    weights_all = lax.all_gather(out_weights, CTX, axis=2, tiled=True)[0]
    half = weights_all.shape[1] // 2
    tp_rank = lax.axis_index("tp")
    sent_cols = lax.dynamic_slice_in_dim(weights_all, (1 - tp_rank) * half, half, 1)
    kept_cols = lax.dynamic_slice_in_dim(weights_all, tp_rank * half, half, 1)
    sent = jnp.dot(mixed_rows, sent_cols, preferred_element_type=jnp.float32).astype(jnp.bfloat16)
    from_tp = from_partner(sent, "tp", 0)
    kept = jnp.dot(mixed_rows, kept_cols, preferred_element_type=jnp.float32)
    kept_low = kept.astype(jnp.bfloat16)
    first_kept = shifted(kept_low, "pipe", 1)
    first_sent = lax.ppermute(sent, ("pipe", "tp"), [(0, 3), (1, 2)])
    base = resid_in.astype(jnp.float32)
    own_section = (
        (base + kept_low.astype(jnp.float32)) + from_tp.astype(jnp.float32)
    ).astype(jnp.bfloat16)
    rebuilt = (
        (base + first_kept.astype(jnp.float32)) + first_sent.astype(jnp.float32)
    ).astype(jnp.bfloat16)
    second_section = (
        rebuilt.astype(jnp.float32) + (kept + from_tp.astype(jnp.float32))
    ).astype(jnp.bfloat16)
    return jnp.where(section == 0, own_section, second_section)[None]


def solution(mesh):
    pipe, ctx, tp = (mesh.shape[name] for name in ("pipe", "ctx", "tp"))
    outer = 4 if ctx % 4 == 0 else 1
    pair = 2 if ctx % (2 * outer) == 0 else 1
    split = jax.sharding.Mesh(
        mesh.devices.reshape(pipe, outer, ctx // outer // pair, pair, tp),
        ("pipe", "y", "z", "c", "tp"),
    )
    return jax.shard_map(
        per_device,
        mesh=split,
        in_specs=(
            P(CTX, "tp"),
            P(CTX, "tp"),
            P(CTX, "tp"),
            P(CTX, "tp"),
            P(CTX, "tp"),
            P(CTX, "tp"),
            P("tp"),
            P("tp"),
            P("tp"),
            P(CTX, "tp"),
            P(CTX, "tp"),
            P(CTX, "tp"),
            P("pipe", "tp", CTX),
        ),
        out_specs=P("pipe", CTX, "tp"),
        check_vma=False,
    )
```
